128 devices in a mesh: gx: 16 (over x_hi, z, core), gy: 8 (over x_lo, y).
Axes of the slice: x: 4 (x_hi: 2, x_lo: 2; x = x_hi * 2 + x_lo), y: 4, z: 4, core: 2. Of those that a mesh axis runs over, the one named last changes fastest.
Arguments:
- wave_tokens: bfloat16 [128, 256, 512], P('gx', 'gy'), may hold values from -6 to 6
- grad_out: bfloat16 [128, 256, 512], P('gx', 'gy'), may hold values from -6 to 6
- w_qkv: bfloat16 [512, 1536], replicated, may hold values from -0.25 to 0.25
- w_proj: bfloat16 [512, 512], replicated, may hold values from -0.25 to 0.25
- w_fc1: bfloat16 [512, 2048], replicated, may hold values from -0.25 to 0.25
- w_fc2: bfloat16 [2048, 512], replicated, may hold values from -0.125 to 0.125
- gain_attn: float32 [512], replicated, may hold values from 0.25 to 1.75
- gain_mlp: float32 [512], replicated, may hold values from 0.25 to 1.75
- attn_scale: float32 [16], replicated, may hold values from 2 to 16
- bias_table: float32 [16, 225], replicated, may hold values from -4 to 4
- r_wq: bfloat16 [512, 512], replicated, may hold values from -0.25 to 0.25
- r_wkv: bfloat16 [512, 1024], replicated, may hold values from -0.25 to 0.25
- r_wo: bfloat16 [512, 512], replicated, may hold values from -0.25 to 0.25
- read_scale: float32 [16], replicated, may hold values from 2 to 16
- floe_feat: bfloat16 [128, 768, 512], P(('gx', 'gy')), may hold values from -6 to 6
- floe_count: int32 [128], P(('gx', 'gy')), may hold values from 1 to 768, 32768 in all
- floe_patch: int32 [128, 768], P(('gx', 'gy')), may hold values from 0 to 32767, as said below
- floe_cover: int32 [128, 3, 768], P(('gx', 'gy')), may hold values 0 or 1
Outputs:
- patch_out: bfloat16 [128, 256, 512], P('gx', 'gy')
- grad_in: bfloat16 [128, 256, 512], P('gx', 'gy')
- floe_out: bfloat16 [128, 768, 512], P(('gx', 'gy'))
The draws below stay inside these ranges and needn't reach their ends.
Inputs may be any that keep to these rules, and one draw needn't show every extreme that they name: `floe_patch`: among one device's 768 slots, exactly 6 name a patch in each device's block of 8 x 32 patches. The live floes of a device are its first floe_count slots; the counts sum to 32768 and the largest is 768.
All inputs are finite; a program needn't handle non-finite values. No bound on the sum of `floe_cover` on one device may be relied on, other than what follows from the above.
Results may differ from the reference program's by a relative error of at most 0.02.
Values may be sent and summed in bfloat16 or wider, within the bound.
No kernel may reach another device: no remote copies, remote signals or barrier semaphores. Data moves between devices by JAX's collectives and lax.ppermute only.
A program may use at most 128 MiB of HBM per device.

```python
import math
import jax
import jax.numpy as jnp
import numpy as np
from jax import lax

WIDTH = 512
HEADS = 16
FF = 2048
WIN = 8
SHIFT = 4
H_DEV = 8
W_DEV = 32
FLOE_MEAN = 256
NROWS = 128
NCOLS = 256
FLOE_CAP = 768
DEVICES = 128


def draw_floe_patch(key, part):
    dev_rows = NROWS // H_DEV
    dev_cols = NCOLS // W_DEV
    dev_total = dev_rows * dev_cols
    block_keys = jax.random.split(jax.random.fold_in(key, 11), dev_total)
    orders = jax.vmap(lambda block_key: jax.random.permutation(block_key, FLOE_CAP))(block_keys)
    target = orders % dev_total
    cell_pos = jax.random.randint(jax.random.fold_in(key, 12), (dev_total, FLOE_CAP), 0, H_DEV * W_DEV)
    row_pos = target // dev_cols * H_DEV + cell_pos // W_DEV
    col_pos = target % dev_cols * W_DEV + cell_pos % W_DEV
    return (row_pos * NCOLS + col_pos).astype(jnp.int32)


def set_ends(values, rng, low, high):
    extent = values.shape
    index_at = [jax.random.randint(jax.random.fold_in(rng, axis), (), 0, extent[axis]) for axis in range(len(extent))]
    values = values.at[tuple(index_at)].set(low)
    longest = extent.index(max(extent))
    index_at[longest] = (index_at[longest] + 1) % extent[longest]
    return values.at[tuple(index_at)].set(high)


def steps_of(key, shape, pieces, smallest, top_value):
    def one(axis_at, parts):
        steps = jax.random.uniform(jax.random.fold_in(jax.random.fold_in(key, 6), axis_at), (parts,), jnp.float32, smallest / len(pieces), top_value / len(pieces))
        return jnp.repeat(jnp.exp(steps), shape[axis_at] // parts).reshape((-1,) + (1,) * (len(shape) - axis_at - 1))

    gain = one(*pieces[0])
    for cut in pieces[1:]:
        gain = gain * one(*cut)
    return gain


def split_up(amount, total, most, skew):
    weights = [(1 << 20) // math.isqrt(grade ** skew) + 1 for grade in range(2, amount + 1)]
    surplus, counts = total - most - (amount - 1), [1] * (amount - 1)
    while surplus > 0:
        free = [i for i in range(amount - 1) if counts[i] < most]
        whole, budget = sum([weights[i] for i in free]), surplus
        for i in free:
            more = min(most - counts[i], max(1, budget * weights[i] // whole), surplus)
            counts[i] = counts[i] + more
            surplus = surplus - more
    return np.array([most] + counts)


def uneven(rng, number_of, total, most, skew):
    if number_of == 2:
        one = jax.random.randint(rng, (), max(1, total - most), min(most, total - 1) + 1)
        return jnp.stack([one, total - one])
    tallies = jnp.asarray(split_up(number_of, total, most, skew), jnp.int32)
    pairs = (number_of - 1) // 2
    giver, taker = tallies[1:1 + 2 * pairs:2], tallies[2:2 + 2 * pairs:2]
    slack = jnp.minimum(giver - 1, most - taker)
    passed = jax.random.randint(jax.random.fold_in(rng, 1), (pairs,), 0, 1 << 20) % (slack + 1)
    tallies = tallies.at[1:1 + 2 * pairs:2].set(giver - passed).at[2:2 + 2 * pairs:2].set(taker + passed)
    return tallies[jax.random.permutation(jax.random.fold_in(rng, 2), number_of)]


def noise(own_key, shape, deviation, bound, cuts=(), held_as=jnp.bfloat16):
    entries = jax.random.normal(own_key, shape, jnp.float32) * deviation
    if len(cuts) > 0:
        entries = steps_of(own_key, shape, cuts, -0.22, 0.18) * entries
    return jnp.clip(entries, min=-bound, max=bound).astype(held_as)


def setup_inputs(seed: int = 0) -> dict:
    seeds = jax.random.split(jax.random.key(seed), 19)
    wave_tokens = noise(seeds[0], (NROWS, NCOLS, WIDTH), 1.0, 6.0, ((0, 16), (1, 8)))
    grad_out = noise(seeds[1], (NROWS, NCOLS, WIDTH), 1.0, 6.0, ((0, 16), (1, 8)))
    w_qkv = noise(seeds[2], (WIDTH, 3 * WIDTH), WIDTH ** -0.5, 0.25)
    w_proj = noise(seeds[3], (WIDTH, WIDTH), WIDTH ** -0.5, 0.25)
    w_fc1 = noise(seeds[4], (WIDTH, FF), WIDTH ** -0.5, 0.25)
    w_fc2 = noise(seeds[5], (FF, WIDTH), FF ** -0.5, 0.125)
    gain_attn = jnp.clip(1.0 + 0.15 * jax.random.normal(seeds[6], (WIDTH,), jnp.float32), 0.25, 1.75)
    gain_mlp = jnp.clip(1.0 + 0.15 * jax.random.normal(seeds[7], (WIDTH,), jnp.float32), 0.25, 1.75)
    attn_scale = jnp.clip(jnp.exp(jax.random.uniform(seeds[8], (HEADS,), jnp.float32, math.log(2.0), math.log(16.0))), 2.0, 16.0)
    bias_table = noise(seeds[9], (HEADS, (2 * WIN - 1) * (2 * WIN - 1)), 1.0, 4.0, (), jnp.float32)
    r_wq = noise(seeds[10], (WIDTH, WIDTH), WIDTH ** -0.5, 0.25)
    r_wkv = noise(seeds[11], (WIDTH, 2 * WIDTH), WIDTH ** -0.5, 0.25)
    r_wo = noise(seeds[12], (WIDTH, WIDTH), WIDTH ** -0.5, 0.25)
    read_scale = jnp.clip(jnp.exp(jax.random.uniform(seeds[13], (HEADS,), jnp.float32, math.log(2.0), math.log(16.0))), 2.0, 16.0)
    floe_feat = noise(seeds[14], (DEVICES, FLOE_CAP, WIDTH), 1.0, 6.0, ((0, 128),))
    floe_count = uneven(seeds[15], DEVICES, DEVICES * FLOE_MEAN, FLOE_CAP, 2).astype(jnp.int32)
    floe_patch = draw_floe_patch(jax.random.fold_in(seeds[18], 71), 0)
    floe_cover = set_ends((jax.random.randint(seeds[17], (DEVICES, 3, FLOE_CAP), 0, 2) < 1).astype(jnp.int32), jax.random.fold_in(seeds[17], 1), 0, 1)
    return dict(wave_tokens=wave_tokens, grad_out=grad_out, w_qkv=w_qkv, w_proj=w_proj, w_fc1=w_fc1, w_fc2=w_fc2, gain_attn=gain_attn, gain_mlp=gain_mlp, attn_scale=attn_scale, bias_table=bias_table, r_wq=r_wq, r_wkv=r_wkv, r_wo=r_wo, read_scale=read_scale, floe_feat=floe_feat, floe_count=floe_count, floe_patch=floe_patch, floe_cover=floe_cover)


def layer_norm(values):
    centred = values - lax.optimization_barrier(jnp.mean(values, -1, keepdims=True))
    return centred / jnp.sqrt(lax.optimization_barrier(jnp.mean(centred * centred, -1, keepdims=True)) + 1e-05)

def unit_heads(values):
    return values / jnp.maximum(jnp.sqrt(lax.optimization_barrier(jnp.sum(values * values, -1, keepdims=True))), 1.0)

def bias_index(window):
    grid_pos = np.stack(np.meshgrid(np.arange(window), np.arange(window), indexing='ij')).reshape(2, -1)
    offsets = grid_pos[:, :, None] - grid_pos[:, None, :] + window - 1
    return offsets[0] * (2 * window - 1) + offsets[1]

def swin_block(field, w_qkv, w_proj, w_fc1, w_fc2, gain_attn, gain_mlp, attn_scale, bias_full):
    tok_rows, tok_cols, feat_width = field.shape
    head_count = attn_scale.shape[0]
    head_size = feat_width // head_count
    span = WIN * WIN
    windows = field.reshape(tok_rows // WIN, WIN, tok_cols // WIN, WIN, feat_width).transpose(0, 2, 1, 3, 4).reshape(-1, feat_width)
    win_count = windows.shape[0] // span
    qkv_all = jnp.dot(windows, w_qkv, preferred_element_type=jnp.float32).astype(jnp.bfloat16)
    qkv_all = lax.optimization_barrier(qkv_all)
    qkv_all = qkv_all.reshape(win_count, span, 3, head_count, head_size)
    queries = unit_heads(qkv_all[:, :, 0].astype(jnp.float32))
    keys_unit = unit_heads(qkv_all[:, :, 1].astype(jnp.float32))
    scores = jnp.einsum('wihd,wjhd->whij', queries, keys_unit, precision=lax.Precision.HIGHEST)
    scores = scores * attn_scale[None, :, None, None] + bias_full[None]
    expo = jnp.exp(scores)
    probs = (expo / lax.optimization_barrier(jnp.sum(expo, -1, keepdims=True))).astype(jnp.bfloat16)
    mixed = jnp.einsum('whij,wjhd->wihd', probs, qkv_all[:, :, 2], preferred_element_type=jnp.float32)
    mixed = mixed.astype(jnp.bfloat16).reshape(-1, feat_width)
    attn_out = jnp.dot(mixed, w_proj, preferred_element_type=jnp.float32)
    hidden_one = (windows.astype(jnp.float32) + layer_norm(attn_out) * gain_attn).astype(jnp.bfloat16)
    hidden_one = lax.optimization_barrier(hidden_one)
    inner = jax.nn.gelu(jnp.dot(hidden_one, w_fc1, preferred_element_type=jnp.float32), approximate=True).astype(jnp.bfloat16)
    mlp_out = jnp.dot(inner, w_fc2, preferred_element_type=jnp.float32)
    result = (hidden_one.astype(jnp.float32) + layer_norm(mlp_out) * gain_mlp).astype(jnp.bfloat16)
    result = result.reshape(tok_rows // WIN, tok_cols // WIN, WIN, WIN, feat_width).transpose(0, 2, 1, 3, 4)
    return result.reshape(tok_rows, tok_cols, feat_width)

def readout_mix(query, key_vals, flags, read_scale):
    floe_rows, feat_width = query.shape
    head_count = read_scale.shape[0]
    head_size = feat_width // head_count
    query_unit = unit_heads(query.astype(jnp.float32).reshape(floe_rows, head_count, head_size))
    key_unit = unit_heads(key_vals[:, :, :feat_width].astype(jnp.float32).reshape(floe_rows, 4, head_count, head_size))
    values = key_vals[:, :, feat_width:].astype(jnp.float32).reshape(floe_rows, 4, head_count, head_size)
    scores = lax.optimization_barrier(jnp.sum(query_unit[:, None] * key_unit, -1)) * read_scale
    expo = jnp.exp(scores) * flags[:, :, None]
    weights = expo / lax.optimization_barrier(jnp.sum(expo, 1, keepdims=True))
    return lax.optimization_barrier(jnp.sum(weights[..., None] * values, 1)).reshape(floe_rows, feat_width).astype(jnp.bfloat16)

def reference(wave_tokens, grad_out, w_qkv, w_proj, w_fc1, w_fc2, gain_attn, gain_mlp, attn_scale, bias_table, r_wq, r_wkv, r_wo, read_scale, floe_feat, floe_count, floe_patch, floe_cover):
    bias_full = bias_table[:, bias_index(WIN)]

    def local_block(field):
        return swin_block(field, w_qkv, w_proj, w_fc1, w_fc2, gain_attn, gain_mlp, attn_scale, bias_full)
    rolled = jnp.roll(wave_tokens, (-SHIFT, -SHIFT), (0, 1))
    cot_rolled = jnp.roll(grad_out, (-SHIFT, -SHIFT), (0, 1))

    def band_step(pair):
        band_in, band_cot = pair
        band_out, pull_back = jax.vjp(local_block, band_in)
        return (band_out, pull_back(band_cot)[0])
    band_out, band_grad = lax.map(band_step, (rolled.reshape(NROWS // WIN, WIN, NCOLS, WIDTH), cot_rolled.reshape(NROWS // WIN, WIN, NCOLS, WIDTH)))
    patch_out = jnp.roll(band_out.reshape(NROWS, NCOLS, WIDTH), (SHIFT, SHIFT), (0, 1))
    grad_in = jnp.roll(band_grad.reshape(NROWS, NCOLS, WIDTH), (SHIFT, SHIFT), (0, 1))
    key_all = jnp.dot(patch_out.reshape(-1, WIDTH), r_wkv, preferred_element_type=jnp.float32).astype(jnp.bfloat16)

    def floe_block(item):
        feat, live, patch, cover = item
        row_pos = patch // NCOLS
        col_pos = patch % NCOLS
        row_next = (row_pos + 1) % NROWS
        col_next = (col_pos + 1) % NCOLS
        index_set = jnp.stack([row_pos * NCOLS + col_pos, row_pos * NCOLS + col_next, row_next * NCOLS + col_pos, row_next * NCOLS + col_next], -1).astype(jnp.int32)
        key_vals = key_all[index_set]
        flags = jnp.stack([jnp.ones_like(cover[0]), cover[0], cover[1], cover[2]], -1).astype(jnp.float32)
        query = jnp.dot(feat, r_wq, preferred_element_type=jnp.float32).astype(jnp.bfloat16)
        floe_mix = readout_mix(query, key_vals, flags, read_scale)
        updated = feat.astype(jnp.float32) + jnp.dot(floe_mix, r_wo, preferred_element_type=jnp.float32)
        alive = jnp.arange(FLOE_CAP, dtype=jnp.int32) < live
        return jnp.where(alive[:, None], updated, 0.0).astype(jnp.bfloat16)
    floe_out = lax.map(floe_block, (floe_feat, floe_count, floe_patch, floe_cover))
    return (patch_out, grad_in, floe_out)
```

```python
import jax
import jax.numpy as jnp
import numpy as np
from jax import lax
from jax.sharding import PartitionSpec as P

WIN = 8
SHIFT = 4


def shifted(block, axis, distance):
    devices = range(lax.axis_size(axis))
    route = [((i - distance) % len(devices), i) for i in devices]
    return lax.ppermute(block, axis, route)


def layer_norm(values):
    centred = values - jnp.mean(values, -1, keepdims=True)
    return centred / jnp.sqrt(jnp.mean(centred * centred, -1, keepdims=True) + 1e-05)


def unit_heads(values):
    return values / jnp.maximum(jnp.sqrt(jnp.sum(values * values, -1, keepdims=True)), 1.0)


def bias_index(window):
    grid_pos = np.stack(np.meshgrid(np.arange(window), np.arange(window), indexing="ij")).reshape(
        2, -1
    )
    offsets = grid_pos[:, :, None] - grid_pos[:, None, :] + window - 1
    return offsets[0] * (2 * window - 1) + offsets[1]


def swin_block(field, w_qkv, w_proj, w_fc1, w_fc2, gain_attn, gain_mlp, attn_scale, bias_full):
    tok_rows, tok_cols, feat_width = field.shape
    head_count = attn_scale.shape[0]
    head_size = feat_width // head_count
    span = WIN * WIN
    windows = (
        field.reshape(tok_rows // WIN, WIN, tok_cols // WIN, WIN, feat_width)
        .transpose(0, 2, 1, 3, 4)
        .reshape(-1, feat_width)
    )
    win_count = windows.shape[0] // span
    qkv_all = jnp.dot(windows, w_qkv, preferred_element_type=jnp.float32).astype(jnp.bfloat16)
    qkv_all = lax.optimization_barrier(qkv_all)
    qkv_all = qkv_all.reshape(win_count, span, 3, head_count, head_size)
    queries = unit_heads(qkv_all[:, :, 0].astype(jnp.float32))
    keys_unit = unit_heads(qkv_all[:, :, 1].astype(jnp.float32))
    scores = jnp.einsum("wihd,wjhd->whij", queries, keys_unit, precision=lax.Precision.HIGHEST)
    scores = scores * attn_scale[None, :, None, None] + bias_full[None]
    expo = jnp.exp(scores)
    probs = (expo / jnp.sum(expo, -1, keepdims=True)).astype(jnp.bfloat16)
    mixed = jnp.einsum(
        "whij,wjhd->wihd", probs, qkv_all[:, :, 2], preferred_element_type=jnp.float32
    )
    mixed = mixed.astype(jnp.bfloat16).reshape(-1, feat_width)
    attn_out = jnp.dot(mixed, w_proj, preferred_element_type=jnp.float32)
    hidden_one = (windows.astype(jnp.float32) + layer_norm(attn_out) * gain_attn).astype(
        jnp.bfloat16
    )
    hidden_one = lax.optimization_barrier(hidden_one)
    inner = jax.nn.gelu(
        jnp.dot(hidden_one, w_fc1, preferred_element_type=jnp.float32), approximate=True
    ).astype(jnp.bfloat16)
    mlp_out = jnp.dot(inner, w_fc2, preferred_element_type=jnp.float32)
    result = (hidden_one.astype(jnp.float32) + layer_norm(mlp_out) * gain_mlp).astype(jnp.bfloat16)
    result = result.reshape(tok_rows // WIN, tok_cols // WIN, WIN, WIN, feat_width).transpose(
        0, 2, 1, 3, 4
    )
    return result.reshape(tok_rows, tok_cols, feat_width)


def readout_mix(query, key_vals, flags, read_scale):
    floe_rows, feat_width = query.shape
    head_count = read_scale.shape[0]
    head_size = feat_width // head_count
    query_unit = unit_heads(query.astype(jnp.float32).reshape(floe_rows, head_count, head_size))
    key_unit = unit_heads(
        key_vals[:, :, :feat_width].astype(jnp.float32).reshape(floe_rows, 4, head_count, head_size)
    )
    values = (
        key_vals[:, :, feat_width:].astype(jnp.float32).reshape(floe_rows, 4, head_count, head_size)
    )
    scores = jnp.sum(query_unit[:, None] * key_unit, -1) * read_scale
    expo = jnp.exp(scores) * flags[:, :, None]
    weights = expo / jnp.sum(expo, 1, keepdims=True)
    return (
        jnp.sum(weights[..., None] * values, 1).reshape(floe_rows, feat_width).astype(jnp.bfloat16)
    )


def pull_rows(pieces, offset):
    return shifted(pieces, "gx", offset)


def pull_cols(pieces, offset):
    return shifted(pieces, "gy", offset)


def roll_ahead(field):
    field = jnp.concatenate([field[SHIFT:], pull_rows(field[:SHIFT], -1)], 0)
    return jnp.concatenate([field[:, SHIFT:], pull_cols(field[:, :SHIFT], -1)], 1)


def roll_behind(field):
    field = jnp.concatenate([pull_rows(field[-SHIFT:], 1), field[:-SHIFT]], 0)
    return jnp.concatenate([pull_cols(field[:, -SHIFT:], 1), field[:, :-SHIFT]], 1)


def extend_rims(field):
    field = jnp.concatenate([field, pull_rows(field[:1], -1)], 0)
    return jnp.concatenate([field, pull_cols(field[:, :1], -1)], 1)


def one_hot(index, size, dtype=jnp.bfloat16):
    return (index[..., None] == jnp.arange(size, dtype=jnp.int32)).astype(dtype)


def exact_dot(a, b):
    return jnp.dot(a, b, precision=lax.Precision.HIGHEST, preferred_element_type=jnp.float32)


def pick_dot(a, b):
    return jnp.dot(a, b, preferred_element_type=jnp.float32)


def bias_matrix(bias_table, window):
    span = window * window
    flat = jnp.arange(span * span, dtype=jnp.int32)
    query_at = flat // span
    key_at = flat % span
    row_step = query_at // window - key_at // window + window - 1
    col_step = query_at % window - key_at % window + window - 1
    table_at = row_step * (2 * window - 1) + col_step
    picks = one_hot(table_at, bias_table.shape[1], jnp.float32)
    return exact_dot(bias_table, picks.T).reshape(bias_table.shape[0], span, span)


def head_sum(values, head_mat):
    return exact_dot(values, head_mat)


def unit_rows(values, head_mat):
    norms = jnp.maximum(jnp.sqrt(head_sum(values * values, head_mat)), 1.0)
    return values / exact_dot(norms, head_mat.T)


def local(
    wave_tokens,
    grad_out,
    w_qkv,
    w_proj,
    w_fc1,
    w_fc2,
    gain_attn,
    gain_mlp,
    attn_scale,
    bias_table,
    r_wq,
    r_wkv,
    r_wo,
    read_scale,
    floe_feat,
    floe_count,
    floe_patch,
    floe_cover,
):
    tok_rows, tok_cols, feat_width = wave_tokens.shape
    head_count = read_scale.shape[0]
    head_size = feat_width // head_count
    bias_full = bias_matrix(bias_table, WIN)

    def local_block(field):
        return swin_block(
            field, w_qkv, w_proj, w_fc1, w_fc2, gain_attn, gain_mlp, attn_scale, bias_full
        )

    both = roll_ahead(jnp.concatenate([wave_tokens, grad_out], -1))
    ahead = both[..., :feat_width]
    cot_ahead = both[..., feat_width:]
    out_ahead, pull_back = jax.vjp(local_block, ahead)
    grad_ahead = pull_back(cot_ahead)[0]
    both_out = roll_behind(jnp.concatenate([out_ahead, grad_ahead], -1))
    patch_out = both_out[..., :feat_width]
    grad_in = both_out[..., feat_width:]
    key_vals = jnp.dot(
        patch_out.reshape(-1, feat_width), r_wkv, preferred_element_type=jnp.float32
    ).astype(jnp.bfloat16)
    key_ext = extend_rims(key_vals.reshape(tok_rows, tok_cols, 2 * feat_width))
    ext_cols = tok_cols + 1
    ext_cells = (tok_rows + 1) * ext_cols
    key_table = key_ext.reshape(ext_cells, 2 * feat_width)
    row_devs = lax.axis_size("gx")
    col_devs = lax.axis_size("gy")
    dev_total = row_devs * col_devs
    grid_cols = tok_cols * col_devs
    feat = floe_feat[0]
    floe_slots = feat.shape[0]
    slot_size = floe_slots // dev_total
    patch = floe_patch[0]
    cover = floe_cover[0]
    row_pos = patch // grid_cols
    col_pos = patch % grid_cols
    target = row_pos // tok_rows * col_devs + col_pos // tok_cols
    targets = one_hot(target, dev_total)
    lower = (
        jnp.arange(floe_slots, dtype=jnp.int32)[:, None]
        >= jnp.arange(floe_slots, dtype=jnp.int32)[None, :]
    ).astype(jnp.bfloat16)
    running = pick_dot(lower, targets)
    rank = jnp.sum(running * targets.astype(jnp.float32), -1).astype(jnp.int32) - 1
    place = target * slot_size + rank
    scatter = one_hot(place, floe_slots).T
    meta_width = 128
    meta = jnp.stack(
        [row_pos % tok_rows, col_pos % tok_cols, cover[0], cover[1], cover[2]], -1
    ).astype(jnp.bfloat16)
    meta = jnp.pad(meta, ((0, 0), (0, meta_width - meta.shape[1])))
    query = jnp.dot(feat, r_wq, preferred_element_type=jnp.float32).astype(jnp.bfloat16)
    packed = pick_dot(scatter, jnp.concatenate([query, meta], -1)).astype(jnp.bfloat16)
    piece = lax.all_to_all(
        packed.reshape(dev_total, slot_size, feat_width + meta_width),
        ("gx", "gy"),
        split_axis=0,
        concat_axis=0,
        tiled=True,
    ).reshape(floe_slots, feat_width + meta_width)
    got_query = piece[:, :feat_width].astype(jnp.float32)
    got_meta = piece[:, feat_width:].astype(jnp.float32).astype(jnp.int32)
    cell_row = got_meta[:, 0]
    cell_col = got_meta[:, 1]
    ones = jnp.ones_like(cell_row)
    flags = jnp.stack([ones, got_meta[:, 2], got_meta[:, 3], got_meta[:, 4]], 0).astype(
        jnp.float32
    )
    corner_rows = jnp.stack([cell_row, cell_row, cell_row + 1, cell_row + 1], 0)
    corner_cols = jnp.stack([cell_col, cell_col + 1, cell_col, cell_col + 1], 0)
    corner_at = (corner_rows * ext_cols + corner_cols).reshape(-1)
    corner_vals = pick_dot(one_hot(corner_at, ext_cells), key_table)
    head_mat = (
        jnp.arange(feat_width, dtype=jnp.int32)[:, None] // head_size
        == jnp.arange(head_count, dtype=jnp.int32)[None, :]
    ).astype(jnp.float32)
    query_unit = unit_rows(got_query, head_mat)
    keys_unit = unit_rows(corner_vals[:, :feat_width], head_mat).reshape(4, floe_slots, feat_width)
    values = corner_vals[:, feat_width:].reshape(4, floe_slots, feat_width)
    scores = head_sum(
        (query_unit[None] * keys_unit).reshape(4 * floe_slots, feat_width), head_mat
    ).reshape(4, floe_slots, head_count)
    expo = jnp.exp(scores * read_scale) * flags[:, :, None]
    weights = expo / jnp.sum(expo, 0, keepdims=True)
    spread = exact_dot(weights.reshape(4 * floe_slots, head_count), head_mat.T).reshape(
        4, floe_slots, feat_width
    )
    floe_mix = jnp.sum(spread * values, 0).astype(jnp.bfloat16)
    returned = lax.all_to_all(
        floe_mix.reshape(dev_total, slot_size, feat_width),
        ("gx", "gy"),
        split_axis=0,
        concat_axis=0,
        tiled=True,
    ).reshape(floe_slots, feat_width)
    floe_mix = pick_dot(scatter.T, returned).astype(jnp.bfloat16)
    updated = feat.astype(jnp.float32) + jnp.dot(floe_mix, r_wo, preferred_element_type=jnp.float32)
    alive = jnp.arange(floe_slots, dtype=jnp.int32) < floe_count[0]
    floe_out = jnp.where(alive[:, None], updated, 0.0).astype(jnp.bfloat16)[None]
    return (patch_out, grad_in, floe_out)


def solution(mesh):
    in_specs = (
        P("gx", "gy", None),
        P("gx", "gy", None),
        P(),
        P(),
        P(),
        P(),
        P(),
        P(),
        P(),
        P(),
        P(),
        P(),
        P(),
        P(),
        P(("gx", "gy"), None, None),
        P(("gx", "gy")),
        P(("gx", "gy"), None),
        P(("gx", "gy"), None, None),
    )
    out_specs = (P("gx", "gy", None), P("gx", "gy", None), P(("gx", "gy"), None, None))
    return jax.shard_map(local, mesh=mesh, in_specs=in_specs, out_specs=out_specs, check_vma=False)
```

```python
import jax
import jax.numpy as jnp
import numpy as np
from jax import lax
from jax.sharding import PartitionSpec as P

WIN = 8
SHIFT = 4


def shifted(block, axis, distance):
    devices = range(lax.axis_size(axis))
    route = [((i - distance) % len(devices), i) for i in devices]
    return lax.ppermute(block, axis, route)


def layer_norm(values):
    centred = values - jnp.mean(values, -1, keepdims=True)
    return centred / jnp.sqrt(jnp.mean(centred * centred, -1, keepdims=True) + 1e-05)


def unit_heads(values):
    return values / jnp.maximum(jnp.sqrt(jnp.sum(values * values, -1, keepdims=True)), 1.0)


def bias_index(window):
    grid_pos = np.stack(np.meshgrid(np.arange(window), np.arange(window), indexing="ij")).reshape(
        2, -1
    )
    offsets = grid_pos[:, :, None] - grid_pos[:, None, :] + window - 1
    return offsets[0] * (2 * window - 1) + offsets[1]


def swin_block(field, w_qkv, w_proj, w_fc1, w_fc2, gain_attn, gain_mlp, attn_scale, bias_full):
    tok_rows, tok_cols, feat_width = field.shape
    head_count = attn_scale.shape[0]
    head_size = feat_width // head_count
    span = WIN * WIN
    windows = (
        field.reshape(tok_rows // WIN, WIN, tok_cols // WIN, WIN, feat_width)
        .transpose(0, 2, 1, 3, 4)
        .reshape(-1, feat_width)
    )
    win_count = windows.shape[0] // span
    qkv_all = jnp.dot(windows, w_qkv, preferred_element_type=jnp.float32).astype(jnp.bfloat16)
    qkv_all = lax.optimization_barrier(qkv_all)
    qkv_all = qkv_all.reshape(win_count, span, 3, head_count, head_size)
    queries = unit_heads(qkv_all[:, :, 0].astype(jnp.float32))
    keys_unit = unit_heads(qkv_all[:, :, 1].astype(jnp.float32))
    scores = jnp.einsum("wihd,wjhd->whij", queries, keys_unit, precision=lax.Precision.HIGHEST)
    scores = scores * attn_scale[None, :, None, None] + bias_full[None]
    expo = jnp.exp(scores)
    probs = (expo / jnp.sum(expo, -1, keepdims=True)).astype(jnp.bfloat16)
    mixed = jnp.einsum(
        "whij,wjhd->wihd", probs, qkv_all[:, :, 2], preferred_element_type=jnp.float32
    )
    mixed = mixed.astype(jnp.bfloat16).reshape(-1, feat_width)
    attn_out = jnp.dot(mixed, w_proj, preferred_element_type=jnp.float32)
    hidden_one = (windows.astype(jnp.float32) + layer_norm(attn_out) * gain_attn).astype(
        jnp.bfloat16
    )
    hidden_one = lax.optimization_barrier(hidden_one)
    inner = jax.nn.gelu(
        jnp.dot(hidden_one, w_fc1, preferred_element_type=jnp.float32), approximate=True
    ).astype(jnp.bfloat16)
    mlp_out = jnp.dot(inner, w_fc2, preferred_element_type=jnp.float32)
    result = (hidden_one.astype(jnp.float32) + layer_norm(mlp_out) * gain_mlp).astype(jnp.bfloat16)
    result = result.reshape(tok_rows // WIN, tok_cols // WIN, WIN, WIN, feat_width).transpose(
        0, 2, 1, 3, 4
    )
    return result.reshape(tok_rows, tok_cols, feat_width)


def readout_mix(query, key_vals, flags, read_scale):
    floe_rows, feat_width = query.shape
    head_count = read_scale.shape[0]
    head_size = feat_width // head_count
    query_unit = unit_heads(query.astype(jnp.float32).reshape(floe_rows, head_count, head_size))
    key_unit = unit_heads(
        key_vals[:, :, :feat_width].astype(jnp.float32).reshape(floe_rows, 4, head_count, head_size)
    )
    values = (
        key_vals[:, :, feat_width:].astype(jnp.float32).reshape(floe_rows, 4, head_count, head_size)
    )
    scores = jnp.sum(query_unit[:, None] * key_unit, -1) * read_scale
    expo = jnp.exp(scores) * flags[:, :, None]
    weights = expo / jnp.sum(expo, 1, keepdims=True)
    return (
        jnp.sum(weights[..., None] * values, 1).reshape(floe_rows, feat_width).astype(jnp.bfloat16)
    )


def pull_rows(pieces, offset):
    return shifted(pieces, "gx", offset)


def pull_cols(pieces, offset):
    return shifted(pieces, "gy", offset)


def pull_diag(pieces, offset):
    row_devs = lax.axis_size("gx")
    col_devs = lax.axis_size("gy")
    route = [
        (((i - offset) % row_devs) * col_devs + (j - offset) % col_devs, i * col_devs + j)
        for i in range(row_devs)
        for j in range(col_devs)
    ]
    return lax.ppermute(pieces, ("gx", "gy"), route)


def roll_ahead(field):
    own = field[SHIFT:, SHIFT:]
    right = pull_cols(field[SHIFT:, :SHIFT], -1)
    below = pull_rows(field[:SHIFT, SHIFT:], -1)
    corner = pull_diag(field[:SHIFT, :SHIFT], -1)
    return jnp.concatenate(
        [jnp.concatenate([own, right], 1), jnp.concatenate([below, corner], 1)], 0
    )


def roll_behind(field, extra):
    tok_rows, tok_cols = field.shape[:2]
    keep_rows = tok_rows - SHIFT + extra
    keep_cols = tok_cols - SHIFT + extra
    corner = pull_diag(field[tok_rows - SHIFT :, tok_cols - SHIFT :], 1)
    above = pull_rows(field[tok_rows - SHIFT :, :keep_cols], 1)
    left = pull_cols(field[:keep_rows, tok_cols - SHIFT :], 1)
    own = field[:keep_rows, :keep_cols]
    return jnp.concatenate(
        [jnp.concatenate([corner, above], 1), jnp.concatenate([left, own], 1)], 0
    )


def one_hot(index, size, dtype=jnp.bfloat16):
    return (index[..., None] == jnp.arange(size, dtype=jnp.int32)).astype(dtype)


def exact_dot(a, b):
    return jnp.dot(a, b, precision=lax.Precision.HIGHEST, preferred_element_type=jnp.float32)


def pick_dot(a, b):
    return jnp.dot(a, b, preferred_element_type=jnp.float32)


def bias_matrix(bias_table, window):
    span = window * window
    flat = jnp.arange(span * span, dtype=jnp.int32)
    query_at = flat // span
    key_at = flat % span
    row_step = query_at // window - key_at // window + window - 1
    col_step = query_at % window - key_at % window + window - 1
    table_at = row_step * (2 * window - 1) + col_step
    picks = one_hot(table_at, bias_table.shape[1], jnp.float32)
    return exact_dot(bias_table, picks.T).reshape(bias_table.shape[0], span, span)


def head_sum(values, head_mat):
    return exact_dot(values, head_mat)


def unit_rows(values, head_mat):
    norms = jnp.maximum(jnp.sqrt(head_sum(values * values, head_mat)), 1.0)
    return values / exact_dot(norms, head_mat.T)


def local(
    wave_tokens,
    grad_out,
    w_qkv,
    w_proj,
    w_fc1,
    w_fc2,
    gain_attn,
    gain_mlp,
    attn_scale,
    bias_table,
    r_wq,
    r_wkv,
    r_wo,
    read_scale,
    floe_feat,
    floe_count,
    floe_patch,
    floe_cover,
):
    tok_rows, tok_cols, feat_width = wave_tokens.shape
    head_count = read_scale.shape[0]
    head_size = feat_width // head_count
    bias_full = bias_matrix(bias_table, WIN)

    def local_block(field):
        return swin_block(
            field, w_qkv, w_proj, w_fc1, w_fc2, gain_attn, gain_mlp, attn_scale, bias_full
        )

    both = roll_ahead(jnp.concatenate([wave_tokens, grad_out], -1))
    ahead = both[..., :feat_width]
    cot_ahead = both[..., feat_width:]
    out_ahead, pull_back = jax.vjp(local_block, ahead)
    out_ext = roll_behind(out_ahead, 1)
    patch_out = out_ext[:tok_rows, :tok_cols]
    ext_cols = tok_cols + 1
    ext_cells = (tok_rows + 1) * ext_cols
    key_table = jnp.dot(
        out_ext.reshape(ext_cells, feat_width), r_wkv, preferred_element_type=jnp.float32
    ).astype(jnp.bfloat16)
    row_devs = lax.axis_size("gx")
    col_devs = lax.axis_size("gy")
    dev_total = row_devs * col_devs
    grid_cols = tok_cols * col_devs
    feat = floe_feat[0]
    floe_slots = feat.shape[0]
    slot_size = floe_slots // dev_total
    patch = floe_patch[0]
    cover = floe_cover[0]
    row_pos = patch // grid_cols
    col_pos = patch % grid_cols
    target = row_pos // tok_rows * col_devs + col_pos // tok_cols
    targets = one_hot(target, dev_total)
    lower = (
        jnp.arange(floe_slots, dtype=jnp.int32)[:, None]
        >= jnp.arange(floe_slots, dtype=jnp.int32)[None, :]
    ).astype(jnp.bfloat16)
    running = pick_dot(lower, targets)
    rank = jnp.sum(running * targets.astype(jnp.float32), -1).astype(jnp.int32) - 1
    place = target * slot_size + rank
    scatter = one_hot(place, floe_slots).T
    meta_width = 128
    meta = jnp.stack(
        [row_pos % tok_rows, col_pos % tok_cols, cover[0], cover[1], cover[2]], -1
    ).astype(jnp.bfloat16)
    meta = jnp.pad(meta, ((0, 0), (0, meta_width - meta.shape[1])))
    query = jnp.dot(feat, r_wq, preferred_element_type=jnp.float32).astype(jnp.bfloat16)
    packed = pick_dot(scatter, jnp.concatenate([query, meta], -1)).astype(jnp.bfloat16)
    piece = lax.all_to_all(
        packed.reshape(dev_total, slot_size, feat_width + meta_width),
        ("gx", "gy"),
        split_axis=0,
        concat_axis=0,
        tiled=True,
    ).reshape(floe_slots, feat_width + meta_width)
    got_query = piece[:, :feat_width].astype(jnp.float32)
    got_meta = piece[:, feat_width:].astype(jnp.float32).astype(jnp.int32)
    cell_row = got_meta[:, 0]
    cell_col = got_meta[:, 1]
    ones = jnp.ones_like(cell_row)
    flags = jnp.stack([ones, got_meta[:, 2], got_meta[:, 3], got_meta[:, 4]], 0).astype(
        jnp.float32
    )
    corner_rows = jnp.stack([cell_row, cell_row, cell_row + 1, cell_row + 1], 0)
    corner_cols = jnp.stack([cell_col, cell_col + 1, cell_col, cell_col + 1], 0)
    corner_at = (corner_rows * ext_cols + corner_cols).reshape(-1)
    corner_vals = pick_dot(one_hot(corner_at, ext_cells), key_table)
    head_mat = (
        jnp.arange(feat_width, dtype=jnp.int32)[:, None] // head_size
        == jnp.arange(head_count, dtype=jnp.int32)[None, :]
    ).astype(jnp.float32)
    query_unit = unit_rows(got_query, head_mat)
    keys_unit = unit_rows(corner_vals[:, :feat_width], head_mat).reshape(4, floe_slots, feat_width)
    values = corner_vals[:, feat_width:].reshape(4, floe_slots, feat_width)
    scores = head_sum(
        (query_unit[None] * keys_unit).reshape(4 * floe_slots, feat_width), head_mat
    ).reshape(4, floe_slots, head_count)
    expo = jnp.exp(scores * read_scale) * flags[:, :, None]
    weights = expo / jnp.sum(expo, 0, keepdims=True)
    spread = exact_dot(weights.reshape(4 * floe_slots, head_count), head_mat.T).reshape(
        4, floe_slots, feat_width
    )
    floe_mix = jnp.sum(spread * values, 0).astype(jnp.bfloat16)
    floe_mix, cot_ahead = lax.optimization_barrier((floe_mix, cot_ahead))
    returned = lax.all_to_all(
        floe_mix.reshape(dev_total, slot_size, feat_width),
        ("gx", "gy"),
        split_axis=0,
        concat_axis=0,
        tiled=True,
    ).reshape(floe_slots, feat_width)
    grad_ahead = pull_back(cot_ahead)[0]
    grad_in = roll_behind(grad_ahead, 0)
    floe_mix = pick_dot(scatter.T, returned).astype(jnp.bfloat16)
    updated = feat.astype(jnp.float32) + jnp.dot(floe_mix, r_wo, preferred_element_type=jnp.float32)
    alive = jnp.arange(floe_slots, dtype=jnp.int32) < floe_count[0]
    floe_out = jnp.where(alive[:, None], updated, 0.0).astype(jnp.bfloat16)[None]
    return (patch_out, grad_in, floe_out)


def solution(mesh):
    in_specs = (
        P("gx", "gy", None),
        P("gx", "gy", None),
        P(),
        P(),
        P(),
        P(),
        P(),
        P(),
        P(),
        P(),
        P(),
        P(),
        P(),
        P(),
        P(("gx", "gy"), None, None),
        P(("gx", "gy")),
        P(("gx", "gy"), None),
        P(("gx", "gy"), None, None),
    )
    out_specs = (P("gx", "gy", None), P("gx", "gy", None), P(("gx", "gy"), None, None))
    return jax.shard_map(local, mesh=mesh, in_specs=in_specs, out_specs=out_specs, check_vma=False)
```

```python
import jax
import jax.numpy as jnp
import numpy as np
from jax import lax
from jax.sharding import PartitionSpec as P

WIN = 8
SHIFT = 4


def shifted(block, axis, distance):
    devices = range(lax.axis_size(axis))
    route = [((i - distance) % len(devices), i) for i in devices]
    return lax.ppermute(block, axis, route)


def layer_norm(values):
    centred = values - jnp.mean(values, -1, keepdims=True)
    return centred / jnp.sqrt(jnp.mean(centred * centred, -1, keepdims=True) + 1e-05)


def unit_heads(values):
    return values / jnp.maximum(jnp.sqrt(jnp.sum(values * values, -1, keepdims=True)), 1.0)


def bias_index(window):
    grid_pos = np.stack(np.meshgrid(np.arange(window), np.arange(window), indexing="ij")).reshape(
        2, -1
    )
    offsets = grid_pos[:, :, None] - grid_pos[:, None, :] + window - 1
    return offsets[0] * (2 * window - 1) + offsets[1]


def swin_block(field, w_qkv, w_proj, w_fc1, w_fc2, gain_attn, gain_mlp, attn_scale, bias_full):
    tok_rows, tok_cols, feat_width = field.shape
    head_count = attn_scale.shape[0]
    head_size = feat_width // head_count
    span = WIN * WIN
    windows = (
        field.reshape(tok_rows // WIN, WIN, tok_cols // WIN, WIN, feat_width)
        .transpose(0, 2, 1, 3, 4)
        .reshape(-1, feat_width)
    )
    win_count = windows.shape[0] // span
    qkv_all = jnp.dot(windows, w_qkv, preferred_element_type=jnp.float32).astype(jnp.bfloat16)
    qkv_all = lax.optimization_barrier(qkv_all)
    qkv_all = qkv_all.reshape(win_count, span, 3, head_count, head_size)
    queries = unit_heads(qkv_all[:, :, 0].astype(jnp.float32))
    keys_unit = unit_heads(qkv_all[:, :, 1].astype(jnp.float32))
    scores = jnp.einsum("wihd,wjhd->whij", queries, keys_unit, precision=lax.Precision.HIGHEST)
    scores = scores * attn_scale[None, :, None, None] + bias_full[None]
    expo = jnp.exp(scores)
    probs = (expo / jnp.sum(expo, -1, keepdims=True)).astype(jnp.bfloat16)
    mixed = jnp.einsum(
        "whij,wjhd->wihd", probs, qkv_all[:, :, 2], preferred_element_type=jnp.float32
    )
    mixed = mixed.astype(jnp.bfloat16).reshape(-1, feat_width)
    attn_out = jnp.dot(mixed, w_proj, preferred_element_type=jnp.float32)
    hidden_one = (windows.astype(jnp.float32) + layer_norm(attn_out) * gain_attn).astype(
        jnp.bfloat16
    )
    hidden_one = lax.optimization_barrier(hidden_one)
    inner = jax.nn.gelu(
        jnp.dot(hidden_one, w_fc1, preferred_element_type=jnp.float32), approximate=True
    ).astype(jnp.bfloat16)
    mlp_out = jnp.dot(inner, w_fc2, preferred_element_type=jnp.float32)
    result = (hidden_one.astype(jnp.float32) + layer_norm(mlp_out) * gain_mlp).astype(jnp.bfloat16)
    result = result.reshape(tok_rows // WIN, tok_cols // WIN, WIN, WIN, feat_width).transpose(
        0, 2, 1, 3, 4
    )
    return result.reshape(tok_rows, tok_cols, feat_width)


def readout_mix(query, key_vals, flags, read_scale):
    floe_rows, feat_width = query.shape
    head_count = read_scale.shape[0]
    head_size = feat_width // head_count
    query_unit = unit_heads(query.astype(jnp.float32).reshape(floe_rows, head_count, head_size))
    key_unit = unit_heads(
        key_vals[:, :, :feat_width].astype(jnp.float32).reshape(floe_rows, 4, head_count, head_size)
    )
    values = (
        key_vals[:, :, feat_width:].astype(jnp.float32).reshape(floe_rows, 4, head_count, head_size)
    )
    scores = jnp.sum(query_unit[:, None] * key_unit, -1) * read_scale
    expo = jnp.exp(scores) * flags[:, :, None]
    weights = expo / jnp.sum(expo, 1, keepdims=True)
    return (
        jnp.sum(weights[..., None] * values, 1).reshape(floe_rows, feat_width).astype(jnp.bfloat16)
    )


def pull_rows(pieces, offset):
    return shifted(pieces, "gx", offset)


def pull_cols(pieces, offset):
    return shifted(pieces, "gy", offset)


def pull_diag(pieces, offset):
    row_devs = lax.axis_size("gx")
    col_devs = lax.axis_size("gy")
    route = [
        (((i - offset) % row_devs) * col_devs + (j - offset) % col_devs, i * col_devs + j)
        for i in range(row_devs)
        for j in range(col_devs)
    ]
    return lax.ppermute(pieces, ("gx", "gy"), route)


def roll_ahead(field):
    own = field[SHIFT:, SHIFT:]
    right = pull_cols(field[SHIFT:, :SHIFT], -1)
    below = pull_rows(field[:SHIFT, SHIFT:], -1)
    corner = pull_diag(field[:SHIFT, :SHIFT], -1)
    return jnp.concatenate(
        [jnp.concatenate([own, right], 1), jnp.concatenate([below, corner], 1)], 0
    )


def roll_behind(field, extra):
    tok_rows, tok_cols = field.shape[:2]
    keep_rows = tok_rows - SHIFT + extra
    keep_cols = tok_cols - SHIFT + extra
    corner = pull_diag(field[tok_rows - SHIFT :, tok_cols - SHIFT :], 1)
    above = pull_rows(field[tok_rows - SHIFT :, :keep_cols], 1)
    left = pull_cols(field[:keep_rows, tok_cols - SHIFT :], 1)
    own = field[:keep_rows, :keep_cols]
    return jnp.concatenate(
        [jnp.concatenate([corner, above], 1), jnp.concatenate([left, own], 1)], 0
    )


def one_hot(index, size, dtype=jnp.bfloat16):
    return (index[..., None] == jnp.arange(size, dtype=jnp.int32)).astype(dtype)


def exact_dot(a, b):
    return jnp.dot(a, b, precision=lax.Precision.HIGHEST, preferred_element_type=jnp.float32)


def pick_dot(a, b):
    return jnp.dot(a, b, preferred_element_type=jnp.float32)


def bias_matrix(bias_table, window):
    span = window * window
    flat = jnp.arange(span * span, dtype=jnp.int32)
    query_at = flat // span
    key_at = flat % span
    row_step = query_at // window - key_at // window + window - 1
    col_step = query_at % window - key_at % window + window - 1
    table_at = row_step * (2 * window - 1) + col_step
    picks = one_hot(table_at, bias_table.shape[1], jnp.float32)
    return exact_dot(bias_table, picks.T).reshape(bias_table.shape[0], span, span)


def head_sum(values, head_mat):
    return exact_dot(values, head_mat)


def unit_rows(values, head_mat):
    norms = jnp.maximum(jnp.sqrt(head_sum(values * values, head_mat)), 1.0)
    return values / exact_dot(norms, head_mat.T)


def unit_cols(values):
    norms = jnp.maximum(jnp.sqrt(jnp.sum(values * values, 1, keepdims=True)), 1.0)
    return values / norms


def local(
    wave_tokens,
    grad_out,
    w_qkv,
    w_proj,
    w_fc1,
    w_fc2,
    gain_attn,
    gain_mlp,
    attn_scale,
    bias_table,
    r_wq,
    r_wkv,
    r_wo,
    read_scale,
    floe_feat,
    floe_count,
    floe_patch,
    floe_cover,
):
    tok_rows, tok_cols, feat_width = wave_tokens.shape
    head_count = read_scale.shape[0]
    head_size = feat_width // head_count
    bias_full = bias_matrix(bias_table, WIN)

    def local_block(field):
        return swin_block(
            field, w_qkv, w_proj, w_fc1, w_fc2, gain_attn, gain_mlp, attn_scale, bias_full
        )

    both = roll_ahead(jnp.concatenate([wave_tokens, grad_out], -1))
    ahead = both[..., :feat_width]
    cot_ahead = both[..., feat_width:]
    out_ahead, pull_back = jax.vjp(local_block, ahead)
    out_ext = roll_behind(out_ahead, 1)
    patch_out = out_ext[:tok_rows, :tok_cols]
    ext_cols = tok_cols + 1
    ext_cells = (tok_rows + 1) * ext_cols
    key_table = jnp.dot(
        out_ext.reshape(ext_cells, feat_width), r_wkv, preferred_element_type=jnp.float32
    ).astype(jnp.bfloat16)
    row_devs = lax.axis_size("gx")
    col_devs = lax.axis_size("gy")
    dev_total = row_devs * col_devs
    grid_cols = tok_cols * col_devs
    feat = floe_feat[0]
    floe_slots = feat.shape[0]
    slot_size = floe_slots // dev_total
    patch = floe_patch[0]
    cover = floe_cover[0]
    row_pos = patch // grid_cols
    col_pos = patch % grid_cols
    target = row_pos // tok_rows * col_devs + col_pos // tok_cols
    targets = one_hot(target, dev_total)
    lower = (
        jnp.arange(floe_slots, dtype=jnp.int32)[:, None]
        >= jnp.arange(floe_slots, dtype=jnp.int32)[None, :]
    ).astype(jnp.bfloat16)
    running = pick_dot(lower, targets)
    rank = jnp.sum(running * targets.astype(jnp.float32), -1).astype(jnp.int32) - 1
    place = target * slot_size + rank
    scatter = one_hot(place, floe_slots).T
    meta_width = 128
    meta = jnp.stack(
        [row_pos % tok_rows, col_pos % tok_cols, cover[0], cover[1], cover[2]], -1
    ).astype(jnp.bfloat16)
    meta = jnp.pad(meta, ((0, 0), (0, meta_width - meta.shape[1])))
    query = jnp.dot(feat, r_wq, preferred_element_type=jnp.float32).astype(jnp.bfloat16)
    packed = pick_dot(scatter, jnp.concatenate([query, meta], -1)).astype(jnp.bfloat16)
    piece = lax.all_to_all(
        packed.reshape(dev_total, slot_size, feat_width + meta_width),
        ("gx", "gy"),
        split_axis=0,
        concat_axis=0,
        tiled=True,
    ).reshape(floe_slots, feat_width + meta_width)
    piece_t = piece.T
    got_query = piece_t[:feat_width].astype(jnp.float32)
    got_meta = piece_t[feat_width:].astype(jnp.float32).astype(jnp.int32)
    cell_row = got_meta[0]
    cell_col = got_meta[1]
    ones = jnp.ones_like(cell_row)
    flags = jnp.stack([ones, got_meta[2], got_meta[3], got_meta[4]], 0).astype(jnp.float32)
    corner_rows = jnp.stack([cell_row, cell_row, cell_row + 1, cell_row + 1], 0)
    corner_cols = jnp.stack([cell_col, cell_col + 1, cell_col, cell_col + 1], 0)
    corner_at = (corner_rows * ext_cols + corner_cols).reshape(-1)
    picks = (
        jnp.arange(ext_cells, dtype=jnp.int32)[:, None] == corner_at[None, :]
    ).astype(jnp.bfloat16)
    corner_vals = lax.dot_general(
        key_table, picks, (((0,), (0,)), ((), ())), preferred_element_type=jnp.bfloat16
    ).astype(jnp.float32)
    query_unit = unit_cols(got_query.reshape(head_count, head_size, floe_slots))
    keys_unit = unit_cols(
        corner_vals[:feat_width].reshape(head_count, head_size, 4 * floe_slots)
    ).reshape(head_count, head_size, 4, floe_slots)
    values = corner_vals[feat_width:].reshape(head_count, head_size, 4, floe_slots)
    scores = jnp.sum(query_unit[:, :, None] * keys_unit, 1)
    expo = jnp.exp(scores * read_scale[:, None, None]) * flags[None]
    weights = expo / jnp.sum(expo, 1, keepdims=True)
    floe_mix = jnp.sum(weights[:, None] * values, 2).reshape(feat_width, floe_slots)
    floe_mix = floe_mix.astype(jnp.bfloat16).T
    floe_mix, cot_ahead = lax.optimization_barrier((floe_mix, cot_ahead))
    returned = lax.all_to_all(
        floe_mix.reshape(dev_total, slot_size, feat_width),
        ("gx", "gy"),
        split_axis=0,
        concat_axis=0,
        tiled=True,
    ).reshape(floe_slots, feat_width)
    grad_ahead = pull_back(cot_ahead)[0]
    grad_in = roll_behind(grad_ahead, 0)
    floe_mix = pick_dot(scatter.T, returned).astype(jnp.bfloat16)
    updated = feat.astype(jnp.float32) + jnp.dot(floe_mix, r_wo, preferred_element_type=jnp.float32)
    alive = jnp.arange(floe_slots, dtype=jnp.int32) < floe_count[0]
    floe_out = jnp.where(alive[:, None], updated, 0.0).astype(jnp.bfloat16)[None]
    return (patch_out, grad_in, floe_out)


def solution(mesh):
    in_specs = (
        P("gx", "gy", None),
        P("gx", "gy", None),
        P(),
        P(),
        P(),
        P(),
        P(),
        P(),
        P(),
        P(),
        P(),
        P(),
        P(),
        P(),
        P(("gx", "gy"), None, None),
        P(("gx", "gy")),
        P(("gx", "gy"), None),
        P(("gx", "gy"), None, None),
    )
    out_specs = (P("gx", "gy", None), P("gx", "gy", None), P(("gx", "gy"), None, None))
    return jax.shard_map(local, mesh=mesh, in_specs=in_specs, out_specs=out_specs, check_vma=False)
```

```python
import jax
import jax.numpy as jnp
import numpy as np
from jax import lax
from jax.sharding import PartitionSpec as P

WIN = 8
SHIFT = 4


def shifted(block, axis, distance):
    devices = range(lax.axis_size(axis))
    route = [((i - distance) % len(devices), i) for i in devices]
    return lax.ppermute(block, axis, route)


def layer_norm(values):
    centred = values - jnp.mean(values, -1, keepdims=True)
    return centred / jnp.sqrt(jnp.mean(centred * centred, -1, keepdims=True) + 1e-05)


def unit_heads(values):
    return values / jnp.maximum(jnp.sqrt(jnp.sum(values * values, -1, keepdims=True)), 1.0)


def bias_index(window):
    grid_pos = np.stack(np.meshgrid(np.arange(window), np.arange(window), indexing="ij")).reshape(
        2, -1
    )
    offsets = grid_pos[:, :, None] - grid_pos[:, None, :] + window - 1
    return offsets[0] * (2 * window - 1) + offsets[1]


def swin_block(field, w_qkv, w_proj, w_fc1, w_fc2, gain_attn, gain_mlp, attn_scale, bias_full):
    tok_rows, tok_cols, feat_width = field.shape
    head_count = attn_scale.shape[0]
    head_size = feat_width // head_count
    span = WIN * WIN
    windows = (
        field.reshape(tok_rows // WIN, WIN, tok_cols // WIN, WIN, feat_width)
        .transpose(0, 2, 1, 3, 4)
        .reshape(-1, feat_width)
    )
    win_count = windows.shape[0] // span
    qkv_all = jnp.dot(windows, w_qkv, preferred_element_type=jnp.float32).astype(jnp.bfloat16)
    qkv_all = lax.optimization_barrier(qkv_all)
    qkv_all = qkv_all.reshape(win_count, span, 3, head_count, head_size)
    queries = unit_heads(qkv_all[:, :, 0].astype(jnp.float32))
    keys_unit = unit_heads(qkv_all[:, :, 1].astype(jnp.float32))
    scores = jnp.einsum("wihd,wjhd->whij", queries, keys_unit, precision=lax.Precision.HIGHEST)
    scores = scores * attn_scale[None, :, None, None] + bias_full[None]
    expo = jnp.exp(scores)
    probs = (expo / jnp.sum(expo, -1, keepdims=True)).astype(jnp.bfloat16)
    mixed = jnp.einsum(
        "whij,wjhd->wihd", probs, qkv_all[:, :, 2], preferred_element_type=jnp.float32
    )
    mixed = mixed.astype(jnp.bfloat16).reshape(-1, feat_width)
    attn_out = jnp.dot(mixed, w_proj, preferred_element_type=jnp.float32)
    hidden_one = (windows.astype(jnp.float32) + layer_norm(attn_out) * gain_attn).astype(
        jnp.bfloat16
    )
    hidden_one = lax.optimization_barrier(hidden_one)
    inner = jax.nn.gelu(
        jnp.dot(hidden_one, w_fc1, preferred_element_type=jnp.float32), approximate=True
    ).astype(jnp.bfloat16)
    mlp_out = jnp.dot(inner, w_fc2, preferred_element_type=jnp.float32)
    result = (hidden_one.astype(jnp.float32) + layer_norm(mlp_out) * gain_mlp).astype(jnp.bfloat16)
    result = result.reshape(tok_rows // WIN, tok_cols // WIN, WIN, WIN, feat_width).transpose(
        0, 2, 1, 3, 4
    )
    return result.reshape(tok_rows, tok_cols, feat_width)


def readout_mix(query, key_vals, flags, read_scale):
    floe_rows, feat_width = query.shape
    head_count = read_scale.shape[0]
    head_size = feat_width // head_count
    query_unit = unit_heads(query.astype(jnp.float32).reshape(floe_rows, head_count, head_size))
    key_unit = unit_heads(
        key_vals[:, :, :feat_width].astype(jnp.float32).reshape(floe_rows, 4, head_count, head_size)
    )
    values = (
        key_vals[:, :, feat_width:].astype(jnp.float32).reshape(floe_rows, 4, head_count, head_size)
    )
    scores = jnp.sum(query_unit[:, None] * key_unit, -1) * read_scale
    expo = jnp.exp(scores) * flags[:, :, None]
    weights = expo / jnp.sum(expo, 1, keepdims=True)
    return (
        jnp.sum(weights[..., None] * values, 1).reshape(floe_rows, feat_width).astype(jnp.bfloat16)
    )


def pull_rows(pieces, offset):
    return shifted(pieces, "gx", offset)


def pull_cols(pieces, offset):
    return shifted(pieces, "gy", offset)


def pull_diag(pieces, offset):
    row_devs = lax.axis_size("gx")
    col_devs = lax.axis_size("gy")
    route = [
        (((i - offset) % row_devs) * col_devs + (j - offset) % col_devs, i * col_devs + j)
        for i in range(row_devs)
        for j in range(col_devs)
    ]
    return lax.ppermute(pieces, ("gx", "gy"), route)


def roll_ahead(field):
    own = field[SHIFT:, SHIFT:]
    right = pull_cols(field[SHIFT:, :SHIFT], -1)
    below = pull_rows(field[:SHIFT, SHIFT:], -1)
    corner = pull_diag(field[:SHIFT, :SHIFT], -1)
    return jnp.concatenate(
        [jnp.concatenate([own, right], 1), jnp.concatenate([below, corner], 1)], 0
    )


def roll_behind(field, extra):
    tok_rows, tok_cols = field.shape[:2]
    keep_rows = tok_rows - SHIFT + extra
    keep_cols = tok_cols - SHIFT + extra
    corner = pull_diag(field[tok_rows - SHIFT :, tok_cols - SHIFT :], 1)
    above = pull_rows(field[tok_rows - SHIFT :, :keep_cols], 1)
    left = pull_cols(field[:keep_rows, tok_cols - SHIFT :], 1)
    own = field[:keep_rows, :keep_cols]
    return jnp.concatenate(
        [jnp.concatenate([corner, above], 1), jnp.concatenate([left, own], 1)], 0
    )


def one_hot(index, size, dtype=jnp.bfloat16):
    return (index[..., None] == jnp.arange(size, dtype=jnp.int32)).astype(dtype)


def exact_dot(a, b):
    return jnp.dot(a, b, precision=lax.Precision.HIGHEST, preferred_element_type=jnp.float32)


def pick_dot(a, b):
    return jnp.dot(a, b, preferred_element_type=jnp.float32)


def bias_matrix(bias_table, window):
    span = window * window
    flat = jnp.arange(span * span, dtype=jnp.int32)
    query_at = flat // span
    key_at = flat % span
    row_step = query_at // window - key_at // window + window - 1
    col_step = query_at % window - key_at % window + window - 1
    table_at = row_step * (2 * window - 1) + col_step
    picks = one_hot(table_at, bias_table.shape[1], jnp.float32)
    return exact_dot(bias_table, picks.T).reshape(bias_table.shape[0], span, span)


def head_sum(values, head_mat):
    high = values.astype(jnp.bfloat16)
    low = (values - high.astype(jnp.float32)).astype(jnp.bfloat16)
    picks = head_mat.astype(jnp.bfloat16)
    return pick_dot(high, picks) + pick_dot(low, picks)


def unit_rows(values, head_mat):
    norms = jnp.maximum(jnp.sqrt(head_sum(values * values, head_mat)), 1.0)
    return values / head_sum(norms, head_mat.T)


def local(
    wave_tokens,
    grad_out,
    w_qkv,
    w_proj,
    w_fc1,
    w_fc2,
    gain_attn,
    gain_mlp,
    attn_scale,
    bias_table,
    r_wq,
    r_wkv,
    r_wo,
    read_scale,
    floe_feat,
    floe_count,
    floe_patch,
    floe_cover,
):
    tok_rows, tok_cols, feat_width = wave_tokens.shape
    head_count = read_scale.shape[0]
    head_size = feat_width // head_count
    bias_full = bias_matrix(bias_table, WIN)

    def local_block(field):
        return swin_block(
            field, w_qkv, w_proj, w_fc1, w_fc2, gain_attn, gain_mlp, attn_scale, bias_full
        )

    both = roll_ahead(jnp.concatenate([wave_tokens, grad_out], -1))
    ahead = both[..., :feat_width]
    cot_ahead = both[..., feat_width:]
    out_ahead, pull_back = jax.vjp(local_block, ahead)
    out_ext = roll_behind(out_ahead, 1)
    patch_out = out_ext[:tok_rows, :tok_cols]
    ext_cols = tok_cols + 1
    ext_cells = (tok_rows + 1) * ext_cols
    key_table = jnp.dot(
        out_ext.reshape(ext_cells, feat_width), r_wkv, preferred_element_type=jnp.float32
    ).astype(jnp.bfloat16)
    row_devs = lax.axis_size("gx")
    col_devs = lax.axis_size("gy")
    dev_total = row_devs * col_devs
    grid_cols = tok_cols * col_devs
    feat = floe_feat[0]
    floe_slots = feat.shape[0]
    slot_size = floe_slots // dev_total
    patch = floe_patch[0]
    cover = floe_cover[0]
    row_pos = patch // grid_cols
    col_pos = patch % grid_cols
    target = row_pos // tok_rows * col_devs + col_pos // tok_cols
    targets = one_hot(target, dev_total)
    lower = (
        jnp.arange(floe_slots, dtype=jnp.int32)[:, None]
        >= jnp.arange(floe_slots, dtype=jnp.int32)[None, :]
    ).astype(jnp.bfloat16)
    running = pick_dot(lower, targets)
    rank = jnp.sum(running * targets.astype(jnp.float32), -1).astype(jnp.int32) - 1
    place = target * slot_size + rank
    scatter = one_hot(place, floe_slots).T
    meta_width = 128
    meta = jnp.stack(
        [row_pos % tok_rows, col_pos % tok_cols, cover[0], cover[1], cover[2]], -1
    ).astype(jnp.bfloat16)
    meta = jnp.pad(meta, ((0, 0), (0, meta_width - meta.shape[1])))
    query = jnp.dot(feat, r_wq, preferred_element_type=jnp.float32).astype(jnp.bfloat16)
    packed = pick_dot(scatter, jnp.concatenate([query, meta], -1)).astype(jnp.bfloat16)
    piece = lax.all_to_all(
        packed.reshape(dev_total, slot_size, feat_width + meta_width),
        ("gx", "gy"),
        split_axis=0,
        concat_axis=0,
        tiled=True,
    ).reshape(floe_slots, feat_width + meta_width)
    got_query = piece[:, :feat_width].astype(jnp.float32)
    got_meta = piece[:, feat_width:].astype(jnp.float32).astype(jnp.int32)
    cell_row = got_meta[:, 0]
    cell_col = got_meta[:, 1]
    ones = jnp.ones_like(cell_row)
    flags = jnp.stack([ones, got_meta[:, 2], got_meta[:, 3], got_meta[:, 4]], 0).astype(
        jnp.float32
    )
    corner_rows = jnp.stack([cell_row, cell_row, cell_row + 1, cell_row + 1], 0)
    corner_cols = jnp.stack([cell_col, cell_col + 1, cell_col, cell_col + 1], 0)
    corner_at = (corner_rows * ext_cols + corner_cols).reshape(-1)
    corner_vals = jnp.dot(
        one_hot(corner_at, ext_cells), key_table, preferred_element_type=jnp.bfloat16
    )
    head_mat = (
        jnp.arange(feat_width, dtype=jnp.int32)[:, None] // head_size
        == jnp.arange(head_count, dtype=jnp.int32)[None, :]
    ).astype(jnp.float32)
    query_unit = unit_rows(got_query, head_mat)
    keys = corner_vals[:, :feat_width].astype(jnp.float32)
    key_norms = jnp.maximum(jnp.sqrt(head_sum(keys * keys, head_mat)), 1.0)
    values = corner_vals[:, feat_width:].astype(jnp.float32).reshape(4, floe_slots, feat_width)
    dots = head_sum(
        (query_unit[None] * keys.reshape(4, floe_slots, feat_width)).reshape(
            4 * floe_slots, feat_width
        ),
        head_mat,
    )
    scores = (dots / key_norms).reshape(4, floe_slots, head_count)
    expo = jnp.exp(scores * read_scale) * flags[:, :, None]
    weights = expo / jnp.sum(expo, 0, keepdims=True)
    spread = head_sum(weights.reshape(4 * floe_slots, head_count), head_mat.T).reshape(
        4, floe_slots, feat_width
    )
    floe_mix = jnp.sum(spread * values, 0).astype(jnp.bfloat16)
    floe_mix, cot_ahead = lax.optimization_barrier((floe_mix, cot_ahead))
    returned = lax.all_to_all(
        floe_mix.reshape(dev_total, slot_size, feat_width),
        ("gx", "gy"),
        split_axis=0,
        concat_axis=0,
        tiled=True,
    ).reshape(floe_slots, feat_width)
    grad_ahead = pull_back(cot_ahead)[0]
    grad_in = roll_behind(grad_ahead, 0)
    floe_mix = pick_dot(scatter.T, returned).astype(jnp.bfloat16)
    updated = feat.astype(jnp.float32) + jnp.dot(floe_mix, r_wo, preferred_element_type=jnp.float32)
    alive = jnp.arange(floe_slots, dtype=jnp.int32) < floe_count[0]
    floe_out = jnp.where(alive[:, None], updated, 0.0).astype(jnp.bfloat16)[None]
    return (patch_out, grad_in, floe_out)


def solution(mesh):
    in_specs = (
        P("gx", "gy", None),
        P("gx", "gy", None),
        P(),
        P(),
        P(),
        P(),
        P(),
        P(),
        P(),
        P(),
        P(),
        P(),
        P(),
        P(),
        P(("gx", "gy"), None, None),
        P(("gx", "gy")),
        P(("gx", "gy"), None),
        P(("gx", "gy"), None, None),
    )
    out_specs = (P("gx", "gy", None), P("gx", "gy", None), P(("gx", "gy"), None, None))
    return jax.shard_map(local, mesh=mesh, in_specs=in_specs, out_specs=out_specs, check_vma=False)
```

```python
import jax
import jax.numpy as jnp
import numpy as np
import functools

from jax import lax
from jax.experimental import pallas as pl
from jax.sharding import PartitionSpec as P

WIN = 8
SHIFT = 4


def shifted(block, axis, distance):
    devices = range(lax.axis_size(axis))
    route = [((i - distance) % len(devices), i) for i in devices]
    return lax.ppermute(block, axis, route)


def layer_norm(values):
    centred = values - jnp.mean(values, -1, keepdims=True)
    return centred / jnp.sqrt(jnp.mean(centred * centred, -1, keepdims=True) + 1e-05)


def unit_heads(values):
    return values / jnp.maximum(jnp.sqrt(jnp.sum(values * values, -1, keepdims=True)), 1.0)


def bias_index(window):
    grid_pos = np.stack(np.meshgrid(np.arange(window), np.arange(window), indexing="ij")).reshape(
        2, -1
    )
    offsets = grid_pos[:, :, None] - grid_pos[:, None, :] + window - 1
    return offsets[0] * (2 * window - 1) + offsets[1]


def swin_block(field, w_qkv, w_proj, w_fc1, w_fc2, gain_attn, gain_mlp, attn_scale, bias_full):
    tok_rows, tok_cols, feat_width = field.shape
    head_count = attn_scale.shape[0]
    head_size = feat_width // head_count
    span = WIN * WIN
    windows = (
        field.reshape(tok_rows // WIN, WIN, tok_cols // WIN, WIN, feat_width)
        .transpose(0, 2, 1, 3, 4)
        .reshape(-1, feat_width)
    )
    win_count = windows.shape[0] // span
    qkv_all = jnp.dot(windows, w_qkv, preferred_element_type=jnp.float32).astype(jnp.bfloat16)
    qkv_all = lax.optimization_barrier(qkv_all)
    qkv_all = qkv_all.reshape(win_count, span, 3, head_count, head_size)
    queries = unit_heads(qkv_all[:, :, 0].astype(jnp.float32))
    keys_unit = unit_heads(qkv_all[:, :, 1].astype(jnp.float32))
    scores = jnp.einsum("wihd,wjhd->whij", queries, keys_unit, precision=lax.Precision.HIGHEST)
    scores = scores * attn_scale[None, :, None, None] + bias_full[None]
    expo = jnp.exp(scores)
    probs = (expo / jnp.sum(expo, -1, keepdims=True)).astype(jnp.bfloat16)
    mixed = jnp.einsum(
        "whij,wjhd->wihd", probs, qkv_all[:, :, 2], preferred_element_type=jnp.float32
    )
    mixed = mixed.astype(jnp.bfloat16).reshape(-1, feat_width)
    attn_out = jnp.dot(mixed, w_proj, preferred_element_type=jnp.float32)
    hidden_one = (windows.astype(jnp.float32) + layer_norm(attn_out) * gain_attn).astype(
        jnp.bfloat16
    )
    hidden_one = lax.optimization_barrier(hidden_one)
    inner = jax.nn.gelu(
        jnp.dot(hidden_one, w_fc1, preferred_element_type=jnp.float32), approximate=True
    ).astype(jnp.bfloat16)
    mlp_out = jnp.dot(inner, w_fc2, preferred_element_type=jnp.float32)
    result = (hidden_one.astype(jnp.float32) + layer_norm(mlp_out) * gain_mlp).astype(jnp.bfloat16)
    result = result.reshape(tok_rows // WIN, tok_cols // WIN, WIN, WIN, feat_width).transpose(
        0, 2, 1, 3, 4
    )
    return result.reshape(tok_rows, tok_cols, feat_width)


def readout_mix(query, key_vals, flags, read_scale):
    floe_rows, feat_width = query.shape
    head_count = read_scale.shape[0]
    head_size = feat_width // head_count
    query_unit = unit_heads(query.astype(jnp.float32).reshape(floe_rows, head_count, head_size))
    key_unit = unit_heads(
        key_vals[:, :, :feat_width].astype(jnp.float32).reshape(floe_rows, 4, head_count, head_size)
    )
    values = (
        key_vals[:, :, feat_width:].astype(jnp.float32).reshape(floe_rows, 4, head_count, head_size)
    )
    scores = jnp.sum(query_unit[:, None] * key_unit, -1) * read_scale
    expo = jnp.exp(scores) * flags[:, :, None]
    weights = expo / jnp.sum(expo, 1, keepdims=True)
    return (
        jnp.sum(weights[..., None] * values, 1).reshape(floe_rows, feat_width).astype(jnp.bfloat16)
    )


def pull_rows(pieces, offset):
    return shifted(pieces, "gx", offset)


def pull_cols(pieces, offset):
    return shifted(pieces, "gy", offset)


def pull_diag(pieces, offset):
    row_devs = lax.axis_size("gx")
    col_devs = lax.axis_size("gy")
    route = [
        (((i - offset) % row_devs) * col_devs + (j - offset) % col_devs, i * col_devs + j)
        for i in range(row_devs)
        for j in range(col_devs)
    ]
    return lax.ppermute(pieces, ("gx", "gy"), route)


def roll_ahead(field):
    own = field[SHIFT:, SHIFT:]
    right = pull_cols(field[SHIFT:, :SHIFT], -1)
    below = pull_rows(field[:SHIFT, SHIFT:], -1)
    corner = pull_diag(field[:SHIFT, :SHIFT], -1)
    return jnp.concatenate(
        [jnp.concatenate([own, right], 1), jnp.concatenate([below, corner], 1)], 0
    )


def roll_behind(field, extra):
    tok_rows, tok_cols = field.shape[:2]
    keep_rows = tok_rows - SHIFT + extra
    keep_cols = tok_cols - SHIFT + extra
    corner = pull_diag(field[tok_rows - SHIFT :, tok_cols - SHIFT :], 1)
    above = pull_rows(field[tok_rows - SHIFT :, :keep_cols], 1)
    left = pull_cols(field[:keep_rows, tok_cols - SHIFT :], 1)
    own = field[:keep_rows, :keep_cols]
    return jnp.concatenate(
        [jnp.concatenate([corner, above], 1), jnp.concatenate([left, own], 1)], 0
    )


def one_hot(index, size, dtype=jnp.bfloat16):
    return (index[..., None] == jnp.arange(size, dtype=jnp.int32)).astype(dtype)


def exact_dot(a, b):
    return jnp.dot(a, b, precision=lax.Precision.HIGHEST, preferred_element_type=jnp.float32)


def pick_dot(a, b):
    return jnp.dot(a, b, preferred_element_type=jnp.float32)


def bias_matrix(bias_table, window):
    span = window * window
    flat = jnp.arange(span * span, dtype=jnp.int32)
    query_at = flat // span
    key_at = flat % span
    row_step = query_at // window - key_at // window + window - 1
    col_step = query_at % window - key_at % window + window - 1
    table_at = row_step * (2 * window - 1) + col_step
    picks = one_hot(table_at, bias_table.shape[1], jnp.float32)
    return exact_dot(bias_table, picks.T).reshape(bias_table.shape[0], span, span)


def head_sum(values, head_mat):
    return exact_dot(values, head_mat)


def unit_rows(values, head_mat):
    norms = jnp.maximum(jnp.sqrt(head_sum(values * values, head_mat)), 1.0)
    return values / exact_dot(norms, head_mat.T)


def split_sum(values, picks):
    high = values.astype(jnp.bfloat16)
    low = (values - high.astype(jnp.float32)).astype(jnp.bfloat16)
    return jnp.dot(high, picks, preferred_element_type=jnp.float32) + jnp.dot(
        low, picks, preferred_element_type=jnp.float32
    )


def readout_kernel(ext_cols, piece_ref, table_ref, heads_ref, spread_ref, scale_ref, out_ref):
    rows = piece_ref.shape[0]
    feat_width = out_ref.shape[1]
    heads = heads_ref[...]
    spread = spread_ref[...]

    def unit(values):
        norms = jnp.maximum(jnp.sqrt(split_sum(values * values, heads)), 1.0)
        return values / split_sum(norms, spread)

    piece = piece_ref[...]
    query = unit(piece[:, :feat_width].astype(jnp.float32))
    meta = piece[:, feat_width:].astype(jnp.float32).astype(jnp.int32)
    table = table_ref[...]
    scale = scale_ref[...]
    cells = lax.broadcasted_iota(jnp.int32, (rows, table.shape[0]), 1)
    expos = []
    values = []
    for corner in range(4):
        down = corner // 2
        side = corner % 2
        at = (meta[:, 0:1] + down) * ext_cols + meta[:, 1:2] + side
        picked = jnp.dot(
            (cells == at).astype(jnp.bfloat16), table, preferred_element_type=jnp.float32
        )
        keys = unit(picked[:, :feat_width])
        values.append(picked[:, feat_width:])
        expo = jnp.exp(split_sum(query * keys, heads) * scale)
        if corner > 0:
            expo = expo * meta[:, 1 + corner : 2 + corner].astype(jnp.float32)
        expos.append(expo)
    total = expos[0] + expos[1] + expos[2] + expos[3]
    mix = split_sum(expos[0] / total, spread) * values[0]
    for corner in range(1, 4):
        mix = mix + split_sum(expos[corner] / total, spread) * values[corner]
    out_ref[...] = mix.astype(out_ref.dtype)


def readout_call(piece, table, read_scale, ext_cols, block_rows=128):
    floe_rows, piece_width = piece.shape
    head_count = read_scale.shape[0]
    feat_width = table.shape[1] // 2
    head_size = feat_width // head_count
    table_rows = -(-table.shape[0] // 16) * 16
    table = jnp.pad(table, ((0, table_rows - table.shape[0]), (0, 0)))
    heads = (
        jnp.arange(feat_width, dtype=jnp.int32)[:, None] // head_size
        == jnp.arange(head_count, dtype=jnp.int32)[None, :]
    ).astype(jnp.bfloat16)
    return pl.pallas_call(
        functools.partial(readout_kernel, ext_cols),
        grid=(floe_rows // block_rows,),
        in_specs=[
            pl.BlockSpec((block_rows, piece_width), lambda i: (i, 0)),
            pl.BlockSpec((table_rows, 2 * feat_width), lambda i: (0, 0)),
            pl.BlockSpec((feat_width, head_count), lambda i: (0, 0)),
            pl.BlockSpec((head_count, feat_width), lambda i: (0, 0)),
            pl.BlockSpec((1, head_count), lambda i: (0, 0)),
        ],
        out_specs=pl.BlockSpec((block_rows, feat_width), lambda i: (i, 0)),
        out_shape=jax.ShapeDtypeStruct((floe_rows, feat_width), jnp.bfloat16),
    )(piece, table, heads, heads.T, read_scale.reshape(1, head_count))


def local(
    wave_tokens,
    grad_out,
    w_qkv,
    w_proj,
    w_fc1,
    w_fc2,
    gain_attn,
    gain_mlp,
    attn_scale,
    bias_table,
    r_wq,
    r_wkv,
    r_wo,
    read_scale,
    floe_feat,
    floe_count,
    floe_patch,
    floe_cover,
):
    tok_rows, tok_cols, feat_width = wave_tokens.shape
    head_count = read_scale.shape[0]
    head_size = feat_width // head_count
    bias_full = bias_matrix(bias_table, WIN)

    def local_block(field):
        return swin_block(
            field, w_qkv, w_proj, w_fc1, w_fc2, gain_attn, gain_mlp, attn_scale, bias_full
        )

    both = roll_ahead(jnp.concatenate([wave_tokens, grad_out], -1))
    ahead = both[..., :feat_width]
    cot_ahead = both[..., feat_width:]
    out_ahead, pull_back = jax.vjp(local_block, ahead)
    out_ext = roll_behind(out_ahead, 1)
    patch_out = out_ext[:tok_rows, :tok_cols]
    ext_cols = tok_cols + 1
    ext_cells = (tok_rows + 1) * ext_cols
    key_table = jnp.dot(
        out_ext.reshape(ext_cells, feat_width), r_wkv, preferred_element_type=jnp.float32
    ).astype(jnp.bfloat16)
    row_devs = lax.axis_size("gx")
    col_devs = lax.axis_size("gy")
    dev_total = row_devs * col_devs
    grid_cols = tok_cols * col_devs
    feat = floe_feat[0]
    floe_slots = feat.shape[0]
    slot_size = floe_slots // dev_total
    patch = floe_patch[0]
    cover = floe_cover[0]
    row_pos = patch // grid_cols
    col_pos = patch % grid_cols
    target = row_pos // tok_rows * col_devs + col_pos // tok_cols
    targets = one_hot(target, dev_total)
    lower = (
        jnp.arange(floe_slots, dtype=jnp.int32)[:, None]
        >= jnp.arange(floe_slots, dtype=jnp.int32)[None, :]
    ).astype(jnp.bfloat16)
    running = pick_dot(lower, targets)
    rank = jnp.sum(running * targets.astype(jnp.float32), -1).astype(jnp.int32) - 1
    place = target * slot_size + rank
    scatter = one_hot(place, floe_slots).T
    meta_width = 128
    meta = jnp.stack(
        [row_pos % tok_rows, col_pos % tok_cols, cover[0], cover[1], cover[2]], -1
    ).astype(jnp.bfloat16)
    meta = jnp.pad(meta, ((0, 0), (0, meta_width - meta.shape[1])))
    query = jnp.dot(feat, r_wq, preferred_element_type=jnp.float32).astype(jnp.bfloat16)
    packed = pick_dot(scatter, jnp.concatenate([query, meta], -1)).astype(jnp.bfloat16)
    piece = lax.all_to_all(
        packed.reshape(dev_total, slot_size, feat_width + meta_width),
        ("gx", "gy"),
        split_axis=0,
        concat_axis=0,
        tiled=True,
    ).reshape(floe_slots, feat_width + meta_width)
    floe_mix = readout_call(piece, key_table, read_scale, ext_cols)
    floe_mix, cot_ahead = lax.optimization_barrier((floe_mix, cot_ahead))
    returned = lax.all_to_all(
        floe_mix.reshape(dev_total, slot_size, feat_width),
        ("gx", "gy"),
        split_axis=0,
        concat_axis=0,
        tiled=True,
    ).reshape(floe_slots, feat_width)
    grad_ahead = pull_back(cot_ahead)[0]
    grad_in = roll_behind(grad_ahead, 0)
    floe_mix = pick_dot(scatter.T, returned).astype(jnp.bfloat16)
    updated = feat.astype(jnp.float32) + jnp.dot(floe_mix, r_wo, preferred_element_type=jnp.float32)
    alive = jnp.arange(floe_slots, dtype=jnp.int32) < floe_count[0]
    floe_out = jnp.where(alive[:, None], updated, 0.0).astype(jnp.bfloat16)[None]
    return (patch_out, grad_in, floe_out)


def solution(mesh):
    in_specs = (
        P("gx", "gy", None),
        P("gx", "gy", None),
        P(),
        P(),
        P(),
        P(),
        P(),
        P(),
        P(),
        P(),
        P(),
        P(),
        P(),
        P(),
        P(("gx", "gy"), None, None),
        P(("gx", "gy")),
        P(("gx", "gy"), None),
        P(("gx", "gy"), None, None),
    )
    out_specs = (P("gx", "gy", None), P("gx", "gy", None), P(("gx", "gy"), None, None))
    return jax.shard_map(local, mesh=mesh, in_specs=in_specs, out_specs=out_specs, check_vma=False)
```

```python
import jax
import jax.numpy as jnp
import numpy as np
import functools

from jax import lax
from jax.experimental import pallas as pl
from jax.experimental.pallas import tpu as pltpu
from jax.sharding import PartitionSpec as P

WIN = 8
SHIFT = 4


def shifted(block, axis, distance):
    devices = range(lax.axis_size(axis))
    route = [((i - distance) % len(devices), i) for i in devices]
    return lax.ppermute(block, axis, route)


def layer_norm(values):
    centred = values - jnp.mean(values, -1, keepdims=True)
    return centred / jnp.sqrt(jnp.mean(centred * centred, -1, keepdims=True) + 1e-05)


def unit_heads(values):
    return values / jnp.maximum(jnp.sqrt(jnp.sum(values * values, -1, keepdims=True)), 1.0)


def bias_index(window):
    grid_pos = np.stack(np.meshgrid(np.arange(window), np.arange(window), indexing="ij")).reshape(
        2, -1
    )
    offsets = grid_pos[:, :, None] - grid_pos[:, None, :] + window - 1
    return offsets[0] * (2 * window - 1) + offsets[1]


def swin_block(field, w_qkv, w_proj, w_fc1, w_fc2, gain_attn, gain_mlp, attn_scale, bias_full):
    tok_rows, tok_cols, feat_width = field.shape
    head_count = attn_scale.shape[0]
    head_size = feat_width // head_count
    span = WIN * WIN
    windows = (
        field.reshape(tok_rows // WIN, WIN, tok_cols // WIN, WIN, feat_width)
        .transpose(0, 2, 1, 3, 4)
        .reshape(-1, feat_width)
    )
    win_count = windows.shape[0] // span
    qkv_all = jnp.dot(windows, w_qkv, preferred_element_type=jnp.float32).astype(jnp.bfloat16)
    qkv_all = lax.optimization_barrier(qkv_all)
    qkv_all = qkv_all.reshape(win_count, span, 3, head_count, head_size)
    queries = unit_heads(qkv_all[:, :, 0].astype(jnp.float32))
    keys_unit = unit_heads(qkv_all[:, :, 1].astype(jnp.float32))
    scores = jnp.einsum("wihd,wjhd->whij", queries, keys_unit, precision=lax.Precision.HIGHEST)
    scores = scores * attn_scale[None, :, None, None] + bias_full[None]
    expo = jnp.exp(scores)
    probs = (expo / jnp.sum(expo, -1, keepdims=True)).astype(jnp.bfloat16)
    mixed = jnp.einsum(
        "whij,wjhd->wihd", probs, qkv_all[:, :, 2], preferred_element_type=jnp.float32
    )
    mixed = mixed.astype(jnp.bfloat16).reshape(-1, feat_width)
    attn_out = jnp.dot(mixed, w_proj, preferred_element_type=jnp.float32)
    hidden_one = (windows.astype(jnp.float32) + layer_norm(attn_out) * gain_attn).astype(
        jnp.bfloat16
    )
    hidden_one = lax.optimization_barrier(hidden_one)
    inner = jax.nn.gelu(
        jnp.dot(hidden_one, w_fc1, preferred_element_type=jnp.float32), approximate=True
    ).astype(jnp.bfloat16)
    mlp_out = jnp.dot(inner, w_fc2, preferred_element_type=jnp.float32)
    result = (hidden_one.astype(jnp.float32) + layer_norm(mlp_out) * gain_mlp).astype(jnp.bfloat16)
    result = result.reshape(tok_rows // WIN, tok_cols // WIN, WIN, WIN, feat_width).transpose(
        0, 2, 1, 3, 4
    )
    return result.reshape(tok_rows, tok_cols, feat_width)


def readout_mix(query, key_vals, flags, read_scale):
    floe_rows, feat_width = query.shape
    head_count = read_scale.shape[0]
    head_size = feat_width // head_count
    query_unit = unit_heads(query.astype(jnp.float32).reshape(floe_rows, head_count, head_size))
    key_unit = unit_heads(
        key_vals[:, :, :feat_width].astype(jnp.float32).reshape(floe_rows, 4, head_count, head_size)
    )
    values = (
        key_vals[:, :, feat_width:].astype(jnp.float32).reshape(floe_rows, 4, head_count, head_size)
    )
    scores = jnp.sum(query_unit[:, None] * key_unit, -1) * read_scale
    expo = jnp.exp(scores) * flags[:, :, None]
    weights = expo / jnp.sum(expo, 1, keepdims=True)
    return (
        jnp.sum(weights[..., None] * values, 1).reshape(floe_rows, feat_width).astype(jnp.bfloat16)
    )


def pull_rows(pieces, offset):
    return shifted(pieces, "gx", offset)


def pull_cols(pieces, offset):
    return shifted(pieces, "gy", offset)


def pull_diag(pieces, offset):
    row_devs = lax.axis_size("gx")
    col_devs = lax.axis_size("gy")
    route = [
        (((i - offset) % row_devs) * col_devs + (j - offset) % col_devs, i * col_devs + j)
        for i in range(row_devs)
        for j in range(col_devs)
    ]
    return lax.ppermute(pieces, ("gx", "gy"), route)


def roll_ahead(field):
    own = field[SHIFT:, SHIFT:]
    right = pull_cols(field[SHIFT:, :SHIFT], -1)
    below = pull_rows(field[:SHIFT, SHIFT:], -1)
    corner = pull_diag(field[:SHIFT, :SHIFT], -1)
    return jnp.concatenate(
        [jnp.concatenate([own, right], 1), jnp.concatenate([below, corner], 1)], 0
    )


def roll_behind(field, extra):
    tok_rows, tok_cols = field.shape[:2]
    keep_rows = tok_rows - SHIFT + extra
    keep_cols = tok_cols - SHIFT + extra
    corner = pull_diag(field[tok_rows - SHIFT :, tok_cols - SHIFT :], 1)
    above = pull_rows(field[tok_rows - SHIFT :, :keep_cols], 1)
    left = pull_cols(field[:keep_rows, tok_cols - SHIFT :], 1)
    own = field[:keep_rows, :keep_cols]
    return jnp.concatenate(
        [jnp.concatenate([corner, above], 1), jnp.concatenate([left, own], 1)], 0
    )


def one_hot(index, size, dtype=jnp.bfloat16):
    return (index[..., None] == jnp.arange(size, dtype=jnp.int32)).astype(dtype)


def exact_dot(a, b):
    return jnp.dot(a, b, precision=lax.Precision.HIGHEST, preferred_element_type=jnp.float32)


def pick_dot(a, b):
    return jnp.dot(a, b, preferred_element_type=jnp.float32)


def bias_matrix(bias_table, window):
    span = window * window
    flat = jnp.arange(span * span, dtype=jnp.int32)
    query_at = flat // span
    key_at = flat % span
    row_step = query_at // window - key_at // window + window - 1
    col_step = query_at % window - key_at % window + window - 1
    table_at = row_step * (2 * window - 1) + col_step
    picks = one_hot(table_at, bias_table.shape[1], jnp.float32)
    return exact_dot(bias_table, picks.T).reshape(bias_table.shape[0], span, span)


def head_sum(values, head_mat):
    return exact_dot(values, head_mat)


def unit_rows(values, head_mat):
    norms = jnp.maximum(jnp.sqrt(head_sum(values * values, head_mat)), 1.0)
    return values / exact_dot(norms, head_mat.T)


def split_sum(values, picks):
    high = values.astype(jnp.bfloat16)
    low = (values - high.astype(jnp.float32)).astype(jnp.bfloat16)
    return jnp.dot(high, picks, preferred_element_type=jnp.float32) + jnp.dot(
        low, picks, preferred_element_type=jnp.float32
    )


def readout_kernel(ext_cols, piece_ref, table_ref, heads_ref, spread_ref, scale_ref, out_ref, aug_ref):
    rows = piece_ref.shape[0]
    feat_width = out_ref.shape[1]
    head_count = heads_ref.shape[1]
    kv_width = table_ref.shape[1]
    lane = 128
    heads = heads_ref[...]
    spread = spread_ref[...]

    @pl.when(pl.program_id(0) == 0)
    def _():
        table = table_ref[...]
        keys = table[:, :feat_width].astype(jnp.float32)
        norms = jnp.maximum(jnp.sqrt(split_sum(keys * keys, heads)), 1.0)
        place = (
            lax.broadcasted_iota(jnp.int32, (head_count, lane), 0)
            == lax.broadcasted_iota(jnp.int32, (head_count, lane), 1)
        ).astype(jnp.bfloat16)
        aug_ref[:, :kv_width] = table
        rest = norms
        for part in range(3):
            piece_part = rest.astype(jnp.bfloat16)
            rest = rest - piece_part.astype(jnp.float32)
            start = kv_width + part * lane
            aug_ref[:, start : start + lane] = jnp.dot(
                piece_part, place, preferred_element_type=jnp.float32
            ).astype(jnp.bfloat16)

    piece = piece_ref[...]
    query = piece[:, :feat_width].astype(jnp.float32)
    query_norms = jnp.maximum(jnp.sqrt(split_sum(query * query, heads)), 1.0)
    query = query / split_sum(query_norms, spread)
    meta = piece[:, feat_width:].astype(jnp.float32).astype(jnp.int32)
    aug = aug_ref[...]
    scale = scale_ref[...]
    cells = lax.broadcasted_iota(jnp.int32, (rows, aug.shape[0]), 1)
    total = jnp.zeros((rows, head_count), jnp.float32)
    mix = jnp.zeros((rows, feat_width), jnp.float32)
    for corner in range(4):
        down = corner // 2
        side = corner % 2
        at = (meta[:, 0:1] + down) * ext_cols + meta[:, 1:2] + side
        picked = jnp.dot(
            (cells == at).astype(jnp.bfloat16), aug, preferred_element_type=jnp.float32
        )
        key_norms = (
            picked[:, kv_width : kv_width + head_count]
            + picked[:, kv_width + lane : kv_width + lane + head_count]
        ) + picked[:, kv_width + 2 * lane : kv_width + 2 * lane + head_count]
        scores = split_sum(query * picked[:, :feat_width], heads) / key_norms
        expo = jnp.exp(scores * scale)
        if corner > 0:
            expo = expo * meta[:, 1 + corner : 2 + corner].astype(jnp.float32)
        total = total + expo
        mix = mix + split_sum(expo, spread) * picked[:, feat_width:kv_width]
    out_ref[...] = (mix / split_sum(total, spread)).astype(out_ref.dtype)


def readout_call(piece, table, read_scale, ext_cols, block_rows=256):
    floe_rows, piece_width = piece.shape
    head_count = read_scale.shape[0]
    kv_width = table.shape[1]
    feat_width = kv_width // 2
    head_size = feat_width // head_count
    table_rows = -(-table.shape[0] // 16) * 16
    table = jnp.pad(table, ((0, table_rows - table.shape[0]), (0, 0)))
    heads = (
        jnp.arange(feat_width, dtype=jnp.int32)[:, None] // head_size
        == jnp.arange(head_count, dtype=jnp.int32)[None, :]
    ).astype(jnp.bfloat16)
    return pl.pallas_call(
        functools.partial(readout_kernel, ext_cols),
        grid=(floe_rows // block_rows,),
        in_specs=[
            pl.BlockSpec((block_rows, piece_width), lambda i: (i, 0)),
            pl.BlockSpec((table_rows, kv_width), lambda i: (0, 0)),
            pl.BlockSpec((feat_width, head_count), lambda i: (0, 0)),
            pl.BlockSpec((head_count, feat_width), lambda i: (0, 0)),
            pl.BlockSpec((1, head_count), lambda i: (0, 0)),
        ],
        out_specs=pl.BlockSpec((block_rows, feat_width), lambda i: (i, 0)),
        out_shape=jax.ShapeDtypeStruct((floe_rows, feat_width), jnp.bfloat16),
        scratch_shapes=[pltpu.VMEM((table_rows, kv_width + 3 * 128), jnp.bfloat16)],
    )(piece, table, heads, heads.T, read_scale.reshape(1, head_count))


def local(
    wave_tokens,
    grad_out,
    w_qkv,
    w_proj,
    w_fc1,
    w_fc2,
    gain_attn,
    gain_mlp,
    attn_scale,
    bias_table,
    r_wq,
    r_wkv,
    r_wo,
    read_scale,
    floe_feat,
    floe_count,
    floe_patch,
    floe_cover,
):
    tok_rows, tok_cols, feat_width = wave_tokens.shape
    head_count = read_scale.shape[0]
    head_size = feat_width // head_count
    bias_full = bias_matrix(bias_table, WIN)

    def local_block(field):
        return swin_block(
            field, w_qkv, w_proj, w_fc1, w_fc2, gain_attn, gain_mlp, attn_scale, bias_full
        )

    both = roll_ahead(jnp.concatenate([wave_tokens, grad_out], -1))
    ahead = both[..., :feat_width]
    cot_ahead = both[..., feat_width:]
    out_ahead, pull_back = jax.vjp(local_block, ahead)
    out_ext = roll_behind(out_ahead, 1)
    patch_out = out_ext[:tok_rows, :tok_cols]
    ext_cols = tok_cols + 1
    ext_cells = (tok_rows + 1) * ext_cols
    key_table = jnp.dot(
        out_ext.reshape(ext_cells, feat_width), r_wkv, preferred_element_type=jnp.float32
    ).astype(jnp.bfloat16)
    row_devs = lax.axis_size("gx")
    col_devs = lax.axis_size("gy")
    dev_total = row_devs * col_devs
    grid_cols = tok_cols * col_devs
    feat = floe_feat[0]
    floe_slots = feat.shape[0]
    slot_size = floe_slots // dev_total
    patch = floe_patch[0]
    cover = floe_cover[0]
    row_pos = patch // grid_cols
    col_pos = patch % grid_cols
    target = row_pos // tok_rows * col_devs + col_pos // tok_cols
    targets = one_hot(target, dev_total)
    lower = (
        jnp.arange(floe_slots, dtype=jnp.int32)[:, None]
        >= jnp.arange(floe_slots, dtype=jnp.int32)[None, :]
    ).astype(jnp.bfloat16)
    running = pick_dot(lower, targets)
    rank = jnp.sum(running * targets.astype(jnp.float32), -1).astype(jnp.int32) - 1
    place = target * slot_size + rank
    scatter = one_hot(place, floe_slots).T
    meta_width = 128
    meta = jnp.stack(
        [row_pos % tok_rows, col_pos % tok_cols, cover[0], cover[1], cover[2]], -1
    ).astype(jnp.bfloat16)
    meta = jnp.pad(meta, ((0, 0), (0, meta_width - meta.shape[1])))
    query = jnp.dot(feat, r_wq, preferred_element_type=jnp.float32).astype(jnp.bfloat16)
    packed = pick_dot(scatter, jnp.concatenate([query, meta], -1)).astype(jnp.bfloat16)
    piece = lax.all_to_all(
        packed.reshape(dev_total, slot_size, feat_width + meta_width),
        ("gx", "gy"),
        split_axis=0,
        concat_axis=0,
        tiled=True,
    ).reshape(floe_slots, feat_width + meta_width)
    floe_mix = readout_call(piece, key_table, read_scale, ext_cols)
    floe_mix, cot_ahead = lax.optimization_barrier((floe_mix, cot_ahead))
    returned = lax.all_to_all(
        floe_mix.reshape(dev_total, slot_size, feat_width),
        ("gx", "gy"),
        split_axis=0,
        concat_axis=0,
        tiled=True,
    ).reshape(floe_slots, feat_width)
    grad_ahead = pull_back(cot_ahead)[0]
    grad_in = roll_behind(grad_ahead, 0)
    floe_mix = pick_dot(scatter.T, returned).astype(jnp.bfloat16)
    updated = feat.astype(jnp.float32) + jnp.dot(floe_mix, r_wo, preferred_element_type=jnp.float32)
    alive = jnp.arange(floe_slots, dtype=jnp.int32) < floe_count[0]
    floe_out = jnp.where(alive[:, None], updated, 0.0).astype(jnp.bfloat16)[None]
    return (patch_out, grad_in, floe_out)


def solution(mesh):
    in_specs = (
        P("gx", "gy", None),
        P("gx", "gy", None),
        P(),
        P(),
        P(),
        P(),
        P(),
        P(),
        P(),
        P(),
        P(),
        P(),
        P(),
        P(),
        P(("gx", "gy"), None, None),
        P(("gx", "gy")),
        P(("gx", "gy"), None),
        P(("gx", "gy"), None, None),
    )
    out_specs = (P("gx", "gy", None), P("gx", "gy", None), P(("gx", "gy"), None, None))
    return jax.shard_map(local, mesh=mesh, in_specs=in_specs, out_specs=out_specs, check_vma=False)
```

```python
import jax
import jax.numpy as jnp
import numpy as np
import functools

from jax import lax
from jax.experimental import pallas as pl
from jax.experimental.pallas import tpu as pltpu
from jax.sharding import PartitionSpec as P

WIN = 8
SHIFT = 4


def shifted(block, axis, distance):
    devices = range(lax.axis_size(axis))
    route = [((i - distance) % len(devices), i) for i in devices]
    return lax.ppermute(block, axis, route)


def layer_norm(values):
    centred = values - jnp.mean(values, -1, keepdims=True)
    return centred / jnp.sqrt(jnp.mean(centred * centred, -1, keepdims=True) + 1e-05)


def unit_heads(values):
    return values / jnp.maximum(jnp.sqrt(jnp.sum(values * values, -1, keepdims=True)), 1.0)


def bias_index(window):
    grid_pos = np.stack(np.meshgrid(np.arange(window), np.arange(window), indexing="ij")).reshape(
        2, -1
    )
    offsets = grid_pos[:, :, None] - grid_pos[:, None, :] + window - 1
    return offsets[0] * (2 * window - 1) + offsets[1]


def swin_block(field, w_qkv, w_proj, w_fc1, w_fc2, gain_attn, gain_mlp, attn_scale, bias_full):
    tok_rows, tok_cols, feat_width = field.shape
    head_count = attn_scale.shape[0]
    head_size = feat_width // head_count
    span = WIN * WIN
    windows = (
        field.reshape(tok_rows // WIN, WIN, tok_cols // WIN, WIN, feat_width)
        .transpose(0, 2, 1, 3, 4)
        .reshape(-1, feat_width)
    )
    win_count = windows.shape[0] // span
    qkv_all = jnp.dot(windows, w_qkv, preferred_element_type=jnp.float32).astype(jnp.bfloat16)
    qkv_all = lax.optimization_barrier(qkv_all)
    qkv_all = qkv_all.reshape(win_count, span, 3, head_count, head_size)
    queries = unit_heads(qkv_all[:, :, 0].astype(jnp.float32))
    keys_unit = unit_heads(qkv_all[:, :, 1].astype(jnp.float32))
    scores = jnp.einsum("wihd,wjhd->whij", queries, keys_unit, precision=lax.Precision.HIGHEST)
    scores = scores * attn_scale[None, :, None, None] + bias_full[None]
    expo = jnp.exp(scores)
    probs = (expo / jnp.sum(expo, -1, keepdims=True)).astype(jnp.bfloat16)
    mixed = jnp.einsum(
        "whij,wjhd->wihd", probs, qkv_all[:, :, 2], preferred_element_type=jnp.float32
    )
    mixed = mixed.astype(jnp.bfloat16).reshape(-1, feat_width)
    attn_out = jnp.dot(mixed, w_proj, preferred_element_type=jnp.float32)
    hidden_one = (windows.astype(jnp.float32) + layer_norm(attn_out) * gain_attn).astype(
        jnp.bfloat16
    )
    hidden_one = lax.optimization_barrier(hidden_one)
    inner = jax.nn.gelu(
        jnp.dot(hidden_one, w_fc1, preferred_element_type=jnp.float32), approximate=True
    ).astype(jnp.bfloat16)
    mlp_out = jnp.dot(inner, w_fc2, preferred_element_type=jnp.float32)
    result = (hidden_one.astype(jnp.float32) + layer_norm(mlp_out) * gain_mlp).astype(jnp.bfloat16)
    result = result.reshape(tok_rows // WIN, tok_cols // WIN, WIN, WIN, feat_width).transpose(
        0, 2, 1, 3, 4
    )
    return result.reshape(tok_rows, tok_cols, feat_width)


def readout_mix(query, key_vals, flags, read_scale):
    floe_rows, feat_width = query.shape
    head_count = read_scale.shape[0]
    head_size = feat_width // head_count
    query_unit = unit_heads(query.astype(jnp.float32).reshape(floe_rows, head_count, head_size))
    key_unit = unit_heads(
        key_vals[:, :, :feat_width].astype(jnp.float32).reshape(floe_rows, 4, head_count, head_size)
    )
    values = (
        key_vals[:, :, feat_width:].astype(jnp.float32).reshape(floe_rows, 4, head_count, head_size)
    )
    scores = jnp.sum(query_unit[:, None] * key_unit, -1) * read_scale
    expo = jnp.exp(scores) * flags[:, :, None]
    weights = expo / jnp.sum(expo, 1, keepdims=True)
    return (
        jnp.sum(weights[..., None] * values, 1).reshape(floe_rows, feat_width).astype(jnp.bfloat16)
    )


def pull_rows(pieces, offset):
    return shifted(pieces, "gx", offset)


def pull_cols(pieces, offset):
    return shifted(pieces, "gy", offset)


def pull_diag(pieces, offset):
    row_devs = lax.axis_size("gx")
    col_devs = lax.axis_size("gy")
    route = [
        (((i - offset) % row_devs) * col_devs + (j - offset) % col_devs, i * col_devs + j)
        for i in range(row_devs)
        for j in range(col_devs)
    ]
    return lax.ppermute(pieces, ("gx", "gy"), route)


def roll_ahead(field):
    own = field[SHIFT:, SHIFT:]
    right = pull_cols(field[SHIFT:, :SHIFT], -1)
    below = pull_rows(field[:SHIFT, SHIFT:], -1)
    corner = pull_diag(field[:SHIFT, :SHIFT], -1)
    return jnp.concatenate(
        [jnp.concatenate([own, right], 1), jnp.concatenate([below, corner], 1)], 0
    )


def roll_behind(field, extra):
    tok_rows, tok_cols = field.shape[:2]
    keep_rows = tok_rows - SHIFT + extra
    keep_cols = tok_cols - SHIFT + extra
    corner = pull_diag(field[tok_rows - SHIFT :, tok_cols - SHIFT :], 1)
    above = pull_rows(field[tok_rows - SHIFT :, :keep_cols], 1)
    left = pull_cols(field[:keep_rows, tok_cols - SHIFT :], 1)
    own = field[:keep_rows, :keep_cols]
    return jnp.concatenate(
        [jnp.concatenate([corner, above], 1), jnp.concatenate([left, own], 1)], 0
    )


def one_hot(index, size, dtype=jnp.bfloat16):
    return (index[..., None] == jnp.arange(size, dtype=jnp.int32)).astype(dtype)


def exact_dot(a, b):
    return jnp.dot(a, b, precision=lax.Precision.HIGHEST, preferred_element_type=jnp.float32)


def pick_dot(a, b):
    return jnp.dot(a, b, preferred_element_type=jnp.float32)


def bias_matrix(bias_table, window):
    span = window * window
    flat = jnp.arange(span * span, dtype=jnp.int32)
    query_at = flat // span
    key_at = flat % span
    row_step = query_at // window - key_at // window + window - 1
    col_step = query_at % window - key_at % window + window - 1
    table_at = row_step * (2 * window - 1) + col_step
    picks = one_hot(table_at, bias_table.shape[1], jnp.float32)
    return exact_dot(bias_table, picks.T).reshape(bias_table.shape[0], span, span)


def head_sum(values, head_mat):
    return exact_dot(values, head_mat)


def unit_rows(values, head_mat):
    norms = jnp.maximum(jnp.sqrt(head_sum(values * values, head_mat)), 1.0)
    return values / exact_dot(norms, head_mat.T)


def split_sum(values, picks):
    high = values.astype(jnp.bfloat16)
    low = (values - high.astype(jnp.float32)).astype(jnp.bfloat16)
    return jnp.dot(high, picks, preferred_element_type=jnp.float32) + jnp.dot(
        low, picks, preferred_element_type=jnp.float32
    )


def readout_kernel(ext_cols, piece_ref, table_ref, heads_ref, spread_ref, scale_ref, out_ref, aug_ref):
    rows = piece_ref.shape[0]
    feat_width = out_ref.shape[1]
    head_count = heads_ref.shape[1]
    kv_width = table_ref.shape[1]
    lane = 128
    heads = heads_ref[...]
    spread = spread_ref[...]

    @pl.when(pl.program_id(0) == 0)
    def _():
        table = table_ref[...]
        keys = table[:, :feat_width].astype(jnp.float32)
        norms = jnp.maximum(jnp.sqrt(split_sum(keys * keys, heads)), 1.0)
        place = (
            lax.broadcasted_iota(jnp.int32, (head_count, lane), 0)
            == lax.broadcasted_iota(jnp.int32, (head_count, lane), 1)
        ).astype(jnp.bfloat16)
        aug_ref[:, :kv_width] = table
        rest = norms
        for part in range(3):
            piece_part = rest.astype(jnp.bfloat16)
            rest = rest - piece_part.astype(jnp.float32)
            start = kv_width + part * lane
            aug_ref[:, start : start + lane] = jnp.dot(
                piece_part, place, preferred_element_type=jnp.float32
            ).astype(jnp.bfloat16)

    piece = piece_ref[...]
    query = piece[:, :feat_width].astype(jnp.float32)
    query_norms = jnp.maximum(jnp.sqrt(split_sum(query * query, heads)), 1.0)
    query = query / split_sum(query_norms, spread)
    meta = piece[:, feat_width:].astype(jnp.float32).astype(jnp.int32)
    aug = aug_ref[...]
    scale = scale_ref[...]
    cells = lax.broadcasted_iota(jnp.int32, (rows, aug.shape[0]), 1)
    total = jnp.zeros((rows, head_count), jnp.float32)
    mix = jnp.zeros((rows, feat_width), jnp.float32)
    for corner in range(4):
        down = corner // 2
        side = corner % 2
        at = (meta[:, 0:1] + down) * ext_cols + meta[:, 1:2] + side
        picked = jnp.dot(
            (cells == at).astype(jnp.bfloat16), aug, preferred_element_type=jnp.float32
        )
        key_norms = (
            picked[:, kv_width : kv_width + head_count]
            + picked[:, kv_width + lane : kv_width + lane + head_count]
        ) + picked[:, kv_width + 2 * lane : kv_width + 2 * lane + head_count]
        scores = split_sum(query * picked[:, :feat_width], heads) / key_norms
        expo = jnp.exp(scores * scale)
        if corner > 0:
            expo = expo * meta[:, 1 + corner : 2 + corner].astype(jnp.float32)
        total = total + expo
        mix = mix + split_sum(expo, spread) * picked[:, feat_width:kv_width]
    out_ref[...] = (mix / split_sum(total, spread)).astype(out_ref.dtype)


def readout_call(piece, table, read_scale, ext_cols, block_rows=256):
    floe_rows, piece_width = piece.shape
    head_count = read_scale.shape[0]
    kv_width = table.shape[1]
    feat_width = kv_width // 2
    head_size = feat_width // head_count
    table_rows = -(-table.shape[0] // 16) * 16
    table = jnp.pad(table, ((0, table_rows - table.shape[0]), (0, 0)))
    heads = (
        jnp.arange(feat_width, dtype=jnp.int32)[:, None] // head_size
        == jnp.arange(head_count, dtype=jnp.int32)[None, :]
    ).astype(jnp.bfloat16)
    return pl.pallas_call(
        functools.partial(readout_kernel, ext_cols),
        grid=(floe_rows // block_rows,),
        in_specs=[
            pl.BlockSpec((block_rows, piece_width), lambda i: (i, 0)),
            pl.BlockSpec((table_rows, kv_width), lambda i: (0, 0)),
            pl.BlockSpec((feat_width, head_count), lambda i: (0, 0)),
            pl.BlockSpec((head_count, feat_width), lambda i: (0, 0)),
            pl.BlockSpec((1, head_count), lambda i: (0, 0)),
        ],
        out_specs=pl.BlockSpec((block_rows, feat_width), lambda i: (i, 0)),
        out_shape=jax.ShapeDtypeStruct((floe_rows, feat_width), jnp.bfloat16),
        scratch_shapes=[pltpu.VMEM((table_rows, kv_width + 3 * 128), jnp.bfloat16)],
    )(piece, table, heads, heads.T, read_scale.reshape(1, head_count))


def local(
    wave_tokens,
    grad_out,
    w_qkv,
    w_proj,
    w_fc1,
    w_fc2,
    gain_attn,
    gain_mlp,
    attn_scale,
    bias_table,
    r_wq,
    r_wkv,
    r_wo,
    read_scale,
    floe_feat,
    floe_count,
    floe_patch,
    floe_cover,
):
    tok_rows, tok_cols, feat_width = wave_tokens.shape
    head_count = read_scale.shape[0]
    head_size = feat_width // head_count
    bias_full = bias_matrix(bias_table, WIN)

    def local_block(field):
        return swin_block(
            field, w_qkv, w_proj, w_fc1, w_fc2, gain_attn, gain_mlp, attn_scale, bias_full
        )

    both = roll_ahead(jnp.concatenate([wave_tokens, grad_out], -1))
    ahead = both[..., :feat_width]
    cot_ahead = both[..., feat_width:]
    out_ahead, pull_back = jax.vjp(local_block, ahead)
    out_ext = roll_behind(out_ahead, 1)
    patch_out = out_ext[:tok_rows, :tok_cols]
    ext_cols = tok_cols + 1
    ext_cells = (tok_rows + 1) * ext_cols
    key_table = jnp.dot(
        out_ext.reshape(ext_cells, feat_width), r_wkv, preferred_element_type=jnp.float32
    ).astype(jnp.bfloat16)
    row_devs = lax.axis_size("gx")
    col_devs = lax.axis_size("gy")
    dev_total = row_devs * col_devs
    grid_cols = tok_cols * col_devs
    feat = floe_feat[0]
    floe_slots = feat.shape[0]
    slot_size = floe_slots // dev_total
    patch = floe_patch[0]
    cover = floe_cover[0]
    row_pos = patch // grid_cols
    col_pos = patch % grid_cols
    target = row_pos // tok_rows * col_devs + col_pos // tok_cols
    targets = one_hot(target, dev_total)
    lower = (
        jnp.arange(floe_slots, dtype=jnp.int32)[:, None]
        >= jnp.arange(floe_slots, dtype=jnp.int32)[None, :]
    ).astype(jnp.bfloat16)
    running = pick_dot(lower, targets)
    rank = jnp.sum(running * targets.astype(jnp.float32), -1).astype(jnp.int32) - 1
    place = target * slot_size + rank
    scatter = one_hot(place, floe_slots).T
    meta_width = 128
    meta = jnp.stack(
        [row_pos % tok_rows, col_pos % tok_cols, cover[0], cover[1], cover[2]], -1
    ).astype(jnp.bfloat16)
    meta = jnp.pad(meta, ((0, 0), (0, meta_width - meta.shape[1])))
    query = jnp.dot(feat, r_wq, preferred_element_type=jnp.float32).astype(jnp.bfloat16)
    scatter = scatter.reshape(dev_total, slot_size, floe_slots)
    packed = jnp.einsum(
        "tsf,fc->tsc",
        scatter,
        jnp.concatenate([query, meta], -1),
        preferred_element_type=jnp.float32,
    ).astype(jnp.bfloat16)
    piece = lax.all_to_all(
        packed,
        ("gx", "gy"),
        split_axis=0,
        concat_axis=0,
        tiled=True,
    ).reshape(floe_slots, feat_width + meta_width)
    floe_mix = readout_call(piece, key_table, read_scale, ext_cols)
    floe_mix, cot_ahead = lax.optimization_barrier((floe_mix, cot_ahead))
    returned = lax.all_to_all(
        floe_mix.reshape(dev_total, slot_size, feat_width),
        ("gx", "gy"),
        split_axis=0,
        concat_axis=0,
        tiled=True,
    )
    grad_ahead = pull_back(cot_ahead)[0]
    grad_in = roll_behind(grad_ahead, 0)
    floe_mix = jnp.einsum(
        "tsf,tsc->fc", scatter, returned, preferred_element_type=jnp.float32
    ).astype(jnp.bfloat16)
    updated = feat.astype(jnp.float32) + jnp.dot(floe_mix, r_wo, preferred_element_type=jnp.float32)
    alive = jnp.arange(floe_slots, dtype=jnp.int32) < floe_count[0]
    floe_out = jnp.where(alive[:, None], updated, 0.0).astype(jnp.bfloat16)[None]
    return (patch_out, grad_in, floe_out)


def solution(mesh):
    in_specs = (
        P("gx", "gy", None),
        P("gx", "gy", None),
        P(),
        P(),
        P(),
        P(),
        P(),
        P(),
        P(),
        P(),
        P(),
        P(),
        P(),
        P(),
        P(("gx", "gy"), None, None),
        P(("gx", "gy")),
        P(("gx", "gy"), None),
        P(("gx", "gy"), None, None),
    )
    out_specs = (P("gx", "gy", None), P("gx", "gy", None), P(("gx", "gy"), None, None))
    return jax.shard_map(local, mesh=mesh, in_specs=in_specs, out_specs=out_specs, check_vma=False)
```

```python
import jax
import jax.numpy as jnp
import numpy as np
import functools

from jax import lax
from jax.experimental import pallas as pl
from jax.experimental.pallas import tpu as pltpu
from jax.sharding import PartitionSpec as P

WIN = 8
SHIFT = 4


def shifted(block, axis, distance):
    devices = range(lax.axis_size(axis))
    route = [((i - distance) % len(devices), i) for i in devices]
    return lax.ppermute(block, axis, route)


def layer_norm(values):
    centred = values - jnp.mean(values, -1, keepdims=True)
    return centred / jnp.sqrt(jnp.mean(centred * centred, -1, keepdims=True) + 1e-05)


def unit_heads(values):
    return values / jnp.maximum(jnp.sqrt(jnp.sum(values * values, -1, keepdims=True)), 1.0)


def bias_index(window):
    grid_pos = np.stack(np.meshgrid(np.arange(window), np.arange(window), indexing="ij")).reshape(
        2, -1
    )
    offsets = grid_pos[:, :, None] - grid_pos[:, None, :] + window - 1
    return offsets[0] * (2 * window - 1) + offsets[1]


def swin_block(field, w_qkv, w_proj, w_fc1, w_fc2, gain_attn, gain_mlp, attn_scale, bias_full):
    tok_rows, tok_cols, feat_width = field.shape
    head_count = attn_scale.shape[0]
    head_size = feat_width // head_count
    span = WIN * WIN
    windows = (
        field.reshape(tok_rows // WIN, WIN, tok_cols // WIN, WIN, feat_width)
        .transpose(0, 2, 1, 3, 4)
        .reshape(-1, feat_width)
    )
    win_count = windows.shape[0] // span
    qkv_all = jnp.dot(windows, w_qkv, preferred_element_type=jnp.float32).astype(jnp.bfloat16)
    qkv_all = lax.optimization_barrier(qkv_all)
    head_mat = (
        jnp.arange(feat_width, dtype=jnp.int32)[:, None] // head_size
        == jnp.arange(head_count, dtype=jnp.int32)[None, :]
    ).astype(jnp.float32)
    queries = unit_rows(qkv_all[:, :feat_width].astype(jnp.float32), head_mat).reshape(
        win_count, span, head_count, head_size
    )
    keys_unit = unit_rows(
        qkv_all[:, feat_width : 2 * feat_width].astype(jnp.float32), head_mat
    ).reshape(win_count, span, head_count, head_size)
    qkv_all = qkv_all.reshape(win_count, span, 3, head_count, head_size)
    scores = jnp.einsum("wihd,wjhd->whij", queries, keys_unit, precision=lax.Precision.HIGHEST)
    scores = scores * attn_scale[None, :, None, None] + bias_full[None]
    expo = jnp.exp(scores)
    probs = (expo / jnp.sum(expo, -1, keepdims=True)).astype(jnp.bfloat16)
    mixed = jnp.einsum(
        "whij,wjhd->wihd", probs, qkv_all[:, :, 2], preferred_element_type=jnp.float32
    )
    mixed = mixed.astype(jnp.bfloat16).reshape(-1, feat_width)
    attn_out = jnp.dot(mixed, w_proj, preferred_element_type=jnp.float32)
    hidden_one = (windows.astype(jnp.float32) + layer_norm(attn_out) * gain_attn).astype(
        jnp.bfloat16
    )
    hidden_one = lax.optimization_barrier(hidden_one)
    inner = jax.nn.gelu(
        jnp.dot(hidden_one, w_fc1, preferred_element_type=jnp.float32), approximate=True
    ).astype(jnp.bfloat16)
    mlp_out = jnp.dot(inner, w_fc2, preferred_element_type=jnp.float32)
    result = (hidden_one.astype(jnp.float32) + layer_norm(mlp_out) * gain_mlp).astype(jnp.bfloat16)
    result = result.reshape(tok_rows // WIN, tok_cols // WIN, WIN, WIN, feat_width).transpose(
        0, 2, 1, 3, 4
    )
    return result.reshape(tok_rows, tok_cols, feat_width)


def readout_mix(query, key_vals, flags, read_scale):
    floe_rows, feat_width = query.shape
    head_count = read_scale.shape[0]
    head_size = feat_width // head_count
    query_unit = unit_heads(query.astype(jnp.float32).reshape(floe_rows, head_count, head_size))
    key_unit = unit_heads(
        key_vals[:, :, :feat_width].astype(jnp.float32).reshape(floe_rows, 4, head_count, head_size)
    )
    values = (
        key_vals[:, :, feat_width:].astype(jnp.float32).reshape(floe_rows, 4, head_count, head_size)
    )
    scores = jnp.sum(query_unit[:, None] * key_unit, -1) * read_scale
    expo = jnp.exp(scores) * flags[:, :, None]
    weights = expo / jnp.sum(expo, 1, keepdims=True)
    return (
        jnp.sum(weights[..., None] * values, 1).reshape(floe_rows, feat_width).astype(jnp.bfloat16)
    )


def pull_rows(pieces, offset):
    return shifted(pieces, "gx", offset)


def pull_cols(pieces, offset):
    return shifted(pieces, "gy", offset)


def pull_diag(pieces, offset):
    row_devs = lax.axis_size("gx")
    col_devs = lax.axis_size("gy")
    route = [
        (((i - offset) % row_devs) * col_devs + (j - offset) % col_devs, i * col_devs + j)
        for i in range(row_devs)
        for j in range(col_devs)
    ]
    return lax.ppermute(pieces, ("gx", "gy"), route)


def roll_ahead(field):
    own = field[SHIFT:, SHIFT:]
    right = pull_cols(field[SHIFT:, :SHIFT], -1)
    below = pull_rows(field[:SHIFT, SHIFT:], -1)
    corner = pull_diag(field[:SHIFT, :SHIFT], -1)
    return jnp.concatenate(
        [jnp.concatenate([own, right], 1), jnp.concatenate([below, corner], 1)], 0
    )


def roll_behind(field, extra):
    tok_rows, tok_cols = field.shape[:2]
    keep_rows = tok_rows - SHIFT + extra
    keep_cols = tok_cols - SHIFT + extra
    corner = pull_diag(field[tok_rows - SHIFT :, tok_cols - SHIFT :], 1)
    above = pull_rows(field[tok_rows - SHIFT :, :keep_cols], 1)
    left = pull_cols(field[:keep_rows, tok_cols - SHIFT :], 1)
    own = field[:keep_rows, :keep_cols]
    return jnp.concatenate(
        [jnp.concatenate([corner, above], 1), jnp.concatenate([left, own], 1)], 0
    )


def one_hot(index, size, dtype=jnp.bfloat16):
    return (index[..., None] == jnp.arange(size, dtype=jnp.int32)).astype(dtype)


def exact_dot(a, b):
    return jnp.dot(a, b, precision=lax.Precision.HIGHEST, preferred_element_type=jnp.float32)


def pick_dot(a, b):
    return jnp.dot(a, b, preferred_element_type=jnp.float32)


def bias_matrix(bias_table, window):
    span = window * window
    flat = jnp.arange(span * span, dtype=jnp.int32)
    query_at = flat // span
    key_at = flat % span
    row_step = query_at // window - key_at // window + window - 1
    col_step = query_at % window - key_at % window + window - 1
    table_at = row_step * (2 * window - 1) + col_step
    picks = one_hot(table_at, bias_table.shape[1], jnp.float32)
    return exact_dot(bias_table, picks.T).reshape(bias_table.shape[0], span, span)


def head_sum(values, head_mat):
    return exact_dot(values, head_mat)


def unit_rows(values, head_mat):
    norms = jnp.maximum(jnp.sqrt(head_sum(values * values, head_mat)), 1.0)
    return values / exact_dot(norms, head_mat.T)


def split_sum(values, picks):
    high = values.astype(jnp.bfloat16)
    low = (values - high.astype(jnp.float32)).astype(jnp.bfloat16)
    return jnp.dot(high, picks, preferred_element_type=jnp.float32) + jnp.dot(
        low, picks, preferred_element_type=jnp.float32
    )


def readout_kernel(ext_cols, piece_ref, table_ref, heads_ref, spread_ref, scale_ref, out_ref, aug_ref):
    rows = piece_ref.shape[0]
    feat_width = out_ref.shape[1]
    head_count = heads_ref.shape[1]
    kv_width = table_ref.shape[1]
    lane = 128
    heads = heads_ref[...]
    spread = spread_ref[...]

    @pl.when(pl.program_id(0) == 0)
    def _():
        table = table_ref[...]
        keys = table[:, :feat_width].astype(jnp.float32)
        norms = jnp.maximum(jnp.sqrt(split_sum(keys * keys, heads)), 1.0)
        place = (
            lax.broadcasted_iota(jnp.int32, (head_count, lane), 0)
            == lax.broadcasted_iota(jnp.int32, (head_count, lane), 1)
        ).astype(jnp.bfloat16)
        aug_ref[:, :kv_width] = table
        rest = norms
        for part in range(3):
            piece_part = rest.astype(jnp.bfloat16)
            rest = rest - piece_part.astype(jnp.float32)
            start = kv_width + part * lane
            aug_ref[:, start : start + lane] = jnp.dot(
                piece_part, place, preferred_element_type=jnp.float32
            ).astype(jnp.bfloat16)

    piece = piece_ref[...]
    query = piece[:, :feat_width].astype(jnp.float32)
    query_norms = jnp.maximum(jnp.sqrt(split_sum(query * query, heads)), 1.0)
    query = query / split_sum(query_norms, spread)
    meta = piece[:, feat_width:].astype(jnp.float32).astype(jnp.int32)
    aug = aug_ref[...]
    scale = scale_ref[...]
    cells = lax.broadcasted_iota(jnp.int32, (rows, aug.shape[0]), 1)
    total = jnp.zeros((rows, head_count), jnp.float32)
    mix = jnp.zeros((rows, feat_width), jnp.float32)
    for corner in range(4):
        down = corner // 2
        side = corner % 2
        at = (meta[:, 0:1] + down) * ext_cols + meta[:, 1:2] + side
        picked = jnp.dot(
            (cells == at).astype(jnp.bfloat16), aug, preferred_element_type=jnp.float32
        )
        key_norms = (
            picked[:, kv_width : kv_width + head_count]
            + picked[:, kv_width + lane : kv_width + lane + head_count]
        ) + picked[:, kv_width + 2 * lane : kv_width + 2 * lane + head_count]
        scores = split_sum(query * picked[:, :feat_width], heads) / key_norms
        expo = jnp.exp(scores * scale)
        if corner > 0:
            expo = expo * meta[:, 1 + corner : 2 + corner].astype(jnp.float32)
        total = total + expo
        mix = mix + split_sum(expo, spread) * picked[:, feat_width:kv_width]
    out_ref[...] = (mix / split_sum(total, spread)).astype(out_ref.dtype)


def readout_call(piece, table, read_scale, ext_cols, block_rows=256):
    floe_rows, piece_width = piece.shape
    head_count = read_scale.shape[0]
    kv_width = table.shape[1]
    feat_width = kv_width // 2
    head_size = feat_width // head_count
    table_rows = -(-table.shape[0] // 16) * 16
    table = jnp.pad(table, ((0, table_rows - table.shape[0]), (0, 0)))
    heads = (
        jnp.arange(feat_width, dtype=jnp.int32)[:, None] // head_size
        == jnp.arange(head_count, dtype=jnp.int32)[None, :]
    ).astype(jnp.bfloat16)
    return pl.pallas_call(
        functools.partial(readout_kernel, ext_cols),
        grid=(floe_rows // block_rows,),
        in_specs=[
            pl.BlockSpec((block_rows, piece_width), lambda i: (i, 0)),
            pl.BlockSpec((table_rows, kv_width), lambda i: (0, 0)),
            pl.BlockSpec((feat_width, head_count), lambda i: (0, 0)),
            pl.BlockSpec((head_count, feat_width), lambda i: (0, 0)),
            pl.BlockSpec((1, head_count), lambda i: (0, 0)),
        ],
        out_specs=pl.BlockSpec((block_rows, feat_width), lambda i: (i, 0)),
        out_shape=jax.ShapeDtypeStruct((floe_rows, feat_width), jnp.bfloat16),
        scratch_shapes=[pltpu.VMEM((table_rows, kv_width + 3 * 128), jnp.bfloat16)],
    )(piece, table, heads, heads.T, read_scale.reshape(1, head_count))


def local(
    wave_tokens,
    grad_out,
    w_qkv,
    w_proj,
    w_fc1,
    w_fc2,
    gain_attn,
    gain_mlp,
    attn_scale,
    bias_table,
    r_wq,
    r_wkv,
    r_wo,
    read_scale,
    floe_feat,
    floe_count,
    floe_patch,
    floe_cover,
):
    tok_rows, tok_cols, feat_width = wave_tokens.shape
    head_count = read_scale.shape[0]
    head_size = feat_width // head_count
    bias_full = bias_matrix(bias_table, WIN)

    def local_block(field):
        return swin_block(
            field, w_qkv, w_proj, w_fc1, w_fc2, gain_attn, gain_mlp, attn_scale, bias_full
        )

    both = roll_ahead(jnp.concatenate([wave_tokens, grad_out], -1))
    ahead = both[..., :feat_width]
    cot_ahead = both[..., feat_width:]
    out_ahead, pull_back = jax.vjp(local_block, ahead)
    out_ext = roll_behind(out_ahead, 1)
    patch_out = out_ext[:tok_rows, :tok_cols]
    ext_cols = tok_cols + 1
    ext_cells = (tok_rows + 1) * ext_cols
    key_table = jnp.dot(
        out_ext.reshape(ext_cells, feat_width), r_wkv, preferred_element_type=jnp.float32
    ).astype(jnp.bfloat16)
    row_devs = lax.axis_size("gx")
    col_devs = lax.axis_size("gy")
    dev_total = row_devs * col_devs
    grid_cols = tok_cols * col_devs
    feat = floe_feat[0]
    floe_slots = feat.shape[0]
    slot_size = floe_slots // dev_total
    patch = floe_patch[0]
    cover = floe_cover[0]
    row_pos = patch // grid_cols
    col_pos = patch % grid_cols
    target = row_pos // tok_rows * col_devs + col_pos // tok_cols
    targets = one_hot(target, dev_total)
    lower = (
        jnp.arange(floe_slots, dtype=jnp.int32)[:, None]
        >= jnp.arange(floe_slots, dtype=jnp.int32)[None, :]
    ).astype(jnp.bfloat16)
    running = pick_dot(lower, targets)
    rank = jnp.sum(running * targets.astype(jnp.float32), -1).astype(jnp.int32) - 1
    place = target * slot_size + rank
    scatter = one_hot(place, floe_slots).T
    meta_width = 128
    meta = jnp.stack(
        [row_pos % tok_rows, col_pos % tok_cols, cover[0], cover[1], cover[2]], -1
    ).astype(jnp.bfloat16)
    meta = jnp.pad(meta, ((0, 0), (0, meta_width - meta.shape[1])))
    query = jnp.dot(feat, r_wq, preferred_element_type=jnp.float32).astype(jnp.bfloat16)
    scatter = scatter.reshape(dev_total, slot_size, floe_slots)
    packed = jnp.einsum(
        "tsf,fc->tsc",
        scatter,
        jnp.concatenate([query, meta], -1),
        preferred_element_type=jnp.float32,
    ).astype(jnp.bfloat16)
    piece = lax.all_to_all(
        packed,
        ("gx", "gy"),
        split_axis=0,
        concat_axis=0,
        tiled=True,
    ).reshape(floe_slots, feat_width + meta_width)
    floe_mix = readout_call(piece, key_table, read_scale, ext_cols)
    floe_mix, cot_ahead = lax.optimization_barrier((floe_mix, cot_ahead))
    returned = lax.all_to_all(
        floe_mix.reshape(dev_total, slot_size, feat_width),
        ("gx", "gy"),
        split_axis=0,
        concat_axis=0,
        tiled=True,
    )
    grad_ahead = pull_back(cot_ahead)[0]
    grad_in = roll_behind(grad_ahead, 0)
    floe_mix = jnp.einsum(
        "tsf,tsc->fc", scatter, returned, preferred_element_type=jnp.float32
    ).astype(jnp.bfloat16)
    updated = feat.astype(jnp.float32) + jnp.dot(floe_mix, r_wo, preferred_element_type=jnp.float32)
    alive = jnp.arange(floe_slots, dtype=jnp.int32) < floe_count[0]
    floe_out = jnp.where(alive[:, None], updated, 0.0).astype(jnp.bfloat16)[None]
    return (patch_out, grad_in, floe_out)


def solution(mesh):
    in_specs = (
        P("gx", "gy", None),
        P("gx", "gy", None),
        P(),
        P(),
        P(),
        P(),
        P(),
        P(),
        P(),
        P(),
        P(),
        P(),
        P(),
        P(),
        P(("gx", "gy"), None, None),
        P(("gx", "gy")),
        P(("gx", "gy"), None),
        P(("gx", "gy"), None, None),
    )
    out_specs = (P("gx", "gy", None), P("gx", "gy", None), P(("gx", "gy"), None, None))
    return jax.shard_map(local, mesh=mesh, in_specs=in_specs, out_specs=out_specs, check_vma=False)
```

```python
import jax
import jax.numpy as jnp
import numpy as np
import functools

from jax import lax
from jax.experimental import pallas as pl
from jax.experimental.pallas import tpu as pltpu
from jax.sharding import PartitionSpec as P

WIN = 8
SHIFT = 4


def shifted(block, axis, distance):
    devices = range(lax.axis_size(axis))
    route = [((i - distance) % len(devices), i) for i in devices]
    return lax.ppermute(block, axis, route)


def layer_norm(values):
    centred = values - jnp.mean(values, -1, keepdims=True)
    return centred / jnp.sqrt(jnp.mean(centred * centred, -1, keepdims=True) + 1e-05)


def unit_heads(values):
    return values / jnp.maximum(jnp.sqrt(jnp.sum(values * values, -1, keepdims=True)), 1.0)


def bias_index(window):
    grid_pos = np.stack(np.meshgrid(np.arange(window), np.arange(window), indexing="ij")).reshape(
        2, -1
    )
    offsets = grid_pos[:, :, None] - grid_pos[:, None, :] + window - 1
    return offsets[0] * (2 * window - 1) + offsets[1]


def swin_block(field, w_qkv, w_proj, w_fc1, w_fc2, gain_attn, gain_mlp, attn_scale, bias_full):
    tok_rows, tok_cols, feat_width = field.shape
    head_count = attn_scale.shape[0]
    head_size = feat_width // head_count
    span = WIN * WIN
    windows = (
        field.reshape(tok_rows // WIN, WIN, tok_cols // WIN, WIN, feat_width)
        .transpose(0, 2, 1, 3, 4)
        .reshape(-1, feat_width)
    )
    win_count = windows.shape[0] // span
    qkv_all = jnp.dot(windows, w_qkv, preferred_element_type=jnp.float32).astype(jnp.bfloat16)
    qkv_all = lax.optimization_barrier(qkv_all)
    qkv_all = qkv_all.reshape(win_count, span, 3, head_count, head_size)
    queries = unit_heads(qkv_all[:, :, 0].astype(jnp.float32))
    keys_unit = unit_heads(qkv_all[:, :, 1].astype(jnp.float32))
    scores = jnp.einsum("wihd,wjhd->whij", queries, keys_unit, precision=lax.Precision.HIGHEST)
    scores = scores * attn_scale[None, :, None, None] + bias_full[None]
    expo = jnp.exp(scores)
    probs = (expo / jnp.sum(expo, -1, keepdims=True)).astype(jnp.bfloat16)
    mixed = jnp.einsum(
        "whij,wjhd->wihd", probs, qkv_all[:, :, 2], preferred_element_type=jnp.float32
    )
    mixed = mixed.astype(jnp.bfloat16).reshape(-1, feat_width)
    attn_out = jnp.dot(mixed, w_proj, preferred_element_type=jnp.float32)
    hidden_one = (windows.astype(jnp.float32) + layer_norm(attn_out) * gain_attn).astype(
        jnp.bfloat16
    )
    hidden_one = lax.optimization_barrier(hidden_one)
    inner = jax.nn.gelu(
        jnp.dot(hidden_one, w_fc1, preferred_element_type=jnp.float32), approximate=True
    ).astype(jnp.bfloat16)
    mlp_out = jnp.dot(inner, w_fc2, preferred_element_type=jnp.float32)
    result = (hidden_one.astype(jnp.float32) + layer_norm(mlp_out) * gain_mlp).astype(jnp.bfloat16)
    result = result.reshape(tok_rows // WIN, tok_cols // WIN, WIN, WIN, feat_width).transpose(
        0, 2, 1, 3, 4
    )
    return result.reshape(tok_rows, tok_cols, feat_width)


def readout_mix(query, key_vals, flags, read_scale):
    floe_rows, feat_width = query.shape
    head_count = read_scale.shape[0]
    head_size = feat_width // head_count
    query_unit = unit_heads(query.astype(jnp.float32).reshape(floe_rows, head_count, head_size))
    key_unit = unit_heads(
        key_vals[:, :, :feat_width].astype(jnp.float32).reshape(floe_rows, 4, head_count, head_size)
    )
    values = (
        key_vals[:, :, feat_width:].astype(jnp.float32).reshape(floe_rows, 4, head_count, head_size)
    )
    scores = jnp.sum(query_unit[:, None] * key_unit, -1) * read_scale
    expo = jnp.exp(scores) * flags[:, :, None]
    weights = expo / jnp.sum(expo, 1, keepdims=True)
    return (
        jnp.sum(weights[..., None] * values, 1).reshape(floe_rows, feat_width).astype(jnp.bfloat16)
    )


def pull_rows(pieces, offset):
    return shifted(pieces, "gx", offset)


def pull_cols(pieces, offset):
    return shifted(pieces, "gy", offset)


def pull_diag(pieces, offset):
    row_devs = lax.axis_size("gx")
    col_devs = lax.axis_size("gy")
    route = [
        (((i - offset) % row_devs) * col_devs + (j - offset) % col_devs, i * col_devs + j)
        for i in range(row_devs)
        for j in range(col_devs)
    ]
    return lax.ppermute(pieces, ("gx", "gy"), route)


def roll_ahead(field):
    own = field[SHIFT:, SHIFT:]
    right = pull_cols(field[SHIFT:, :SHIFT], -1)
    below = pull_rows(field[:SHIFT, SHIFT:], -1)
    corner = pull_diag(field[:SHIFT, :SHIFT], -1)
    return jnp.concatenate(
        [jnp.concatenate([own, right], 1), jnp.concatenate([below, corner], 1)], 0
    )


def roll_behind(field, extra):
    tok_rows, tok_cols = field.shape[:2]
    keep_rows = tok_rows - SHIFT + extra
    keep_cols = tok_cols - SHIFT + extra
    corner = pull_diag(field[tok_rows - SHIFT :, tok_cols - SHIFT :], 1)
    above = pull_rows(field[tok_rows - SHIFT :, :keep_cols], 1)
    left = pull_cols(field[:keep_rows, tok_cols - SHIFT :], 1)
    own = field[:keep_rows, :keep_cols]
    return jnp.concatenate(
        [jnp.concatenate([corner, above], 1), jnp.concatenate([left, own], 1)], 0
    )


def one_hot(index, size, dtype=jnp.bfloat16):
    return (index[..., None] == jnp.arange(size, dtype=jnp.int32)).astype(dtype)


def exact_dot(a, b):
    return jnp.dot(a, b, precision=lax.Precision.HIGHEST, preferred_element_type=jnp.float32)


def pick_dot(a, b):
    return jnp.dot(a, b, preferred_element_type=jnp.float32)


def bias_matrix(bias_table, window):
    span = window * window
    flat = jnp.arange(span * span, dtype=jnp.int32)
    query_at = flat // span
    key_at = flat % span
    row_step = query_at // window - key_at // window + window - 1
    col_step = query_at % window - key_at % window + window - 1
    table_at = row_step * (2 * window - 1) + col_step
    picks = one_hot(table_at, bias_table.shape[1], jnp.float32)
    return exact_dot(bias_table, picks.T).reshape(bias_table.shape[0], span, span)


def head_sum(values, head_mat):
    return exact_dot(values, head_mat)


def unit_rows(values, head_mat):
    norms = jnp.maximum(jnp.sqrt(head_sum(values * values, head_mat)), 1.0)
    return values / exact_dot(norms, head_mat.T)


def split_sum(values, picks):
    high = values.astype(jnp.bfloat16)
    low = (values - high.astype(jnp.float32)).astype(jnp.bfloat16)
    return jnp.dot(high, picks, preferred_element_type=jnp.float32) + jnp.dot(
        low, picks, preferred_element_type=jnp.float32
    )


def readout_kernel(ext_cols, piece_ref, table_ref, heads_ref, spread_ref, scale_ref, out_ref, aug_ref):
    rows = piece_ref.shape[0]
    feat_width = out_ref.shape[1]
    head_count = heads_ref.shape[1]
    kv_width = table_ref.shape[1]
    lane = 128
    heads = heads_ref[...]
    spread = spread_ref[...]

    @pl.when(pl.program_id(0) == 0)
    def _():
        table = table_ref[...]
        keys = table[:, :feat_width].astype(jnp.float32)
        norms = jnp.maximum(jnp.sqrt(split_sum(keys * keys, heads)), 1.0)
        place = (
            lax.broadcasted_iota(jnp.int32, (head_count, lane), 0)
            == lax.broadcasted_iota(jnp.int32, (head_count, lane), 1)
        ).astype(jnp.bfloat16)
        aug_ref[:, :kv_width] = table
        rest = norms
        for part in range(3):
            piece_part = rest.astype(jnp.bfloat16)
            rest = rest - piece_part.astype(jnp.float32)
            start = kv_width + part * lane
            aug_ref[:, start : start + lane] = jnp.dot(
                piece_part, place, preferred_element_type=jnp.float32
            ).astype(jnp.bfloat16)

    piece = piece_ref[...]
    query = piece[:, :feat_width].astype(jnp.float32)
    query_norms = jnp.maximum(jnp.sqrt(split_sum(query * query, heads)), 1.0)
    query = query / split_sum(query_norms, spread)
    meta = piece[:, feat_width:].astype(jnp.float32).astype(jnp.int32)
    aug = aug_ref[...]
    scale = scale_ref[...]
    cells = lax.broadcasted_iota(jnp.int32, (rows, aug.shape[0]), 1)
    total = jnp.zeros((rows, head_count), jnp.float32)
    mix = jnp.zeros((rows, feat_width), jnp.float32)
    for corner in range(4):
        down = corner // 2
        side = corner % 2
        at = (meta[:, 0:1] + down) * ext_cols + meta[:, 1:2] + side
        picked = jnp.dot(
            (cells == at).astype(jnp.bfloat16), aug, preferred_element_type=jnp.float32
        )
        key_norms = (
            picked[:, kv_width : kv_width + head_count]
            + picked[:, kv_width + lane : kv_width + lane + head_count]
        ) + picked[:, kv_width + 2 * lane : kv_width + 2 * lane + head_count]
        scores = split_sum(query * picked[:, :feat_width], heads) / key_norms
        expo = jnp.exp(scores * scale)
        if corner > 0:
            expo = expo * meta[:, 1 + corner : 2 + corner].astype(jnp.float32)
        total = total + expo
        mix = mix + split_sum(expo, spread) * picked[:, feat_width:kv_width]
    out_ref[...] = (mix / split_sum(total, spread)).astype(out_ref.dtype)


def readout_call(piece, table, read_scale, ext_cols, block_rows=256):
    floe_rows, piece_width = piece.shape
    head_count = read_scale.shape[0]
    kv_width = table.shape[1]
    feat_width = kv_width // 2
    head_size = feat_width // head_count
    table_rows = -(-table.shape[0] // 16) * 16
    table = jnp.pad(table, ((0, table_rows - table.shape[0]), (0, 0)))
    heads = (
        jnp.arange(feat_width, dtype=jnp.int32)[:, None] // head_size
        == jnp.arange(head_count, dtype=jnp.int32)[None, :]
    ).astype(jnp.bfloat16)
    return pl.pallas_call(
        functools.partial(readout_kernel, ext_cols),
        grid=(floe_rows // block_rows,),
        in_specs=[
            pl.BlockSpec((block_rows, piece_width), lambda i: (i, 0)),
            pl.BlockSpec((table_rows, kv_width), lambda i: (0, 0)),
            pl.BlockSpec((feat_width, head_count), lambda i: (0, 0)),
            pl.BlockSpec((head_count, feat_width), lambda i: (0, 0)),
            pl.BlockSpec((1, head_count), lambda i: (0, 0)),
        ],
        out_specs=pl.BlockSpec((block_rows, feat_width), lambda i: (i, 0)),
        out_shape=jax.ShapeDtypeStruct((floe_rows, feat_width), jnp.bfloat16),
        scratch_shapes=[pltpu.VMEM((table_rows, kv_width + 3 * 128), jnp.bfloat16)],
    )(piece, table, heads, heads.T, read_scale.reshape(1, head_count))


def local(
    wave_tokens,
    grad_out,
    w_qkv,
    w_proj,
    w_fc1,
    w_fc2,
    gain_attn,
    gain_mlp,
    attn_scale,
    bias_table,
    r_wq,
    r_wkv,
    r_wo,
    read_scale,
    floe_feat,
    floe_count,
    floe_patch,
    floe_cover,
):
    tok_rows, tok_cols, feat_width = wave_tokens.shape
    head_count = read_scale.shape[0]
    head_size = feat_width // head_count
    bias_full = bias_matrix(bias_table, WIN)

    def local_block(field):
        return swin_block(
            field, w_qkv, w_proj, w_fc1, w_fc2, gain_attn, gain_mlp, attn_scale, bias_full
        )

    both = roll_ahead(jnp.concatenate([wave_tokens, grad_out], -1))
    ahead = both[..., :feat_width]
    cot_ahead = both[..., feat_width:]
    out_ahead, pull_back = jax.vjp(local_block, ahead)
    out_ext = roll_behind(out_ahead, 1)
    patch_out = out_ext[:tok_rows, :tok_cols]
    ext_cols = tok_cols + 1
    ext_cells = (tok_rows + 1) * ext_cols
    key_table = jnp.dot(
        out_ext.reshape(ext_cells, feat_width), r_wkv, preferred_element_type=jnp.float32
    ).astype(jnp.bfloat16)
    row_devs = lax.axis_size("gx")
    col_devs = lax.axis_size("gy")
    dev_total = row_devs * col_devs
    grid_cols = tok_cols * col_devs
    feat = floe_feat[0]
    floe_slots = feat.shape[0]
    slot_size = floe_slots // dev_total
    patch = floe_patch[0]
    cover = floe_cover[0]
    row_pos = patch // grid_cols
    col_pos = patch % grid_cols
    target = row_pos // tok_rows * col_devs + col_pos // tok_cols
    targets = one_hot(target, dev_total)
    lower = (
        jnp.arange(floe_slots, dtype=jnp.int32)[:, None]
        >= jnp.arange(floe_slots, dtype=jnp.int32)[None, :]
    ).astype(jnp.bfloat16)
    running = pick_dot(lower, targets)
    rank = jnp.sum(running * targets.astype(jnp.float32), -1).astype(jnp.int32) - 1
    place = (target % col_devs * row_devs + target // col_devs) * slot_size + rank
    scatter = one_hot(place, floe_slots).T
    meta_width = 128
    meta = jnp.stack(
        [row_pos % tok_rows, col_pos % tok_cols, cover[0], cover[1], cover[2]], -1
    ).astype(jnp.bfloat16)
    meta = jnp.pad(meta, ((0, 0), (0, meta_width - meta.shape[1])))
    query = jnp.dot(feat, r_wq, preferred_element_type=jnp.float32).astype(jnp.bfloat16)
    scatter = scatter.reshape(col_devs, row_devs * slot_size, floe_slots)
    packed = jnp.einsum(
        "tsf,fc->tsc",
        scatter,
        jnp.concatenate([query, meta], -1),
        preferred_element_type=jnp.float32,
    ).astype(jnp.bfloat16)
    piece = lax.all_to_all(packed, "gy", split_axis=0, concat_axis=0, tiled=True)
    piece = piece.reshape(col_devs, row_devs, slot_size, feat_width + meta_width)
    piece = lax.all_to_all(piece, "gx", split_axis=1, concat_axis=1, tiled=True)
    piece = piece.reshape(floe_slots, feat_width + meta_width)
    floe_mix = readout_call(piece, key_table, read_scale, ext_cols)
    floe_mix, cot_ahead = lax.optimization_barrier((floe_mix, cot_ahead))
    returned = lax.all_to_all(
        floe_mix.reshape(col_devs, row_devs, slot_size, feat_width),
        "gx",
        split_axis=1,
        concat_axis=1,
        tiled=True,
    ).reshape(col_devs, row_devs * slot_size, feat_width)
    returned = lax.all_to_all(returned, "gy", split_axis=0, concat_axis=0, tiled=True)
    grad_ahead = pull_back(cot_ahead)[0]
    grad_in = roll_behind(grad_ahead, 0)
    floe_mix = jnp.einsum(
        "tsf,tsc->fc", scatter, returned, preferred_element_type=jnp.float32
    ).astype(jnp.bfloat16)
    updated = feat.astype(jnp.float32) + jnp.dot(floe_mix, r_wo, preferred_element_type=jnp.float32)
    alive = jnp.arange(floe_slots, dtype=jnp.int32) < floe_count[0]
    floe_out = jnp.where(alive[:, None], updated, 0.0).astype(jnp.bfloat16)[None]
    return (patch_out, grad_in, floe_out)


def solution(mesh):
    in_specs = (
        P("gx", "gy", None),
        P("gx", "gy", None),
        P(),
        P(),
        P(),
        P(),
        P(),
        P(),
        P(),
        P(),
        P(),
        P(),
        P(),
        P(),
        P(("gx", "gy"), None, None),
        P(("gx", "gy")),
        P(("gx", "gy"), None),
        P(("gx", "gy"), None, None),
    )
    out_specs = (P("gx", "gy", None), P("gx", "gy", None), P(("gx", "gy"), None, None))
    return jax.shard_map(local, mesh=mesh, in_specs=in_specs, out_specs=out_specs, check_vma=False)
```

```python
import jax
import jax.numpy as jnp
import numpy as np
import functools

from jax import lax
from jax.experimental import pallas as pl
from jax.experimental.pallas import tpu as pltpu
from jax.sharding import PartitionSpec as P

WIN = 8
SHIFT = 4


def shifted(block, axis, distance):
    devices = range(lax.axis_size(axis))
    route = [((i - distance) % len(devices), i) for i in devices]
    return lax.ppermute(block, axis, route)


def layer_norm(values):
    centred = values - jnp.mean(values, -1, keepdims=True)
    return centred / jnp.sqrt(jnp.mean(centred * centred, -1, keepdims=True) + 1e-05)


def unit_heads(values):
    return values / jnp.maximum(jnp.sqrt(jnp.sum(values * values, -1, keepdims=True)), 1.0)


def bias_index(window):
    grid_pos = np.stack(np.meshgrid(np.arange(window), np.arange(window), indexing="ij")).reshape(
        2, -1
    )
    offsets = grid_pos[:, :, None] - grid_pos[:, None, :] + window - 1
    return offsets[0] * (2 * window - 1) + offsets[1]


def swin_block(field, w_qkv, w_proj, w_fc1, w_fc2, gain_attn, gain_mlp, attn_scale, bias_full):
    tok_rows, tok_cols, feat_width = field.shape
    head_count = attn_scale.shape[0]
    head_size = feat_width // head_count
    span = WIN * WIN
    windows = (
        field.reshape(tok_rows // WIN, WIN, tok_cols // WIN, WIN, feat_width)
        .transpose(0, 2, 1, 3, 4)
        .reshape(-1, feat_width)
    )
    win_count = windows.shape[0] // span
    qkv_all = jnp.dot(windows, w_qkv, preferred_element_type=jnp.float32).astype(jnp.bfloat16)
    qkv_all = lax.optimization_barrier(qkv_all)
    qkv_all = qkv_all.reshape(win_count, span, 3, head_count, head_size)
    queries = unit_heads(qkv_all[:, :, 0].astype(jnp.float32))
    keys_unit = unit_heads(qkv_all[:, :, 1].astype(jnp.float32))
    scores = jnp.einsum("wihd,wjhd->whij", queries, keys_unit, precision=lax.Precision.HIGHEST)
    scores = scores * attn_scale[None, :, None, None] + bias_full[None]
    expo = jnp.exp(scores)
    probs = (expo / jnp.sum(expo, -1, keepdims=True)).astype(jnp.bfloat16)
    mixed = jnp.einsum(
        "whij,wjhd->wihd", probs, qkv_all[:, :, 2], preferred_element_type=jnp.float32
    )
    mixed = mixed.astype(jnp.bfloat16).reshape(-1, feat_width)
    attn_out = jnp.dot(mixed, w_proj, preferred_element_type=jnp.float32)
    hidden_one = (windows.astype(jnp.float32) + layer_norm(attn_out) * gain_attn).astype(
        jnp.bfloat16
    )
    hidden_one = lax.optimization_barrier(hidden_one)
    inner = jax.nn.gelu(
        jnp.dot(hidden_one, w_fc1, preferred_element_type=jnp.float32), approximate=True
    ).astype(jnp.bfloat16)
    mlp_out = jnp.dot(inner, w_fc2, preferred_element_type=jnp.float32)
    result = (hidden_one.astype(jnp.float32) + layer_norm(mlp_out) * gain_mlp).astype(jnp.bfloat16)
    result = result.reshape(tok_rows // WIN, tok_cols // WIN, WIN, WIN, feat_width).transpose(
        0, 2, 1, 3, 4
    )
    return result.reshape(tok_rows, tok_cols, feat_width)


def readout_mix(query, key_vals, flags, read_scale):
    floe_rows, feat_width = query.shape
    head_count = read_scale.shape[0]
    head_size = feat_width // head_count
    query_unit = unit_heads(query.astype(jnp.float32).reshape(floe_rows, head_count, head_size))
    key_unit = unit_heads(
        key_vals[:, :, :feat_width].astype(jnp.float32).reshape(floe_rows, 4, head_count, head_size)
    )
    values = (
        key_vals[:, :, feat_width:].astype(jnp.float32).reshape(floe_rows, 4, head_count, head_size)
    )
    scores = jnp.sum(query_unit[:, None] * key_unit, -1) * read_scale
    expo = jnp.exp(scores) * flags[:, :, None]
    weights = expo / jnp.sum(expo, 1, keepdims=True)
    return (
        jnp.sum(weights[..., None] * values, 1).reshape(floe_rows, feat_width).astype(jnp.bfloat16)
    )


def pull_rows(pieces, offset):
    return shifted(pieces, "gx", offset)


def pull_cols(pieces, offset):
    return shifted(pieces, "gy", offset)


def pull_diag(pieces, offset):
    row_devs = lax.axis_size("gx")
    col_devs = lax.axis_size("gy")
    route = [
        (((i - offset) % row_devs) * col_devs + (j - offset) % col_devs, i * col_devs + j)
        for i in range(row_devs)
        for j in range(col_devs)
    ]
    return lax.ppermute(pieces, ("gx", "gy"), route)


def roll_ahead(field):
    own = field[SHIFT:, SHIFT:]
    right = pull_cols(field[SHIFT:, :SHIFT], -1)
    below = pull_rows(field[:SHIFT, SHIFT:], -1)
    corner = pull_diag(field[:SHIFT, :SHIFT], -1)
    return jnp.concatenate(
        [jnp.concatenate([own, right], 1), jnp.concatenate([below, corner], 1)], 0
    )


def roll_behind(field, extra):
    tok_rows, tok_cols = field.shape[:2]
    keep_rows = tok_rows - SHIFT + extra
    keep_cols = tok_cols - SHIFT + extra
    corner = pull_diag(field[tok_rows - SHIFT :, tok_cols - SHIFT :], 1)
    above = pull_rows(field[tok_rows - SHIFT :, :keep_cols], 1)
    left = pull_cols(field[:keep_rows, tok_cols - SHIFT :], 1)
    own = field[:keep_rows, :keep_cols]
    return jnp.concatenate(
        [jnp.concatenate([corner, above], 1), jnp.concatenate([left, own], 1)], 0
    )


def one_hot(index, size, dtype=jnp.bfloat16):
    return (index[..., None] == jnp.arange(size, dtype=jnp.int32)).astype(dtype)


def exact_dot(a, b):
    return jnp.dot(a, b, precision=lax.Precision.HIGHEST, preferred_element_type=jnp.float32)


def pick_dot(a, b):
    return jnp.dot(a, b, preferred_element_type=jnp.float32)


def bias_matrix(bias_table, window):
    span = window * window
    flat = jnp.arange(span * span, dtype=jnp.int32)
    query_at = flat // span
    key_at = flat % span
    row_step = query_at // window - key_at // window + window - 1
    col_step = query_at % window - key_at % window + window - 1
    table_at = row_step * (2 * window - 1) + col_step
    picks = one_hot(table_at, bias_table.shape[1]).T
    rest = bias_table
    total = None
    for _ in range(3):
        part = rest.astype(jnp.bfloat16)
        rest = rest - part.astype(jnp.float32)
        term = pick_dot(part, picks)
        total = term if total is None else total + term
    return total.reshape(bias_table.shape[0], span, span)


def head_sum(values, head_mat):
    return exact_dot(values, head_mat)


def unit_rows(values, head_mat):
    norms = jnp.maximum(jnp.sqrt(head_sum(values * values, head_mat)), 1.0)
    return values / exact_dot(norms, head_mat.T)


def split_sum(values, picks):
    high = values.astype(jnp.bfloat16)
    low = (values - high.astype(jnp.float32)).astype(jnp.bfloat16)
    return jnp.dot(high, picks, preferred_element_type=jnp.float32) + jnp.dot(
        low, picks, preferred_element_type=jnp.float32
    )


def readout_kernel(ext_cols, piece_ref, table_ref, heads_ref, spread_ref, scale_ref, out_ref, aug_ref):
    rows = piece_ref.shape[0]
    feat_width = out_ref.shape[1]
    head_count = heads_ref.shape[1]
    kv_width = table_ref.shape[1]
    lane = 128
    heads = heads_ref[...]
    spread = spread_ref[...]

    @pl.when(pl.program_id(0) == 0)
    def _():
        table = table_ref[...]
        keys = table[:, :feat_width].astype(jnp.float32)
        norms = jnp.maximum(jnp.sqrt(split_sum(keys * keys, heads)), 1.0)
        place = (
            lax.broadcasted_iota(jnp.int32, (head_count, lane), 0)
            == lax.broadcasted_iota(jnp.int32, (head_count, lane), 1)
        ).astype(jnp.bfloat16)
        aug_ref[:, :kv_width] = table
        rest = norms
        for part in range(3):
            piece_part = rest.astype(jnp.bfloat16)
            rest = rest - piece_part.astype(jnp.float32)
            start = kv_width + part * lane
            aug_ref[:, start : start + lane] = jnp.dot(
                piece_part, place, preferred_element_type=jnp.float32
            ).astype(jnp.bfloat16)

    piece = piece_ref[...]
    query = piece[:, :feat_width].astype(jnp.float32)
    query_norms = jnp.maximum(jnp.sqrt(split_sum(query * query, heads)), 1.0)
    query = query / split_sum(query_norms, spread)
    meta = piece[:, feat_width:].astype(jnp.float32).astype(jnp.int32)
    aug = aug_ref[...]
    scale = scale_ref[...]
    cells = lax.broadcasted_iota(jnp.int32, (rows, aug.shape[0]), 1)
    total = jnp.zeros((rows, head_count), jnp.float32)
    mix = jnp.zeros((rows, feat_width), jnp.float32)
    for corner in range(4):
        down = corner // 2
        side = corner % 2
        at = (meta[:, 0:1] + down) * ext_cols + meta[:, 1:2] + side
        picked = jnp.dot(
            (cells == at).astype(jnp.bfloat16), aug, preferred_element_type=jnp.float32
        )
        key_norms = (
            picked[:, kv_width : kv_width + head_count]
            + picked[:, kv_width + lane : kv_width + lane + head_count]
        ) + picked[:, kv_width + 2 * lane : kv_width + 2 * lane + head_count]
        scores = split_sum(query * picked[:, :feat_width], heads) / key_norms
        expo = jnp.exp(scores * scale)
        if corner > 0:
            expo = expo * meta[:, 1 + corner : 2 + corner].astype(jnp.float32)
        total = total + expo
        mix = mix + split_sum(expo, spread) * picked[:, feat_width:kv_width]
    out_ref[...] = (mix / split_sum(total, spread)).astype(out_ref.dtype)


def readout_call(piece, table, read_scale, ext_cols, block_rows=384):
    floe_rows, piece_width = piece.shape
    head_count = read_scale.shape[0]
    kv_width = table.shape[1]
    feat_width = kv_width // 2
    head_size = feat_width // head_count
    table_rows = -(-table.shape[0] // 16) * 16
    table = jnp.pad(table, ((0, table_rows - table.shape[0]), (0, 0)))
    heads = (
        jnp.arange(feat_width, dtype=jnp.int32)[:, None] // head_size
        == jnp.arange(head_count, dtype=jnp.int32)[None, :]
    ).astype(jnp.bfloat16)
    return pl.pallas_call(
        functools.partial(readout_kernel, ext_cols),
        grid=(floe_rows // block_rows,),
        in_specs=[
            pl.BlockSpec((block_rows, piece_width), lambda i: (i, 0)),
            pl.BlockSpec((table_rows, kv_width), lambda i: (0, 0)),
            pl.BlockSpec((feat_width, head_count), lambda i: (0, 0)),
            pl.BlockSpec((head_count, feat_width), lambda i: (0, 0)),
            pl.BlockSpec((1, head_count), lambda i: (0, 0)),
        ],
        out_specs=pl.BlockSpec((block_rows, feat_width), lambda i: (i, 0)),
        out_shape=jax.ShapeDtypeStruct((floe_rows, feat_width), jnp.bfloat16),
        scratch_shapes=[pltpu.VMEM((table_rows, kv_width + 3 * 128), jnp.bfloat16)],
    )(piece, table, heads, heads.T, read_scale.reshape(1, head_count))


def local(
    wave_tokens,
    grad_out,
    w_qkv,
    w_proj,
    w_fc1,
    w_fc2,
    gain_attn,
    gain_mlp,
    attn_scale,
    bias_table,
    r_wq,
    r_wkv,
    r_wo,
    read_scale,
    floe_feat,
    floe_count,
    floe_patch,
    floe_cover,
):
    tok_rows, tok_cols, feat_width = wave_tokens.shape
    head_count = read_scale.shape[0]
    head_size = feat_width // head_count
    bias_full = bias_matrix(bias_table, WIN)

    def local_block(field):
        return swin_block(
            field, w_qkv, w_proj, w_fc1, w_fc2, gain_attn, gain_mlp, attn_scale, bias_full
        )

    both = roll_ahead(jnp.concatenate([wave_tokens, grad_out], -1))
    ahead = both[..., :feat_width]
    cot_ahead = both[..., feat_width:]
    out_ahead, pull_back = jax.vjp(local_block, ahead)
    out_ext = roll_behind(out_ahead, 1)
    patch_out = out_ext[:tok_rows, :tok_cols]
    ext_cols = tok_cols + 1
    ext_cells = (tok_rows + 1) * ext_cols
    key_table = jnp.dot(
        out_ext.reshape(ext_cells, feat_width), r_wkv, preferred_element_type=jnp.float32
    ).astype(jnp.bfloat16)
    row_devs = lax.axis_size("gx")
    col_devs = lax.axis_size("gy")
    dev_total = row_devs * col_devs
    grid_cols = tok_cols * col_devs
    feat = floe_feat[0]
    floe_slots = feat.shape[0]
    slot_size = floe_slots // dev_total
    patch = floe_patch[0]
    cover = floe_cover[0]
    row_pos = patch // grid_cols
    col_pos = patch % grid_cols
    target = row_pos // tok_rows * col_devs + col_pos // tok_cols
    targets = one_hot(target, dev_total)
    lower = (
        jnp.arange(floe_slots, dtype=jnp.int32)[:, None]
        >= jnp.arange(floe_slots, dtype=jnp.int32)[None, :]
    ).astype(jnp.bfloat16)
    running = pick_dot(lower, targets)
    rank = jnp.sum(running * targets.astype(jnp.float32), -1).astype(jnp.int32) - 1
    place = target * slot_size + rank
    scatter = one_hot(place, floe_slots).T
    meta_width = 128
    meta = jnp.stack(
        [row_pos % tok_rows, col_pos % tok_cols, cover[0], cover[1], cover[2]], -1
    ).astype(jnp.bfloat16)
    meta = jnp.pad(meta, ((0, 0), (0, meta_width - meta.shape[1])))
    query = jnp.dot(feat, r_wq, preferred_element_type=jnp.float32).astype(jnp.bfloat16)
    scatter = scatter.reshape(dev_total, slot_size, floe_slots)
    packed = jnp.einsum(
        "tsf,fc->tsc",
        scatter,
        jnp.concatenate([query, meta], -1),
        preferred_element_type=jnp.float32,
    ).astype(jnp.bfloat16)
    piece = lax.all_to_all(
        packed,
        ("gx", "gy"),
        split_axis=0,
        concat_axis=0,
        tiled=True,
    ).reshape(floe_slots, feat_width + meta_width)
    floe_mix = readout_call(piece, key_table, read_scale, ext_cols)
    floe_mix, cot_ahead = lax.optimization_barrier((floe_mix, cot_ahead))
    returned = lax.all_to_all(
        floe_mix.reshape(dev_total, slot_size, feat_width),
        ("gx", "gy"),
        split_axis=0,
        concat_axis=0,
        tiled=True,
    )
    grad_ahead = pull_back(cot_ahead)[0]
    grad_in = roll_behind(grad_ahead, 0)
    floe_mix = jnp.einsum(
        "tsf,tsc->fc", scatter, returned, preferred_element_type=jnp.float32
    ).astype(jnp.bfloat16)
    updated = feat.astype(jnp.float32) + jnp.dot(floe_mix, r_wo, preferred_element_type=jnp.float32)
    alive = jnp.arange(floe_slots, dtype=jnp.int32) < floe_count[0]
    floe_out = jnp.where(alive[:, None], updated, 0.0).astype(jnp.bfloat16)[None]
    return (patch_out, grad_in, floe_out)


def solution(mesh):
    in_specs = (
        P("gx", "gy", None),
        P("gx", "gy", None),
        P(),
        P(),
        P(),
        P(),
        P(),
        P(),
        P(),
        P(),
        P(),
        P(),
        P(),
        P(),
        P(("gx", "gy"), None, None),
        P(("gx", "gy")),
        P(("gx", "gy"), None),
        P(("gx", "gy"), None, None),
    )
    out_specs = (P("gx", "gy", None), P("gx", "gy", None), P(("gx", "gy"), None, None))
    return jax.shard_map(local, mesh=mesh, in_specs=in_specs, out_specs=out_specs, check_vma=False)
```

```python
import jax
import jax.numpy as jnp
import numpy as np
import functools

from jax import lax
from jax.experimental import pallas as pl
from jax.experimental.pallas import tpu as pltpu
from jax.sharding import PartitionSpec as P

WIN = 8
SHIFT = 4


def shifted(block, axis, distance):
    devices = range(lax.axis_size(axis))
    route = [((i - distance) % len(devices), i) for i in devices]
    return lax.ppermute(block, axis, route)


def layer_norm(values):
    centred = values - jnp.mean(values, -1, keepdims=True)
    return centred / jnp.sqrt(jnp.mean(centred * centred, -1, keepdims=True) + 1e-05)


def unit_heads(values):
    return values / jnp.maximum(jnp.sqrt(jnp.sum(values * values, -1, keepdims=True)), 1.0)


def bias_index(window):
    grid_pos = np.stack(np.meshgrid(np.arange(window), np.arange(window), indexing="ij")).reshape(
        2, -1
    )
    offsets = grid_pos[:, :, None] - grid_pos[:, None, :] + window - 1
    return offsets[0] * (2 * window - 1) + offsets[1]


def swin_block(field, w_qkv, w_proj, w_fc1, w_fc2, gain_attn, gain_mlp, attn_scale, bias_full):
    tok_rows, tok_cols, feat_width = field.shape
    head_count = attn_scale.shape[0]
    head_size = feat_width // head_count
    span = WIN * WIN
    windows = (
        field.reshape(tok_rows // WIN, WIN, tok_cols // WIN, WIN, feat_width)
        .transpose(0, 2, 1, 3, 4)
        .reshape(-1, feat_width)
    )
    win_count = windows.shape[0] // span
    qkv_all = jnp.dot(windows, w_qkv, preferred_element_type=jnp.float32).astype(jnp.bfloat16)
    qkv_all = lax.optimization_barrier(qkv_all)
    qkv_all = qkv_all.reshape(win_count, span, 3, head_count, head_size)
    queries = unit_heads(qkv_all[:, :, 0].astype(jnp.float32))
    keys_unit = unit_heads(qkv_all[:, :, 1].astype(jnp.float32))
    scores = jnp.einsum("wihd,wjhd->whij", queries, keys_unit, precision=lax.Precision.HIGHEST)
    scores = scores * attn_scale[None, :, None, None] + bias_full[None]
    expo = jnp.exp(scores)
    probs = (expo / jnp.sum(expo, -1, keepdims=True)).astype(jnp.bfloat16)
    mixed = jnp.einsum(
        "whij,wjhd->wihd", probs, qkv_all[:, :, 2], preferred_element_type=jnp.float32
    )
    mixed = mixed.astype(jnp.bfloat16).reshape(-1, feat_width)
    attn_out = jnp.dot(mixed, w_proj, preferred_element_type=jnp.float32)
    hidden_one = (windows.astype(jnp.float32) + layer_norm(attn_out) * gain_attn).astype(
        jnp.bfloat16
    )
    hidden_one = lax.optimization_barrier(hidden_one)
    inner = jax.nn.gelu(
        jnp.dot(hidden_one, w_fc1, preferred_element_type=jnp.float32), approximate=True
    ).astype(jnp.bfloat16)
    mlp_out = jnp.dot(inner, w_fc2, preferred_element_type=jnp.float32)
    result = (hidden_one.astype(jnp.float32) + layer_norm(mlp_out) * gain_mlp).astype(jnp.bfloat16)
    result = result.reshape(tok_rows // WIN, tok_cols // WIN, WIN, WIN, feat_width).transpose(
        0, 2, 1, 3, 4
    )
    return result.reshape(tok_rows, tok_cols, feat_width)


def readout_mix(query, key_vals, flags, read_scale):
    floe_rows, feat_width = query.shape
    head_count = read_scale.shape[0]
    head_size = feat_width // head_count
    query_unit = unit_heads(query.astype(jnp.float32).reshape(floe_rows, head_count, head_size))
    key_unit = unit_heads(
        key_vals[:, :, :feat_width].astype(jnp.float32).reshape(floe_rows, 4, head_count, head_size)
    )
    values = (
        key_vals[:, :, feat_width:].astype(jnp.float32).reshape(floe_rows, 4, head_count, head_size)
    )
    scores = jnp.sum(query_unit[:, None] * key_unit, -1) * read_scale
    expo = jnp.exp(scores) * flags[:, :, None]
    weights = expo / jnp.sum(expo, 1, keepdims=True)
    return (
        jnp.sum(weights[..., None] * values, 1).reshape(floe_rows, feat_width).astype(jnp.bfloat16)
    )


def pull_rows(pieces, offset):
    return shifted(pieces, "gx", offset)


def pull_cols(pieces, offset):
    return shifted(pieces, "gy", offset)


def pull_diag(pieces, offset):
    row_devs = lax.axis_size("gx")
    col_devs = lax.axis_size("gy")
    route = [
        (((i - offset) % row_devs) * col_devs + (j - offset) % col_devs, i * col_devs + j)
        for i in range(row_devs)
        for j in range(col_devs)
    ]
    return lax.ppermute(pieces, ("gx", "gy"), route)


def roll_ahead(field):
    own = field[SHIFT:, SHIFT:]
    right = pull_cols(field[SHIFT:, :SHIFT], -1)
    below = pull_rows(field[:SHIFT, SHIFT:], -1)
    corner = pull_diag(field[:SHIFT, :SHIFT], -1)
    return jnp.concatenate(
        [jnp.concatenate([own, right], 1), jnp.concatenate([below, corner], 1)], 0
    )


def roll_behind(field, extra):
    tok_rows, tok_cols = field.shape[:2]
    keep_rows = tok_rows - SHIFT + extra
    keep_cols = tok_cols - SHIFT + extra
    corner = pull_diag(field[tok_rows - SHIFT :, tok_cols - SHIFT :], 1)
    above = pull_rows(field[tok_rows - SHIFT :, :keep_cols], 1)
    left = pull_cols(field[:keep_rows, tok_cols - SHIFT :], 1)
    own = field[:keep_rows, :keep_cols]
    return jnp.concatenate(
        [jnp.concatenate([corner, above], 1), jnp.concatenate([left, own], 1)], 0
    )


def one_hot(index, size, dtype=jnp.bfloat16):
    return (index[..., None] == jnp.arange(size, dtype=jnp.int32)).astype(dtype)


def exact_dot(a, b):
    return jnp.dot(a, b, precision=lax.Precision.HIGHEST, preferred_element_type=jnp.float32)


def pick_dot(a, b):
    return jnp.dot(a, b, preferred_element_type=jnp.float32)


def bias_matrix(bias_table, window):
    span = window * window
    flat = jnp.arange(span * span, dtype=jnp.int32)
    query_at = flat // span
    key_at = flat % span
    row_step = query_at // window - key_at // window + window - 1
    col_step = query_at % window - key_at % window + window - 1
    table_at = row_step * (2 * window - 1) + col_step
    picks = one_hot(table_at, bias_table.shape[1], jnp.float32)
    return exact_dot(bias_table, picks.T).reshape(bias_table.shape[0], span, span)


def head_sum(values, head_mat):
    return exact_dot(values, head_mat)


def unit_rows(values, head_mat):
    norms = jnp.maximum(jnp.sqrt(head_sum(values * values, head_mat)), 1.0)
    return values / exact_dot(norms, head_mat.T)


def split_sum(values, picks):
    high = values.astype(jnp.bfloat16)
    low = (values - high.astype(jnp.float32)).astype(jnp.bfloat16)
    return jnp.dot(high, picks, preferred_element_type=jnp.float32) + jnp.dot(
        low, picks, preferred_element_type=jnp.float32
    )


def readout_kernel(ext_cols, piece_ref, table_ref, heads_ref, spread_ref, scale_ref, out_ref, aug_ref):
    rows = piece_ref.shape[0]
    feat_width = out_ref.shape[1]
    head_count = heads_ref.shape[1]
    kv_width = table_ref.shape[1]
    lane = 128
    heads = heads_ref[...]
    spread = spread_ref[...]

    @pl.when(pl.program_id(0) == 0)
    def _():
        table = table_ref[...]
        keys = table[:, :feat_width].astype(jnp.float32)
        norms = jnp.maximum(jnp.sqrt(split_sum(keys * keys, heads)), 1.0)
        place = (
            lax.broadcasted_iota(jnp.int32, (head_count, lane), 0)
            == lax.broadcasted_iota(jnp.int32, (head_count, lane), 1)
        ).astype(jnp.bfloat16)
        aug_ref[:, :kv_width] = table
        rest = norms
        for part in range(3):
            piece_part = rest.astype(jnp.bfloat16)
            rest = rest - piece_part.astype(jnp.float32)
            start = kv_width + part * lane
            aug_ref[:, start : start + lane] = jnp.dot(
                piece_part, place, preferred_element_type=jnp.float32
            ).astype(jnp.bfloat16)

    piece = piece_ref[...]
    query = piece[:, :feat_width].astype(jnp.float32)
    query_norms = jnp.maximum(jnp.sqrt(split_sum(query * query, heads)), 1.0)
    query = query / split_sum(query_norms, spread)
    meta = piece[:, feat_width:].astype(jnp.float32).astype(jnp.int32)
    aug = aug_ref[...]
    scale = scale_ref[...]
    cells = lax.broadcasted_iota(jnp.int32, (rows, aug.shape[0]), 1)
    total = jnp.zeros((rows, head_count), jnp.float32)
    mix = jnp.zeros((rows, feat_width), jnp.float32)
    for corner in range(4):
        down = corner // 2
        side = corner % 2
        at = (meta[:, 0:1] + down) * ext_cols + meta[:, 1:2] + side
        picked = jnp.dot(
            (cells == at).astype(jnp.bfloat16), aug, preferred_element_type=jnp.float32
        )
        key_norms = (
            picked[:, kv_width : kv_width + head_count]
            + picked[:, kv_width + lane : kv_width + lane + head_count]
        ) + picked[:, kv_width + 2 * lane : kv_width + 2 * lane + head_count]
        scores = split_sum(query * picked[:, :feat_width], heads) / key_norms
        expo = jnp.exp(scores * scale)
        if corner > 0:
            expo = expo * meta[:, 1 + corner : 2 + corner].astype(jnp.float32)
        total = total + expo
        mix = mix + split_sum(expo, spread) * picked[:, feat_width:kv_width]
    out_ref[...] = (mix / split_sum(total, spread)).astype(out_ref.dtype)


def readout_call(piece, table, read_scale, ext_cols, block_rows=256):
    floe_rows, piece_width = piece.shape
    head_count = read_scale.shape[0]
    kv_width = table.shape[1]
    feat_width = kv_width // 2
    head_size = feat_width // head_count
    table_rows = -(-table.shape[0] // 16) * 16
    table = jnp.pad(table, ((0, table_rows - table.shape[0]), (0, 0)))
    heads = (
        jnp.arange(feat_width, dtype=jnp.int32)[:, None] // head_size
        == jnp.arange(head_count, dtype=jnp.int32)[None, :]
    ).astype(jnp.bfloat16)
    return pl.pallas_call(
        functools.partial(readout_kernel, ext_cols),
        grid=(floe_rows // block_rows,),
        in_specs=[
            pl.BlockSpec((block_rows, piece_width), lambda i: (i, 0)),
            pl.BlockSpec((table_rows, kv_width), lambda i: (0, 0)),
            pl.BlockSpec((feat_width, head_count), lambda i: (0, 0)),
            pl.BlockSpec((head_count, feat_width), lambda i: (0, 0)),
            pl.BlockSpec((1, head_count), lambda i: (0, 0)),
        ],
        out_specs=pl.BlockSpec((block_rows, feat_width), lambda i: (i, 0)),
        out_shape=jax.ShapeDtypeStruct((floe_rows, feat_width), jnp.bfloat16),
        scratch_shapes=[pltpu.VMEM((table_rows, kv_width + 3 * 128), jnp.bfloat16)],
    )(piece, table, heads, heads.T, read_scale.reshape(1, head_count))


def local(
    wave_tokens,
    grad_out,
    w_qkv,
    w_proj,
    w_fc1,
    w_fc2,
    gain_attn,
    gain_mlp,
    attn_scale,
    bias_table,
    r_wq,
    r_wkv,
    r_wo,
    read_scale,
    floe_feat,
    floe_count,
    floe_patch,
    floe_cover,
):
    tok_rows, tok_cols, feat_width = wave_tokens.shape
    head_count = read_scale.shape[0]
    head_size = feat_width // head_count
    bias_full = bias_matrix(bias_table, WIN)

    def local_block(field):
        return swin_block(
            field, w_qkv, w_proj, w_fc1, w_fc2, gain_attn, gain_mlp, attn_scale, bias_full
        )

    row_devs = lax.axis_size("gx")
    col_devs = lax.axis_size("gy")
    dev_total = row_devs * col_devs
    grid_cols = tok_cols * col_devs
    feat = floe_feat[0]
    floe_slots = feat.shape[0]
    slot_size = floe_slots // dev_total
    patch = floe_patch[0]
    cover = floe_cover[0]
    row_pos = patch // grid_cols
    col_pos = patch % grid_cols
    target = row_pos // tok_rows * col_devs + col_pos // tok_cols
    targets = one_hot(target, dev_total)
    lower = (
        jnp.arange(floe_slots, dtype=jnp.int32)[:, None]
        >= jnp.arange(floe_slots, dtype=jnp.int32)[None, :]
    ).astype(jnp.bfloat16)
    running = pick_dot(lower, targets)
    rank = jnp.sum(running * targets.astype(jnp.float32), -1).astype(jnp.int32) - 1
    place = target * slot_size + rank
    scatter = one_hot(place, floe_slots).T
    meta_width = 128
    meta = jnp.stack(
        [row_pos % tok_rows, col_pos % tok_cols, cover[0], cover[1], cover[2]], -1
    ).astype(jnp.bfloat16)
    meta = jnp.pad(meta, ((0, 0), (0, meta_width - meta.shape[1])))
    query = jnp.dot(feat, r_wq, preferred_element_type=jnp.float32).astype(jnp.bfloat16)
    scatter = scatter.reshape(dev_total, slot_size, floe_slots)
    packed = jnp.einsum(
        "tsf,fc->tsc",
        scatter,
        jnp.concatenate([query, meta], -1),
        preferred_element_type=jnp.float32,
    ).astype(jnp.bfloat16)
    field_in = jnp.concatenate([wave_tokens, grad_out], -1)
    packed, field_in = lax.optimization_barrier((packed, field_in))
    piece = lax.all_to_all(
        packed,
        ("gx", "gy"),
        split_axis=0,
        concat_axis=0,
        tiled=True,
    ).reshape(floe_slots, feat_width + meta_width)
    both = roll_ahead(field_in)
    ahead = both[..., :feat_width]
    cot_ahead = both[..., feat_width:]
    out_ahead, pull_back = jax.vjp(local_block, ahead)
    out_ext = roll_behind(out_ahead, 1)
    patch_out = out_ext[:tok_rows, :tok_cols]
    ext_cols = tok_cols + 1
    ext_cells = (tok_rows + 1) * ext_cols
    key_table = jnp.dot(
        out_ext.reshape(ext_cells, feat_width), r_wkv, preferred_element_type=jnp.float32
    ).astype(jnp.bfloat16)
    floe_mix = readout_call(piece, key_table, read_scale, ext_cols)
    floe_mix, cot_ahead = lax.optimization_barrier((floe_mix, cot_ahead))
    returned = lax.all_to_all(
        floe_mix.reshape(dev_total, slot_size, feat_width),
        ("gx", "gy"),
        split_axis=0,
        concat_axis=0,
        tiled=True,
    )
    grad_ahead = pull_back(cot_ahead)[0]
    grad_in = roll_behind(grad_ahead, 0)
    floe_mix = jnp.einsum(
        "tsf,tsc->fc", scatter, returned, preferred_element_type=jnp.float32
    ).astype(jnp.bfloat16)
    updated = feat.astype(jnp.float32) + jnp.dot(floe_mix, r_wo, preferred_element_type=jnp.float32)
    alive = jnp.arange(floe_slots, dtype=jnp.int32) < floe_count[0]
    floe_out = jnp.where(alive[:, None], updated, 0.0).astype(jnp.bfloat16)[None]
    return (patch_out, grad_in, floe_out)


def solution(mesh):
    in_specs = (
        P("gx", "gy", None),
        P("gx", "gy", None),
        P(),
        P(),
        P(),
        P(),
        P(),
        P(),
        P(),
        P(),
        P(),
        P(),
        P(),
        P(),
        P(("gx", "gy"), None, None),
        P(("gx", "gy")),
        P(("gx", "gy"), None),
        P(("gx", "gy"), None, None),
    )
    out_specs = (P("gx", "gy", None), P("gx", "gy", None), P(("gx", "gy"), None, None))
    return jax.shard_map(local, mesh=mesh, in_specs=in_specs, out_specs=out_specs, check_vma=False)
```

```python
import jax
import jax.numpy as jnp
import numpy as np
import functools

from jax import lax
from jax.experimental import pallas as pl
from jax.experimental.pallas import tpu as pltpu
from jax.sharding import PartitionSpec as P

WIN = 8
SHIFT = 4


def shifted(block, axis, distance):
    devices = range(lax.axis_size(axis))
    route = [((i - distance) % len(devices), i) for i in devices]
    return lax.ppermute(block, axis, route)


def layer_norm(values):
    centred = values - jnp.mean(values, -1, keepdims=True)
    return centred / jnp.sqrt(jnp.mean(centred * centred, -1, keepdims=True) + 1e-05)


def unit_heads(values):
    return values / jnp.maximum(jnp.sqrt(jnp.sum(values * values, -1, keepdims=True)), 1.0)


def bias_index(window):
    grid_pos = np.stack(np.meshgrid(np.arange(window), np.arange(window), indexing="ij")).reshape(
        2, -1
    )
    offsets = grid_pos[:, :, None] - grid_pos[:, None, :] + window - 1
    return offsets[0] * (2 * window - 1) + offsets[1]


def swin_block(field, w_qkv, w_proj, w_fc1, w_fc2, gain_attn, gain_mlp, attn_scale, bias_full):
    tok_rows, tok_cols, feat_width = field.shape
    head_count = attn_scale.shape[0]
    head_size = feat_width // head_count
    span = WIN * WIN
    windows = (
        field.reshape(tok_rows // WIN, WIN, tok_cols // WIN, WIN, feat_width)
        .transpose(0, 2, 1, 3, 4)
        .reshape(-1, feat_width)
    )
    win_count = windows.shape[0] // span
    qkv_all = jnp.dot(windows, w_qkv, preferred_element_type=jnp.float32).astype(jnp.bfloat16)
    qkv_all = lax.optimization_barrier(qkv_all)
    qkv_all = qkv_all.reshape(win_count, span, 3, head_count, head_size)
    queries = unit_heads(qkv_all[:, :, 0].astype(jnp.float32))
    keys_unit = unit_heads(qkv_all[:, :, 1].astype(jnp.float32))
    scores = jnp.einsum("wihd,wjhd->whij", queries, keys_unit, precision=lax.Precision.HIGHEST)
    scores = scores * attn_scale[None, :, None, None] + bias_full[None]
    expo = jnp.exp(scores)
    probs = (expo / jnp.sum(expo, -1, keepdims=True)).astype(jnp.bfloat16)
    mixed = jnp.einsum(
        "whij,wjhd->wihd", probs, qkv_all[:, :, 2], preferred_element_type=jnp.float32
    )
    mixed = mixed.astype(jnp.bfloat16).reshape(-1, feat_width)
    attn_out = jnp.dot(mixed, w_proj, preferred_element_type=jnp.float32)
    hidden_one = (windows.astype(jnp.float32) + layer_norm(attn_out) * gain_attn).astype(
        jnp.bfloat16
    )
    hidden_one = lax.optimization_barrier(hidden_one)
    inner = jax.nn.gelu(
        jnp.dot(hidden_one, w_fc1, preferred_element_type=jnp.float32), approximate=True
    ).astype(jnp.bfloat16)
    mlp_out = jnp.dot(inner, w_fc2, preferred_element_type=jnp.float32)
    result = (hidden_one.astype(jnp.float32) + layer_norm(mlp_out) * gain_mlp).astype(jnp.bfloat16)
    result = result.reshape(tok_rows // WIN, tok_cols // WIN, WIN, WIN, feat_width).transpose(
        0, 2, 1, 3, 4
    )
    return result.reshape(tok_rows, tok_cols, feat_width)


def readout_mix(query, key_vals, flags, read_scale):
    floe_rows, feat_width = query.shape
    head_count = read_scale.shape[0]
    head_size = feat_width // head_count
    query_unit = unit_heads(query.astype(jnp.float32).reshape(floe_rows, head_count, head_size))
    key_unit = unit_heads(
        key_vals[:, :, :feat_width].astype(jnp.float32).reshape(floe_rows, 4, head_count, head_size)
    )
    values = (
        key_vals[:, :, feat_width:].astype(jnp.float32).reshape(floe_rows, 4, head_count, head_size)
    )
    scores = jnp.sum(query_unit[:, None] * key_unit, -1) * read_scale
    expo = jnp.exp(scores) * flags[:, :, None]
    weights = expo / jnp.sum(expo, 1, keepdims=True)
    return (
        jnp.sum(weights[..., None] * values, 1).reshape(floe_rows, feat_width).astype(jnp.bfloat16)
    )


def flat_send(pieces, send):
    return send(pieces.reshape(-1, pieces.shape[-1])).reshape(pieces.shape)


def pull_rows(pieces, offset):
    return flat_send(pieces, lambda flat: shifted(flat, "gx", offset))


def pull_cols(pieces, offset):
    return flat_send(pieces, lambda flat: shifted(flat, "gy", offset))


def pull_diag(pieces, offset):
    row_devs = lax.axis_size("gx")
    col_devs = lax.axis_size("gy")
    route = [
        (((i - offset) % row_devs) * col_devs + (j - offset) % col_devs, i * col_devs + j)
        for i in range(row_devs)
        for j in range(col_devs)
    ]
    return flat_send(pieces, lambda flat: lax.ppermute(flat, ("gx", "gy"), route))


def roll_ahead(field):
    own = field[SHIFT:, SHIFT:]
    right = pull_cols(field[SHIFT:, :SHIFT], -1)
    below = pull_rows(field[:SHIFT, SHIFT:], -1)
    corner = pull_diag(field[:SHIFT, :SHIFT], -1)
    return jnp.concatenate(
        [jnp.concatenate([own, right], 1), jnp.concatenate([below, corner], 1)], 0
    )


def roll_behind(field, extra):
    tok_rows, tok_cols = field.shape[:2]
    keep_rows = tok_rows - SHIFT + extra
    keep_cols = tok_cols - SHIFT + extra
    corner = pull_diag(field[tok_rows - SHIFT :, tok_cols - SHIFT :], 1)
    above = pull_rows(field[tok_rows - SHIFT :, :keep_cols], 1)
    left = pull_cols(field[:keep_rows, tok_cols - SHIFT :], 1)
    own = field[:keep_rows, :keep_cols]
    return jnp.concatenate(
        [jnp.concatenate([corner, above], 1), jnp.concatenate([left, own], 1)], 0
    )


def one_hot(index, size, dtype=jnp.bfloat16):
    return (index[..., None] == jnp.arange(size, dtype=jnp.int32)).astype(dtype)


def exact_dot(a, b):
    return jnp.dot(a, b, precision=lax.Precision.HIGHEST, preferred_element_type=jnp.float32)


def pick_dot(a, b):
    return jnp.dot(a, b, preferred_element_type=jnp.float32)


def bias_matrix(bias_table, window):
    span = window * window
    flat = jnp.arange(span * span, dtype=jnp.int32)
    query_at = flat // span
    key_at = flat % span
    row_step = query_at // window - key_at // window + window - 1
    col_step = query_at % window - key_at % window + window - 1
    table_at = row_step * (2 * window - 1) + col_step
    picks = one_hot(table_at, bias_table.shape[1], jnp.float32)
    return exact_dot(bias_table, picks.T).reshape(bias_table.shape[0], span, span)


def head_sum(values, head_mat):
    return exact_dot(values, head_mat)


def unit_rows(values, head_mat):
    norms = jnp.maximum(jnp.sqrt(head_sum(values * values, head_mat)), 1.0)
    return values / exact_dot(norms, head_mat.T)


def split_sum(values, picks):
    high = values.astype(jnp.bfloat16)
    low = (values - high.astype(jnp.float32)).astype(jnp.bfloat16)
    return jnp.dot(high, picks, preferred_element_type=jnp.float32) + jnp.dot(
        low, picks, preferred_element_type=jnp.float32
    )


def readout_kernel(ext_cols, piece_ref, table_ref, heads_ref, spread_ref, scale_ref, out_ref, aug_ref):
    rows = piece_ref.shape[0]
    feat_width = out_ref.shape[1]
    head_count = heads_ref.shape[1]
    kv_width = table_ref.shape[1]
    lane = 128
    heads = heads_ref[...]
    spread = spread_ref[...]

    @pl.when(pl.program_id(0) == 0)
    def _():
        table = table_ref[...]
        keys = table[:, :feat_width].astype(jnp.float32)
        norms = jnp.maximum(jnp.sqrt(split_sum(keys * keys, heads)), 1.0)
        place = (
            lax.broadcasted_iota(jnp.int32, (head_count, lane), 0)
            == lax.broadcasted_iota(jnp.int32, (head_count, lane), 1)
        ).astype(jnp.bfloat16)
        aug_ref[:, :kv_width] = table
        rest = norms
        for part in range(3):
            piece_part = rest.astype(jnp.bfloat16)
            rest = rest - piece_part.astype(jnp.float32)
            start = kv_width + part * lane
            aug_ref[:, start : start + lane] = jnp.dot(
                piece_part, place, preferred_element_type=jnp.float32
            ).astype(jnp.bfloat16)

    piece = piece_ref[...]
    query = piece[:, :feat_width].astype(jnp.float32)
    query_norms = jnp.maximum(jnp.sqrt(split_sum(query * query, heads)), 1.0)
    query = query / split_sum(query_norms, spread)
    meta = piece[:, feat_width:].astype(jnp.float32).astype(jnp.int32)
    aug = aug_ref[...]
    scale = scale_ref[...]
    cells = lax.broadcasted_iota(jnp.int32, (rows, aug.shape[0]), 1)
    total = jnp.zeros((rows, head_count), jnp.float32)
    mix = jnp.zeros((rows, feat_width), jnp.float32)
    for corner in range(4):
        down = corner // 2
        side = corner % 2
        at = (meta[:, 0:1] + down) * ext_cols + meta[:, 1:2] + side
        picked = jnp.dot(
            (cells == at).astype(jnp.bfloat16), aug, preferred_element_type=jnp.float32
        )
        key_norms = (
            picked[:, kv_width : kv_width + head_count]
            + picked[:, kv_width + lane : kv_width + lane + head_count]
        ) + picked[:, kv_width + 2 * lane : kv_width + 2 * lane + head_count]
        scores = split_sum(query * picked[:, :feat_width], heads) / key_norms
        expo = jnp.exp(scores * scale)
        if corner > 0:
            expo = expo * meta[:, 1 + corner : 2 + corner].astype(jnp.float32)
        total = total + expo
        mix = mix + split_sum(expo, spread) * picked[:, feat_width:kv_width]
    out_ref[...] = (mix / split_sum(total, spread)).astype(out_ref.dtype)


def readout_call(piece, table, read_scale, ext_cols, block_rows=256):
    floe_rows, piece_width = piece.shape
    head_count = read_scale.shape[0]
    kv_width = table.shape[1]
    feat_width = kv_width // 2
    head_size = feat_width // head_count
    table_rows = -(-table.shape[0] // 16) * 16
    table = jnp.pad(table, ((0, table_rows - table.shape[0]), (0, 0)))
    heads = (
        jnp.arange(feat_width, dtype=jnp.int32)[:, None] // head_size
        == jnp.arange(head_count, dtype=jnp.int32)[None, :]
    ).astype(jnp.bfloat16)
    return pl.pallas_call(
        functools.partial(readout_kernel, ext_cols),
        grid=(floe_rows // block_rows,),
        in_specs=[
            pl.BlockSpec((block_rows, piece_width), lambda i: (i, 0)),
            pl.BlockSpec((table_rows, kv_width), lambda i: (0, 0)),
            pl.BlockSpec((feat_width, head_count), lambda i: (0, 0)),
            pl.BlockSpec((head_count, feat_width), lambda i: (0, 0)),
            pl.BlockSpec((1, head_count), lambda i: (0, 0)),
        ],
        out_specs=pl.BlockSpec((block_rows, feat_width), lambda i: (i, 0)),
        out_shape=jax.ShapeDtypeStruct((floe_rows, feat_width), jnp.bfloat16),
        scratch_shapes=[pltpu.VMEM((table_rows, kv_width + 3 * 128), jnp.bfloat16)],
    )(piece, table, heads, heads.T, read_scale.reshape(1, head_count))


def local(
    wave_tokens,
    grad_out,
    w_qkv,
    w_proj,
    w_fc1,
    w_fc2,
    gain_attn,
    gain_mlp,
    attn_scale,
    bias_table,
    r_wq,
    r_wkv,
    r_wo,
    read_scale,
    floe_feat,
    floe_count,
    floe_patch,
    floe_cover,
):
    tok_rows, tok_cols, feat_width = wave_tokens.shape
    head_count = read_scale.shape[0]
    head_size = feat_width // head_count
    bias_full = bias_matrix(bias_table, WIN)

    def local_block(field):
        return swin_block(
            field, w_qkv, w_proj, w_fc1, w_fc2, gain_attn, gain_mlp, attn_scale, bias_full
        )

    both = roll_ahead(jnp.concatenate([wave_tokens, grad_out], -1))
    ahead = both[..., :feat_width]
    cot_ahead = both[..., feat_width:]
    out_ahead, pull_back = jax.vjp(local_block, ahead)
    out_ext = roll_behind(out_ahead, 1)
    patch_out = out_ext[:tok_rows, :tok_cols]
    ext_cols = tok_cols + 1
    ext_cells = (tok_rows + 1) * ext_cols
    key_table = jnp.dot(
        out_ext.reshape(ext_cells, feat_width), r_wkv, preferred_element_type=jnp.float32
    ).astype(jnp.bfloat16)
    row_devs = lax.axis_size("gx")
    col_devs = lax.axis_size("gy")
    dev_total = row_devs * col_devs
    grid_cols = tok_cols * col_devs
    feat = floe_feat[0]
    floe_slots = feat.shape[0]
    slot_size = floe_slots // dev_total
    patch = floe_patch[0]
    cover = floe_cover[0]
    row_pos = patch // grid_cols
    col_pos = patch % grid_cols
    target = row_pos // tok_rows * col_devs + col_pos // tok_cols
    targets = one_hot(target, dev_total)
    lower = (
        jnp.arange(floe_slots, dtype=jnp.int32)[:, None]
        >= jnp.arange(floe_slots, dtype=jnp.int32)[None, :]
    ).astype(jnp.bfloat16)
    running = pick_dot(lower, targets)
    rank = jnp.sum(running * targets.astype(jnp.float32), -1).astype(jnp.int32) - 1
    place = target * slot_size + rank
    scatter = one_hot(place, floe_slots).T
    meta_width = 128
    meta = jnp.stack(
        [row_pos % tok_rows, col_pos % tok_cols, cover[0], cover[1], cover[2]], -1
    ).astype(jnp.bfloat16)
    meta = jnp.pad(meta, ((0, 0), (0, meta_width - meta.shape[1])))
    query = jnp.dot(feat, r_wq, preferred_element_type=jnp.float32).astype(jnp.bfloat16)
    scatter = scatter.reshape(dev_total, slot_size, floe_slots)
    packed = jnp.einsum(
        "tsf,fc->tsc",
        scatter,
        jnp.concatenate([query, meta], -1),
        preferred_element_type=jnp.float32,
    ).astype(jnp.bfloat16)
    piece = lax.all_to_all(
        packed,
        ("gx", "gy"),
        split_axis=0,
        concat_axis=0,
        tiled=True,
    ).reshape(floe_slots, feat_width + meta_width)
    floe_mix = readout_call(piece, key_table, read_scale, ext_cols)
    floe_mix, cot_ahead = lax.optimization_barrier((floe_mix, cot_ahead))
    returned = lax.all_to_all(
        floe_mix.reshape(dev_total, slot_size, feat_width),
        ("gx", "gy"),
        split_axis=0,
        concat_axis=0,
        tiled=True,
    )
    grad_ahead = pull_back(cot_ahead)[0]
    grad_in = roll_behind(grad_ahead, 0)
    floe_mix = jnp.einsum(
        "tsf,tsc->fc", scatter, returned, preferred_element_type=jnp.float32
    ).astype(jnp.bfloat16)
    updated = feat.astype(jnp.float32) + jnp.dot(floe_mix, r_wo, preferred_element_type=jnp.float32)
    alive = jnp.arange(floe_slots, dtype=jnp.int32) < floe_count[0]
    floe_out = jnp.where(alive[:, None], updated, 0.0).astype(jnp.bfloat16)[None]
    return (patch_out, grad_in, floe_out)


def solution(mesh):
    in_specs = (
        P("gx", "gy", None),
        P("gx", "gy", None),
        P(),
        P(),
        P(),
        P(),
        P(),
        P(),
        P(),
        P(),
        P(),
        P(),
        P(),
        P(),
        P(("gx", "gy"), None, None),
        P(("gx", "gy")),
        P(("gx", "gy"), None),
        P(("gx", "gy"), None, None),
    )
    out_specs = (P("gx", "gy", None), P("gx", "gy", None), P(("gx", "gy"), None, None))
    return jax.shard_map(local, mesh=mesh, in_specs=in_specs, out_specs=out_specs, check_vma=False)
```

```python
import jax
import jax.numpy as jnp
import numpy as np
import functools

from jax import lax
from jax.experimental import pallas as pl
from jax.experimental.pallas import tpu as pltpu
from jax.sharding import PartitionSpec as P

WIN = 8
SHIFT = 4


def shifted(block, axis, distance):
    devices = range(lax.axis_size(axis))
    route = [((i - distance) % len(devices), i) for i in devices]
    return lax.ppermute(block, axis, route)


def layer_norm(values):
    centred = values - jnp.mean(values, -1, keepdims=True)
    return centred / jnp.sqrt(jnp.mean(centred * centred, -1, keepdims=True) + 1e-05)


def unit_heads(values):
    return values / jnp.maximum(jnp.sqrt(jnp.sum(values * values, -1, keepdims=True)), 1.0)


def bias_index(window):
    grid_pos = np.stack(np.meshgrid(np.arange(window), np.arange(window), indexing="ij")).reshape(
        2, -1
    )
    offsets = grid_pos[:, :, None] - grid_pos[:, None, :] + window - 1
    return offsets[0] * (2 * window - 1) + offsets[1]


def swin_block(field, w_qkv, w_proj, w_fc1, w_fc2, gain_attn, gain_mlp, attn_scale, bias_full):
    tok_rows, tok_cols, feat_width = field.shape
    head_count = attn_scale.shape[0]
    head_size = feat_width // head_count
    span = WIN * WIN
    windows = (
        field.reshape(tok_rows // WIN, WIN, tok_cols // WIN, WIN, feat_width)
        .transpose(0, 2, 1, 3, 4)
        .reshape(-1, feat_width)
    )
    win_count = windows.shape[0] // span
    qkv_all = jnp.dot(windows, w_qkv, preferred_element_type=jnp.float32).astype(jnp.bfloat16)
    qkv_all = lax.optimization_barrier(qkv_all)
    qkv_all = qkv_all.reshape(win_count, span, 3, head_count, head_size)
    queries = unit_heads(qkv_all[:, :, 0].astype(jnp.float32))
    keys_unit = unit_heads(qkv_all[:, :, 1].astype(jnp.float32))
    scores = jnp.einsum("wihd,wjhd->whij", queries, keys_unit, precision=lax.Precision.HIGHEST)
    scores = scores * attn_scale[None, :, None, None] + bias_full[None]
    expo = jnp.exp(scores)
    probs = (expo / jnp.sum(expo, -1, keepdims=True)).astype(jnp.bfloat16)
    mixed = jnp.einsum(
        "whij,wjhd->wihd", probs, qkv_all[:, :, 2], preferred_element_type=jnp.float32
    )
    mixed = mixed.astype(jnp.bfloat16).reshape(-1, feat_width)
    attn_out = jnp.dot(mixed, w_proj, preferred_element_type=jnp.float32)
    hidden_one = (windows.astype(jnp.float32) + layer_norm(attn_out) * gain_attn).astype(
        jnp.bfloat16
    )
    hidden_one = lax.optimization_barrier(hidden_one)
    inner = jax.nn.gelu(
        jnp.dot(hidden_one, w_fc1, preferred_element_type=jnp.float32), approximate=True
    ).astype(jnp.bfloat16)
    mlp_out = jnp.dot(inner, w_fc2, preferred_element_type=jnp.float32)
    result = (hidden_one.astype(jnp.float32) + layer_norm(mlp_out) * gain_mlp).astype(jnp.bfloat16)
    result = result.reshape(tok_rows // WIN, tok_cols // WIN, WIN, WIN, feat_width).transpose(
        0, 2, 1, 3, 4
    )
    return result.reshape(tok_rows, tok_cols, feat_width)


def readout_mix(query, key_vals, flags, read_scale):
    floe_rows, feat_width = query.shape
    head_count = read_scale.shape[0]
    head_size = feat_width // head_count
    query_unit = unit_heads(query.astype(jnp.float32).reshape(floe_rows, head_count, head_size))
    key_unit = unit_heads(
        key_vals[:, :, :feat_width].astype(jnp.float32).reshape(floe_rows, 4, head_count, head_size)
    )
    values = (
        key_vals[:, :, feat_width:].astype(jnp.float32).reshape(floe_rows, 4, head_count, head_size)
    )
    scores = jnp.sum(query_unit[:, None] * key_unit, -1) * read_scale
    expo = jnp.exp(scores) * flags[:, :, None]
    weights = expo / jnp.sum(expo, 1, keepdims=True)
    return (
        jnp.sum(weights[..., None] * values, 1).reshape(floe_rows, feat_width).astype(jnp.bfloat16)
    )


def pull_rows(pieces, offset):
    return shifted(pieces, "gx", offset)


def pull_cols(pieces, offset):
    return shifted(pieces, "gy", offset)


def pull_diag(pieces, offset):
    row_devs = lax.axis_size("gx")
    col_devs = lax.axis_size("gy")
    route = [
        (((i - offset) % row_devs) * col_devs + (j - offset) % col_devs, i * col_devs + j)
        for i in range(row_devs)
        for j in range(col_devs)
    ]
    return lax.ppermute(pieces, ("gx", "gy"), route)


def roll_ahead(field):
    own = field[SHIFT:, SHIFT:]
    right = pull_cols(field[SHIFT:, :SHIFT], -1)
    below = pull_rows(field[:SHIFT, SHIFT:], -1)
    corner = pull_diag(field[:SHIFT, :SHIFT], -1)
    return jnp.concatenate(
        [jnp.concatenate([own, right], 1), jnp.concatenate([below, corner], 1)], 0
    )


def roll_behind(field, extra):
    tok_rows, tok_cols = field.shape[:2]
    keep_rows = tok_rows - SHIFT + extra
    keep_cols = tok_cols - SHIFT + extra
    corner = pull_diag(field[tok_rows - SHIFT :, tok_cols - SHIFT :], 1)
    above = pull_rows(field[tok_rows - SHIFT :, :keep_cols], 1)
    left = pull_cols(field[:keep_rows, tok_cols - SHIFT :], 1)
    own = field[:keep_rows, :keep_cols]
    return jnp.concatenate(
        [jnp.concatenate([corner, above], 1), jnp.concatenate([left, own], 1)], 0
    )


def one_hot(index, size, dtype=jnp.bfloat16):
    return (index[..., None] == jnp.arange(size, dtype=jnp.int32)).astype(dtype)


def exact_dot(a, b):
    return jnp.dot(a, b, precision=lax.Precision.HIGHEST, preferred_element_type=jnp.float32)


def pick_dot(a, b):
    return jnp.dot(a, b, preferred_element_type=jnp.float32)


def bias_matrix(bias_table, window):
    span = window * window
    flat = jnp.arange(span * span, dtype=jnp.int32)
    query_at = flat // span
    key_at = flat % span
    row_step = query_at // window - key_at // window + window - 1
    col_step = query_at % window - key_at % window + window - 1
    table_at = row_step * (2 * window - 1) + col_step
    picks = one_hot(table_at, bias_table.shape[1], jnp.float32)
    return exact_dot(bias_table, picks.T).reshape(bias_table.shape[0], span, span)


def head_sum(values, head_mat):
    return exact_dot(values, head_mat)


def unit_rows(values, head_mat):
    norms = jnp.maximum(jnp.sqrt(head_sum(values * values, head_mat)), 1.0)
    return values / exact_dot(norms, head_mat.T)


def split_sum(values, picks):
    high = values.astype(jnp.bfloat16)
    low = (values - high.astype(jnp.float32)).astype(jnp.bfloat16)
    return jnp.dot(high, picks, preferred_element_type=jnp.float32) + jnp.dot(
        low, picks, preferred_element_type=jnp.float32
    )


def readout_kernel(
    ext_cols, piece_ref, tokens_ref, weight_ref, heads_ref, spread_ref, scale_ref, out_ref, aug_ref
):
    rows = piece_ref.shape[0]
    feat_width = out_ref.shape[1]
    head_count = heads_ref.shape[1]
    kv_width = weight_ref.shape[1]
    lane = 128
    heads = heads_ref[...]
    spread = spread_ref[...]

    @pl.when(pl.program_id(0) == 0)
    def _():
        table = jnp.dot(
            tokens_ref[...], weight_ref[...], preferred_element_type=jnp.float32
        ).astype(jnp.bfloat16)
        keys = table[:, :feat_width].astype(jnp.float32)
        norms = jnp.maximum(jnp.sqrt(split_sum(keys * keys, heads)), 1.0)
        place = (
            lax.broadcasted_iota(jnp.int32, (head_count, lane), 0)
            == lax.broadcasted_iota(jnp.int32, (head_count, lane), 1)
        ).astype(jnp.bfloat16)
        aug_ref[:, :kv_width] = table
        rest = norms
        for part in range(3):
            piece_part = rest.astype(jnp.bfloat16)
            rest = rest - piece_part.astype(jnp.float32)
            start = kv_width + part * lane
            aug_ref[:, start : start + lane] = jnp.dot(
                piece_part, place, preferred_element_type=jnp.float32
            ).astype(jnp.bfloat16)

    piece = piece_ref[...]
    query = piece[:, :feat_width].astype(jnp.float32)
    query_norms = jnp.maximum(jnp.sqrt(split_sum(query * query, heads)), 1.0)
    query = query / split_sum(query_norms, spread)
    meta = piece[:, feat_width:].astype(jnp.float32).astype(jnp.int32)
    aug = aug_ref[...]
    scale = scale_ref[...]
    cells = lax.broadcasted_iota(jnp.int32, (rows, aug.shape[0]), 1)
    total = jnp.zeros((rows, head_count), jnp.float32)
    mix = jnp.zeros((rows, feat_width), jnp.float32)
    for corner in range(4):
        down = corner // 2
        side = corner % 2
        at = (meta[:, 0:1] + down) * ext_cols + meta[:, 1:2] + side
        picked = jnp.dot(
            (cells == at).astype(jnp.bfloat16), aug, preferred_element_type=jnp.float32
        )
        key_norms = (
            picked[:, kv_width : kv_width + head_count]
            + picked[:, kv_width + lane : kv_width + lane + head_count]
        ) + picked[:, kv_width + 2 * lane : kv_width + 2 * lane + head_count]
        scores = split_sum(query * picked[:, :feat_width], heads) / key_norms
        expo = jnp.exp(scores * scale)
        if corner > 0:
            expo = expo * meta[:, 1 + corner : 2 + corner].astype(jnp.float32)
        total = total + expo
        mix = mix + split_sum(expo, spread) * picked[:, feat_width:kv_width]
    out_ref[...] = (mix / split_sum(total, spread)).astype(out_ref.dtype)


def readout_call(piece, tokens, weight, read_scale, ext_cols, block_rows=256):
    floe_rows, piece_width = piece.shape
    head_count = read_scale.shape[0]
    kv_width = weight.shape[1]
    feat_width = kv_width // 2
    head_size = feat_width // head_count
    table_rows = -(-tokens.shape[0] // 16) * 16
    tokens = jnp.pad(tokens, ((0, table_rows - tokens.shape[0]), (0, 0)))
    heads = (
        jnp.arange(feat_width, dtype=jnp.int32)[:, None] // head_size
        == jnp.arange(head_count, dtype=jnp.int32)[None, :]
    ).astype(jnp.bfloat16)
    return pl.pallas_call(
        functools.partial(readout_kernel, ext_cols),
        grid=(floe_rows // block_rows,),
        in_specs=[
            pl.BlockSpec((block_rows, piece_width), lambda i: (i, 0)),
            pl.BlockSpec((table_rows, feat_width), lambda i: (0, 0)),
            pl.BlockSpec((feat_width, kv_width), lambda i: (0, 0)),
            pl.BlockSpec((feat_width, head_count), lambda i: (0, 0)),
            pl.BlockSpec((head_count, feat_width), lambda i: (0, 0)),
            pl.BlockSpec((1, head_count), lambda i: (0, 0)),
        ],
        out_specs=pl.BlockSpec((block_rows, feat_width), lambda i: (i, 0)),
        out_shape=jax.ShapeDtypeStruct((floe_rows, feat_width), jnp.bfloat16),
        scratch_shapes=[pltpu.VMEM((table_rows, kv_width + 3 * 128), jnp.bfloat16)],
    )(piece, tokens, weight, heads, heads.T, read_scale.reshape(1, head_count))


def local(
    wave_tokens,
    grad_out,
    w_qkv,
    w_proj,
    w_fc1,
    w_fc2,
    gain_attn,
    gain_mlp,
    attn_scale,
    bias_table,
    r_wq,
    r_wkv,
    r_wo,
    read_scale,
    floe_feat,
    floe_count,
    floe_patch,
    floe_cover,
):
    tok_rows, tok_cols, feat_width = wave_tokens.shape
    head_count = read_scale.shape[0]
    head_size = feat_width // head_count
    bias_full = bias_matrix(bias_table, WIN)

    def local_block(field):
        return swin_block(
            field, w_qkv, w_proj, w_fc1, w_fc2, gain_attn, gain_mlp, attn_scale, bias_full
        )

    both = roll_ahead(jnp.concatenate([wave_tokens, grad_out], -1))
    ahead = both[..., :feat_width]
    cot_ahead = both[..., feat_width:]
    out_ahead, pull_back = jax.vjp(local_block, ahead)
    out_ext = roll_behind(out_ahead, 1)
    patch_out = out_ext[:tok_rows, :tok_cols]
    ext_cols = tok_cols + 1
    ext_cells = (tok_rows + 1) * ext_cols
    ext_tokens = out_ext.reshape(ext_cells, feat_width)
    row_devs = lax.axis_size("gx")
    col_devs = lax.axis_size("gy")
    dev_total = row_devs * col_devs
    grid_cols = tok_cols * col_devs
    feat = floe_feat[0]
    floe_slots = feat.shape[0]
    slot_size = floe_slots // dev_total
    patch = floe_patch[0]
    cover = floe_cover[0]
    row_pos = patch // grid_cols
    col_pos = patch % grid_cols
    target = row_pos // tok_rows * col_devs + col_pos // tok_cols
    targets = one_hot(target, dev_total)
    lower = (
        jnp.arange(floe_slots, dtype=jnp.int32)[:, None]
        >= jnp.arange(floe_slots, dtype=jnp.int32)[None, :]
    ).astype(jnp.bfloat16)
    running = pick_dot(lower, targets)
    rank = jnp.sum(running * targets.astype(jnp.float32), -1).astype(jnp.int32) - 1
    place = target * slot_size + rank
    scatter = one_hot(place, floe_slots).T
    meta_width = 128
    meta = jnp.stack(
        [row_pos % tok_rows, col_pos % tok_cols, cover[0], cover[1], cover[2]], -1
    ).astype(jnp.bfloat16)
    meta = jnp.pad(meta, ((0, 0), (0, meta_width - meta.shape[1])))
    query = jnp.dot(feat, r_wq, preferred_element_type=jnp.float32).astype(jnp.bfloat16)
    scatter = scatter.reshape(dev_total, slot_size, floe_slots)
    packed = jnp.einsum(
        "tsf,fc->tsc",
        scatter,
        jnp.concatenate([query, meta], -1),
        preferred_element_type=jnp.float32,
    ).astype(jnp.bfloat16)
    piece = lax.all_to_all(
        packed,
        ("gx", "gy"),
        split_axis=0,
        concat_axis=0,
        tiled=True,
    ).reshape(floe_slots, feat_width + meta_width)
    floe_mix = readout_call(piece, ext_tokens, r_wkv, read_scale, ext_cols)
    floe_mix, cot_ahead = lax.optimization_barrier((floe_mix, cot_ahead))
    returned = lax.all_to_all(
        floe_mix.reshape(dev_total, slot_size, feat_width),
        ("gx", "gy"),
        split_axis=0,
        concat_axis=0,
        tiled=True,
    )
    grad_ahead = pull_back(cot_ahead)[0]
    grad_in = roll_behind(grad_ahead, 0)
    floe_mix = jnp.einsum(
        "tsf,tsc->fc", scatter, returned, preferred_element_type=jnp.float32
    ).astype(jnp.bfloat16)
    updated = feat.astype(jnp.float32) + jnp.dot(floe_mix, r_wo, preferred_element_type=jnp.float32)
    alive = jnp.arange(floe_slots, dtype=jnp.int32) < floe_count[0]
    floe_out = jnp.where(alive[:, None], updated, 0.0).astype(jnp.bfloat16)[None]
    return (patch_out, grad_in, floe_out)


def solution(mesh):
    in_specs = (
        P("gx", "gy", None),
        P("gx", "gy", None),
        P(),
        P(),
        P(),
        P(),
        P(),
        P(),
        P(),
        P(),
        P(),
        P(),
        P(),
        P(),
        P(("gx", "gy"), None, None),
        P(("gx", "gy")),
        P(("gx", "gy"), None),
        P(("gx", "gy"), None, None),
    )
    out_specs = (P("gx", "gy", None), P("gx", "gy", None), P(("gx", "gy"), None, None))
    return jax.shard_map(local, mesh=mesh, in_specs=in_specs, out_specs=out_specs, check_vma=False)
```

```python
import jax
import jax.numpy as jnp
import numpy as np
import functools

from jax import lax
from jax.experimental import pallas as pl
from jax.experimental.pallas import tpu as pltpu
from jax.sharding import PartitionSpec as P

WIN = 8
SHIFT = 4


def shifted(block, axis, distance):
    devices = range(lax.axis_size(axis))
    route = [((i - distance) % len(devices), i) for i in devices]
    return lax.ppermute(block, axis, route)


def layer_norm(values):
    centred = values - jnp.mean(values, -1, keepdims=True)
    return centred / jnp.sqrt(jnp.mean(centred * centred, -1, keepdims=True) + 1e-05)


def unit_heads(values):
    return values / jnp.maximum(jnp.sqrt(jnp.sum(values * values, -1, keepdims=True)), 1.0)


def bias_index(window):
    grid_pos = np.stack(np.meshgrid(np.arange(window), np.arange(window), indexing="ij")).reshape(
        2, -1
    )
    offsets = grid_pos[:, :, None] - grid_pos[:, None, :] + window - 1
    return offsets[0] * (2 * window - 1) + offsets[1]


def swin_block(field, w_qkv, w_proj, w_fc1, w_fc2, gain_attn, gain_mlp, attn_scale, bias_full):
    tok_rows, tok_cols, feat_width = field.shape
    head_count = attn_scale.shape[0]
    head_size = feat_width // head_count
    span = WIN * WIN
    windows = (
        field.reshape(tok_rows // WIN, WIN, tok_cols // WIN, WIN, feat_width)
        .transpose(0, 2, 1, 3, 4)
        .reshape(-1, feat_width)
    )
    win_count = windows.shape[0] // span
    qkv_all = jnp.dot(windows, w_qkv, preferred_element_type=jnp.float32).astype(jnp.bfloat16)
    qkv_all = lax.optimization_barrier(qkv_all)
    qkv_all = qkv_all.reshape(win_count, span, 3, head_count, head_size)
    queries = unit_heads(qkv_all[:, :, 0].astype(jnp.float32))
    keys_unit = unit_heads(qkv_all[:, :, 1].astype(jnp.float32))
    scores = jnp.einsum("wihd,wjhd->whij", queries, keys_unit, precision=lax.Precision.HIGHEST)
    scores = scores * attn_scale[None, :, None, None] + bias_full[None]
    expo = jnp.exp(scores)
    probs = (expo / jnp.sum(expo, -1, keepdims=True)).astype(jnp.bfloat16)
    mixed = jnp.einsum(
        "whij,wjhd->wihd", probs, qkv_all[:, :, 2], preferred_element_type=jnp.float32
    )
    mixed = mixed.astype(jnp.bfloat16).reshape(-1, feat_width)
    attn_out = jnp.dot(mixed, w_proj, preferred_element_type=jnp.float32)
    hidden_one = (windows.astype(jnp.float32) + layer_norm(attn_out) * gain_attn).astype(
        jnp.bfloat16
    )
    hidden_one = lax.optimization_barrier(hidden_one)
    inner = jax.nn.gelu(
        jnp.dot(hidden_one, w_fc1, preferred_element_type=jnp.float32), approximate=True
    ).astype(jnp.bfloat16)
    mlp_out = jnp.dot(inner, w_fc2, preferred_element_type=jnp.float32)
    result = (hidden_one.astype(jnp.float32) + layer_norm(mlp_out) * gain_mlp).astype(jnp.bfloat16)
    result = result.reshape(tok_rows // WIN, tok_cols // WIN, WIN, WIN, feat_width).transpose(
        0, 2, 1, 3, 4
    )
    return result.reshape(tok_rows, tok_cols, feat_width)


def readout_mix(query, key_vals, flags, read_scale):
    floe_rows, feat_width = query.shape
    head_count = read_scale.shape[0]
    head_size = feat_width // head_count
    query_unit = unit_heads(query.astype(jnp.float32).reshape(floe_rows, head_count, head_size))
    key_unit = unit_heads(
        key_vals[:, :, :feat_width].astype(jnp.float32).reshape(floe_rows, 4, head_count, head_size)
    )
    values = (
        key_vals[:, :, feat_width:].astype(jnp.float32).reshape(floe_rows, 4, head_count, head_size)
    )
    scores = jnp.sum(query_unit[:, None] * key_unit, -1) * read_scale
    expo = jnp.exp(scores) * flags[:, :, None]
    weights = expo / jnp.sum(expo, 1, keepdims=True)
    return (
        jnp.sum(weights[..., None] * values, 1).reshape(floe_rows, feat_width).astype(jnp.bfloat16)
    )


def pull_rows(pieces, offset):
    return shifted(pieces, "gx", offset)


def pull_cols(pieces, offset):
    return shifted(pieces, "gy", offset)


def pull_diag(pieces, offset):
    row_devs = lax.axis_size("gx")
    col_devs = lax.axis_size("gy")
    route = [
        (((i - offset) % row_devs) * col_devs + (j - offset) % col_devs, i * col_devs + j)
        for i in range(row_devs)
        for j in range(col_devs)
    ]
    return lax.ppermute(pieces, ("gx", "gy"), route)


def roll_ahead(field):
    own = field[SHIFT:, SHIFT:]
    right = pull_cols(field[SHIFT:, :SHIFT], -1)
    below = pull_rows(field[:SHIFT, SHIFT:], -1)
    corner = pull_diag(field[:SHIFT, :SHIFT], -1)
    return jnp.concatenate(
        [jnp.concatenate([own, right], 1), jnp.concatenate([below, corner], 1)], 0
    )


def roll_behind(field, extra):
    tok_rows, tok_cols = field.shape[:2]
    keep_rows = tok_rows - SHIFT + extra
    keep_cols = tok_cols - SHIFT + extra
    corner = pull_diag(field[tok_rows - SHIFT :, tok_cols - SHIFT :], 1)
    above = pull_rows(field[tok_rows - SHIFT :, :keep_cols], 1)
    left = pull_cols(field[:keep_rows, tok_cols - SHIFT :], 1)
    own = field[:keep_rows, :keep_cols]
    return jnp.concatenate(
        [jnp.concatenate([corner, above], 1), jnp.concatenate([left, own], 1)], 0
    )


def one_hot(index, size, dtype=jnp.bfloat16):
    return (index[..., None] == jnp.arange(size, dtype=jnp.int32)).astype(dtype)


def exact_dot(a, b):
    return jnp.dot(a, b, precision=lax.Precision.HIGHEST, preferred_element_type=jnp.float32)


def pick_dot(a, b):
    return jnp.dot(a, b, preferred_element_type=jnp.float32)


def bias_matrix(bias_table, window):
    span = window * window
    flat = jnp.arange(span * span, dtype=jnp.int32)
    query_at = flat // span
    key_at = flat % span
    row_step = query_at // window - key_at // window + window - 1
    col_step = query_at % window - key_at % window + window - 1
    table_at = row_step * (2 * window - 1) + col_step
    picks = one_hot(table_at, bias_table.shape[1], jnp.float32)
    return exact_dot(bias_table, picks.T).reshape(bias_table.shape[0], span, span)


def head_sum(values, head_mat):
    return exact_dot(values, head_mat)


def unit_rows(values, head_mat):
    norms = jnp.maximum(jnp.sqrt(head_sum(values * values, head_mat)), 1.0)
    return values / exact_dot(norms, head_mat.T)


def split_sum(values, picks):
    high = values.astype(jnp.bfloat16)
    low = (values - high.astype(jnp.float32)).astype(jnp.bfloat16)
    return jnp.dot(high, picks, preferred_element_type=jnp.float32) + jnp.dot(
        low, picks, preferred_element_type=jnp.float32
    )


def readout_kernel(
    ext_cols, piece_ref, tokens_ref, weight_ref, heads_ref, spread_ref, scale_ref, out_ref, aug_ref
):
    rows = piece_ref.shape[0]
    feat_width = out_ref.shape[1]
    head_count = heads_ref.shape[1]
    kv_width = weight_ref.shape[1]
    lane = 128
    heads = heads_ref[...]
    spread = spread_ref[...]

    @pl.when(pl.program_id(0) == 0)
    def _():
        table = jnp.dot(
            tokens_ref[...], weight_ref[...], preferred_element_type=jnp.float32
        ).astype(jnp.bfloat16)
        keys = table[:, :feat_width].astype(jnp.float32)
        norms = jnp.maximum(jnp.sqrt(split_sum(keys * keys, heads)), 1.0)
        place = (
            lax.broadcasted_iota(jnp.int32, (head_count, lane), 0)
            == lax.broadcasted_iota(jnp.int32, (head_count, lane), 1)
        ).astype(jnp.bfloat16)
        aug_ref[:, :kv_width] = table
        rest = norms
        for part in range(3):
            piece_part = rest.astype(jnp.bfloat16)
            rest = rest - piece_part.astype(jnp.float32)
            start = kv_width + part * lane
            aug_ref[:, start : start + lane] = jnp.dot(
                piece_part, place, preferred_element_type=jnp.float32
            ).astype(jnp.bfloat16)

    piece = piece_ref[...]
    query = piece[:, :feat_width].astype(jnp.float32)
    query_norms = jnp.maximum(jnp.sqrt(split_sum(query * query, heads)), 1.0)
    query = query / split_sum(query_norms, spread)
    meta = piece[:, feat_width:].astype(jnp.float32).astype(jnp.int32)
    aug = aug_ref[...]
    scale = scale_ref[...]
    cells = lax.broadcasted_iota(jnp.int32, (rows, aug.shape[0]), 1)
    total = jnp.zeros((rows, head_count), jnp.float32)
    mix = jnp.zeros((rows, feat_width), jnp.float32)
    for corner in range(4):
        down = corner // 2
        side = corner % 2
        at = (meta[:, 0:1] + down) * ext_cols + meta[:, 1:2] + side
        picked = jnp.dot(
            (cells == at).astype(jnp.bfloat16), aug, preferred_element_type=jnp.float32
        )
        key_norms = (
            picked[:, kv_width : kv_width + head_count]
            + picked[:, kv_width + lane : kv_width + lane + head_count]
        ) + picked[:, kv_width + 2 * lane : kv_width + 2 * lane + head_count]
        scores = split_sum(query * picked[:, :feat_width], heads) / key_norms
        expo = jnp.exp(scores * scale)
        if corner > 0:
            expo = expo * meta[:, 1 + corner : 2 + corner].astype(jnp.float32)
        total = total + expo
        mix = mix + split_sum(expo, spread) * picked[:, feat_width:kv_width]
    out_ref[...] = (mix / split_sum(total, spread)).astype(out_ref.dtype)


def readout_call(piece, tokens, weight, read_scale, ext_cols, block_rows=256):
    floe_rows, piece_width = piece.shape
    head_count = read_scale.shape[0]
    kv_width = weight.shape[1]
    feat_width = kv_width // 2
    head_size = feat_width // head_count
    table_rows = -(-tokens.shape[0] // 16) * 16
    tokens = jnp.pad(tokens, ((0, table_rows - tokens.shape[0]), (0, 0)))
    heads = (
        jnp.arange(feat_width, dtype=jnp.int32)[:, None] // head_size
        == jnp.arange(head_count, dtype=jnp.int32)[None, :]
    ).astype(jnp.bfloat16)
    return pl.pallas_call(
        functools.partial(readout_kernel, ext_cols),
        grid=(floe_rows // block_rows,),
        in_specs=[
            pl.BlockSpec((block_rows, piece_width), lambda i: (i, 0)),
            pl.BlockSpec((table_rows, feat_width), lambda i: (0, 0)),
            pl.BlockSpec((feat_width, kv_width), lambda i: (0, 0)),
            pl.BlockSpec((feat_width, head_count), lambda i: (0, 0)),
            pl.BlockSpec((head_count, feat_width), lambda i: (0, 0)),
            pl.BlockSpec((1, head_count), lambda i: (0, 0)),
        ],
        out_specs=pl.BlockSpec((block_rows, feat_width), lambda i: (i, 0)),
        out_shape=jax.ShapeDtypeStruct((floe_rows, feat_width), jnp.bfloat16),
        scratch_shapes=[pltpu.VMEM((table_rows, kv_width + 3 * 128), jnp.bfloat16)],
    )(piece, tokens, weight, heads, heads.T, read_scale.reshape(1, head_count))


def local(
    wave_tokens,
    grad_out,
    w_qkv,
    w_proj,
    w_fc1,
    w_fc2,
    gain_attn,
    gain_mlp,
    attn_scale,
    bias_table,
    r_wq,
    r_wkv,
    r_wo,
    read_scale,
    floe_feat,
    floe_count,
    floe_patch,
    floe_cover,
):
    tok_rows, tok_cols, feat_width = wave_tokens.shape
    head_count = read_scale.shape[0]
    head_size = feat_width // head_count
    bias_full = bias_matrix(bias_table, WIN)

    def local_block(field):
        return swin_block(
            field, w_qkv, w_proj, w_fc1, w_fc2, gain_attn, gain_mlp, attn_scale, bias_full
        )

    both = roll_ahead(jnp.concatenate([wave_tokens, grad_out], -1))
    ahead = both[..., :feat_width]
    cot_ahead = both[..., feat_width:]
    out_ahead, pull_back = jax.vjp(local_block, ahead)
    out_ext = roll_behind(out_ahead, 1)
    patch_out = out_ext[:tok_rows, :tok_cols]
    ext_cols = tok_cols + 1
    ext_cells = (tok_rows + 1) * ext_cols
    ext_tokens = out_ext.reshape(ext_cells, feat_width)
    row_devs = lax.axis_size("gx")
    col_devs = lax.axis_size("gy")
    dev_total = row_devs * col_devs
    grid_cols = tok_cols * col_devs
    feat = floe_feat[0]
    floe_slots = feat.shape[0]
    slot_size = floe_slots // dev_total
    patch = floe_patch[0]
    cover = floe_cover[0]
    row_pos = patch // grid_cols
    col_pos = patch % grid_cols
    target = row_pos // tok_rows * col_devs + col_pos // tok_cols
    targets = one_hot(target, dev_total)
    lower = (
        jnp.arange(floe_slots, dtype=jnp.int32)[:, None]
        >= jnp.arange(floe_slots, dtype=jnp.int32)[None, :]
    ).astype(jnp.bfloat16)
    running = pick_dot(lower, targets)
    rank = jnp.sum(running * targets.astype(jnp.float32), -1).astype(jnp.int32) - 1
    place = target * slot_size + rank
    scatter = one_hot(place, floe_slots).T
    meta_width = 128
    meta = jnp.stack(
        [row_pos % tok_rows, col_pos % tok_cols, cover[0], cover[1], cover[2]], -1
    ).astype(jnp.bfloat16)
    meta = jnp.pad(meta, ((0, 0), (0, meta_width - meta.shape[1])))
    query = jnp.dot(feat, r_wq, preferred_element_type=jnp.float32).astype(jnp.bfloat16)
    scatter = scatter.reshape(dev_total, slot_size, floe_slots)
    packed = jnp.einsum(
        "tsf,fc->tsc",
        scatter,
        jnp.concatenate([query, meta], -1),
        preferred_element_type=jnp.float32,
    ).astype(jnp.bfloat16)
    piece = lax.all_to_all(
        packed,
        ("gx", "gy"),
        split_axis=0,
        concat_axis=0,
        tiled=True,
    ).reshape(floe_slots, feat_width + meta_width)
    floe_mix = readout_call(piece, ext_tokens, r_wkv, read_scale, ext_cols)
    floe_mix, cot_ahead = lax.optimization_barrier((floe_mix, cot_ahead))
    returned = lax.all_to_all(
        floe_mix.reshape(dev_total, slot_size, feat_width),
        ("gx", "gy"),
        split_axis=0,
        concat_axis=0,
        tiled=True,
    )
    grad_ahead = pull_back(cot_ahead)[0]
    returned, grad_ahead = lax.optimization_barrier((returned, grad_ahead))
    grad_in = roll_behind(grad_ahead, 0)
    floe_mix = jnp.einsum(
        "tsf,tsc->fc", scatter, returned, preferred_element_type=jnp.float32
    ).astype(jnp.bfloat16)
    updated = feat.astype(jnp.float32) + jnp.dot(floe_mix, r_wo, preferred_element_type=jnp.float32)
    alive = jnp.arange(floe_slots, dtype=jnp.int32) < floe_count[0]
    floe_out = jnp.where(alive[:, None], updated, 0.0).astype(jnp.bfloat16)[None]
    return (patch_out, grad_in, floe_out)


def solution(mesh):
    in_specs = (
        P("gx", "gy", None),
        P("gx", "gy", None),
        P(),
        P(),
        P(),
        P(),
        P(),
        P(),
        P(),
        P(),
        P(),
        P(),
        P(),
        P(),
        P(("gx", "gy"), None, None),
        P(("gx", "gy")),
        P(("gx", "gy"), None),
        P(("gx", "gy"), None, None),
    )
    out_specs = (P("gx", "gy", None), P("gx", "gy", None), P(("gx", "gy"), None, None))
    return jax.shard_map(local, mesh=mesh, in_specs=in_specs, out_specs=out_specs, check_vma=False)
```

```python
import jax
import jax.numpy as jnp
import numpy as np
import functools

from jax import lax
from jax.experimental import pallas as pl
from jax.experimental.pallas import tpu as pltpu
from jax.sharding import PartitionSpec as P

WIN = 8
SHIFT = 4


def shifted(block, axis, distance):
    devices = range(lax.axis_size(axis))
    route = [((i - distance) % len(devices), i) for i in devices]
    return lax.ppermute(block, axis, route)


def layer_norm(values):
    centred = values - jnp.mean(values, -1, keepdims=True)
    return centred / jnp.sqrt(jnp.mean(centred * centred, -1, keepdims=True) + 1e-05)


def unit_heads(values):
    return values / jnp.maximum(jnp.sqrt(jnp.sum(values * values, -1, keepdims=True)), 1.0)


def bias_index(window):
    grid_pos = np.stack(np.meshgrid(np.arange(window), np.arange(window), indexing="ij")).reshape(
        2, -1
    )
    offsets = grid_pos[:, :, None] - grid_pos[:, None, :] + window - 1
    return offsets[0] * (2 * window - 1) + offsets[1]


def swin_block(field, w_qkv, w_proj, w_fc1, w_fc2, gain_attn, gain_mlp, attn_scale, bias_full):
    tok_rows, tok_cols, feat_width = field.shape
    head_count = attn_scale.shape[0]
    head_size = feat_width // head_count
    span = WIN * WIN
    windows = (
        field.reshape(tok_rows // WIN, WIN, tok_cols // WIN, WIN, feat_width)
        .transpose(0, 2, 1, 3, 4)
        .reshape(-1, feat_width)
    )
    win_count = windows.shape[0] // span
    qkv_all = jnp.dot(windows, w_qkv, preferred_element_type=jnp.float32).astype(jnp.bfloat16)
    qkv_all = lax.optimization_barrier(qkv_all)
    qkv_all = qkv_all.reshape(win_count, span, 3, head_count, head_size)
    queries = unit_heads(qkv_all[:, :, 0].astype(jnp.float32))
    keys_unit = unit_heads(qkv_all[:, :, 1].astype(jnp.float32))
    scores = jnp.einsum("wihd,wjhd->whij", queries, keys_unit, precision=lax.Precision.HIGHEST)
    scores = scores * attn_scale[None, :, None, None] + bias_full[None]
    expo = jnp.exp(scores)
    probs = (expo / jnp.sum(expo, -1, keepdims=True)).astype(jnp.bfloat16)
    mixed = jnp.einsum(
        "whij,wjhd->wihd", probs, qkv_all[:, :, 2], preferred_element_type=jnp.float32
    )
    mixed = mixed.astype(jnp.bfloat16).reshape(-1, feat_width)
    attn_out = jnp.dot(mixed, w_proj, preferred_element_type=jnp.float32)
    hidden_one = (windows.astype(jnp.float32) + layer_norm(attn_out) * gain_attn).astype(
        jnp.bfloat16
    )
    hidden_one = lax.optimization_barrier(hidden_one)
    inner = jax.nn.gelu(
        jnp.dot(hidden_one, w_fc1, preferred_element_type=jnp.float32), approximate=True
    ).astype(jnp.bfloat16)
    mlp_out = jnp.dot(inner, w_fc2, preferred_element_type=jnp.float32)
    result = (hidden_one.astype(jnp.float32) + layer_norm(mlp_out) * gain_mlp).astype(jnp.bfloat16)
    result = result.reshape(tok_rows // WIN, tok_cols // WIN, WIN, WIN, feat_width).transpose(
        0, 2, 1, 3, 4
    )
    return result.reshape(tok_rows, tok_cols, feat_width)


def readout_mix(query, key_vals, flags, read_scale):
    floe_rows, feat_width = query.shape
    head_count = read_scale.shape[0]
    head_size = feat_width // head_count
    query_unit = unit_heads(query.astype(jnp.float32).reshape(floe_rows, head_count, head_size))
    key_unit = unit_heads(
        key_vals[:, :, :feat_width].astype(jnp.float32).reshape(floe_rows, 4, head_count, head_size)
    )
    values = (
        key_vals[:, :, feat_width:].astype(jnp.float32).reshape(floe_rows, 4, head_count, head_size)
    )
    scores = jnp.sum(query_unit[:, None] * key_unit, -1) * read_scale
    expo = jnp.exp(scores) * flags[:, :, None]
    weights = expo / jnp.sum(expo, 1, keepdims=True)
    return (
        jnp.sum(weights[..., None] * values, 1).reshape(floe_rows, feat_width).astype(jnp.bfloat16)
    )


def pull_rows(pieces, offset):
    return shifted(pieces, "gx", offset)


def pull_cols(pieces, offset):
    return shifted(pieces, "gy", offset)


def pull_diag(pieces, offset):
    row_devs = lax.axis_size("gx")
    col_devs = lax.axis_size("gy")
    route = [
        (((i - offset) % row_devs) * col_devs + (j - offset) % col_devs, i * col_devs + j)
        for i in range(row_devs)
        for j in range(col_devs)
    ]
    return lax.ppermute(pieces, ("gx", "gy"), route)


def roll_ahead(field):
    own = field[SHIFT:, SHIFT:]
    right = pull_cols(field[SHIFT:, :SHIFT], -1)
    below = pull_rows(field[:SHIFT, SHIFT:], -1)
    corner = pull_diag(field[:SHIFT, :SHIFT], -1)
    return jnp.concatenate(
        [jnp.concatenate([own, right], 1), jnp.concatenate([below, corner], 1)], 0
    )


def roll_behind(field, extra):
    tok_rows, tok_cols = field.shape[:2]
    keep_rows = tok_rows - SHIFT + extra
    keep_cols = tok_cols - SHIFT + extra
    corner = pull_diag(field[tok_rows - SHIFT :, tok_cols - SHIFT :], 1)
    above = pull_rows(field[tok_rows - SHIFT :, :keep_cols], 1)
    left = pull_cols(field[:keep_rows, tok_cols - SHIFT :], 1)
    own = field[:keep_rows, :keep_cols]
    return jnp.concatenate(
        [jnp.concatenate([corner, above], 1), jnp.concatenate([left, own], 1)], 0
    )


def one_hot(index, size, dtype=jnp.bfloat16):
    return (index[..., None] == jnp.arange(size, dtype=jnp.int32)).astype(dtype)


def exact_dot(a, b):
    return jnp.dot(a, b, precision=lax.Precision.HIGHEST, preferred_element_type=jnp.float32)


def pick_dot(a, b):
    return jnp.dot(a, b, preferred_element_type=jnp.float32)


def bias_matrix(bias_table, window):
    span = window * window
    flat = jnp.arange(span * span, dtype=jnp.int32)
    query_at = flat // span
    key_at = flat % span
    row_step = query_at // window - key_at // window + window - 1
    col_step = query_at % window - key_at % window + window - 1
    table_at = row_step * (2 * window - 1) + col_step
    picks = one_hot(table_at, bias_table.shape[1], jnp.float32)
    return exact_dot(bias_table, picks.T).reshape(bias_table.shape[0], span, span)


def head_sum(values, head_mat):
    return exact_dot(values, head_mat)


def unit_rows(values, head_mat):
    norms = jnp.maximum(jnp.sqrt(head_sum(values * values, head_mat)), 1.0)
    return values / exact_dot(norms, head_mat.T)


def split_sum(values, picks):
    high = values.astype(jnp.bfloat16)
    low = (values - high.astype(jnp.float32)).astype(jnp.bfloat16)
    return jnp.dot(high, picks, preferred_element_type=jnp.float32) + jnp.dot(
        low, picks, preferred_element_type=jnp.float32
    )


def readout_kernel(
    ext_cols, piece_ref, tokens_ref, weight_ref, heads_ref, spread_ref, scale_ref, out_ref, aug_ref
):
    rows = piece_ref.shape[0]
    feat_width = out_ref.shape[1]
    head_count = heads_ref.shape[1]
    kv_width = weight_ref.shape[1]
    lane = 128
    heads = heads_ref[...]
    spread = spread_ref[...]

    @pl.when(pl.program_id(0) == 0)
    def _():
        table = jnp.dot(
            tokens_ref[...], weight_ref[...], preferred_element_type=jnp.float32
        ).astype(jnp.bfloat16)
        keys = table[:, :feat_width].astype(jnp.float32)
        norms = jnp.maximum(jnp.sqrt(split_sum(keys * keys, heads)), 1.0)
        place = (
            lax.broadcasted_iota(jnp.int32, (head_count, lane), 0)
            == lax.broadcasted_iota(jnp.int32, (head_count, lane), 1)
        ).astype(jnp.bfloat16)
        aug_ref[:, :kv_width] = table
        rest = norms
        for part in range(3):
            piece_part = rest.astype(jnp.bfloat16)
            rest = rest - piece_part.astype(jnp.float32)
            start = kv_width + part * lane
            aug_ref[:, start : start + lane] = jnp.dot(
                piece_part, place, preferred_element_type=jnp.float32
            ).astype(jnp.bfloat16)

    piece = piece_ref[...]
    query = piece[:, :feat_width].astype(jnp.float32)
    query_norms = jnp.maximum(jnp.sqrt(split_sum(query * query, heads)), 1.0)
    query = query / split_sum(query_norms, spread)
    meta = piece[:, feat_width:].astype(jnp.float32).astype(jnp.int32)
    aug = aug_ref[...]
    scale = scale_ref[...]
    cells = lax.broadcasted_iota(jnp.int32, (rows, aug.shape[0]), 1)
    total = jnp.zeros((rows, head_count), jnp.float32)
    mix = jnp.zeros((rows, feat_width), jnp.float32)
    for corner in range(4):
        down = corner // 2
        side = corner % 2
        at = (meta[:, 0:1] + down) * ext_cols + meta[:, 1:2] + side
        picked = jnp.dot(
            (cells == at).astype(jnp.bfloat16), aug, preferred_element_type=jnp.float32
        )
        key_norms = (
            picked[:, kv_width : kv_width + head_count]
            + picked[:, kv_width + lane : kv_width + lane + head_count]
        ) + picked[:, kv_width + 2 * lane : kv_width + 2 * lane + head_count]
        scores = split_sum(query * picked[:, :feat_width], heads) / key_norms
        expo = jnp.exp(scores * scale)
        if corner > 0:
            expo = expo * meta[:, 1 + corner : 2 + corner].astype(jnp.float32)
        total = total + expo
        mix = mix + split_sum(expo, spread) * picked[:, feat_width:kv_width]
    out_ref[...] = (mix / split_sum(total, spread)).astype(out_ref.dtype)


def readout_call(piece, tokens, weight, read_scale, ext_cols, block_rows=384):
    floe_rows, piece_width = piece.shape
    head_count = read_scale.shape[0]
    kv_width = weight.shape[1]
    feat_width = kv_width // 2
    head_size = feat_width // head_count
    table_rows = -(-tokens.shape[0] // 16) * 16
    tokens = jnp.pad(tokens, ((0, table_rows - tokens.shape[0]), (0, 0)))
    heads = (
        jnp.arange(feat_width, dtype=jnp.int32)[:, None] // head_size
        == jnp.arange(head_count, dtype=jnp.int32)[None, :]
    ).astype(jnp.bfloat16)
    return pl.pallas_call(
        functools.partial(readout_kernel, ext_cols),
        grid=(floe_rows // block_rows,),
        in_specs=[
            pl.BlockSpec((block_rows, piece_width), lambda i: (i, 0)),
            pl.BlockSpec((table_rows, feat_width), lambda i: (0, 0)),
            pl.BlockSpec((feat_width, kv_width), lambda i: (0, 0)),
            pl.BlockSpec((feat_width, head_count), lambda i: (0, 0)),
            pl.BlockSpec((head_count, feat_width), lambda i: (0, 0)),
            pl.BlockSpec((1, head_count), lambda i: (0, 0)),
        ],
        out_specs=pl.BlockSpec((block_rows, feat_width), lambda i: (i, 0)),
        out_shape=jax.ShapeDtypeStruct((floe_rows, feat_width), jnp.bfloat16),
        scratch_shapes=[pltpu.VMEM((table_rows, kv_width + 3 * 128), jnp.bfloat16)],
    )(piece, tokens, weight, heads, heads.T, read_scale.reshape(1, head_count))


def local(
    wave_tokens,
    grad_out,
    w_qkv,
    w_proj,
    w_fc1,
    w_fc2,
    gain_attn,
    gain_mlp,
    attn_scale,
    bias_table,
    r_wq,
    r_wkv,
    r_wo,
    read_scale,
    floe_feat,
    floe_count,
    floe_patch,
    floe_cover,
):
    tok_rows, tok_cols, feat_width = wave_tokens.shape
    head_count = read_scale.shape[0]
    head_size = feat_width // head_count
    bias_full = bias_matrix(bias_table, WIN)

    def local_block(field):
        return swin_block(
            field, w_qkv, w_proj, w_fc1, w_fc2, gain_attn, gain_mlp, attn_scale, bias_full
        )

    both = roll_ahead(jnp.concatenate([wave_tokens, grad_out], -1))
    ahead = both[..., :feat_width]
    cot_ahead = both[..., feat_width:]
    out_ahead, pull_back = jax.vjp(local_block, ahead)
    out_ext = roll_behind(out_ahead, 1)
    patch_out = out_ext[:tok_rows, :tok_cols]
    ext_cols = tok_cols + 1
    ext_cells = (tok_rows + 1) * ext_cols
    ext_tokens = out_ext.reshape(ext_cells, feat_width)
    row_devs = lax.axis_size("gx")
    col_devs = lax.axis_size("gy")
    dev_total = row_devs * col_devs
    grid_cols = tok_cols * col_devs
    feat = floe_feat[0]
    floe_slots = feat.shape[0]
    slot_size = floe_slots // dev_total
    patch = floe_patch[0]
    cover = floe_cover[0]
    row_pos = patch // grid_cols
    col_pos = patch % grid_cols
    target = row_pos // tok_rows * col_devs + col_pos // tok_cols
    targets = one_hot(target, dev_total)
    lower = (
        jnp.arange(floe_slots, dtype=jnp.int32)[:, None]
        >= jnp.arange(floe_slots, dtype=jnp.int32)[None, :]
    ).astype(jnp.bfloat16)
    running = pick_dot(lower, targets)
    rank = jnp.sum(running * targets.astype(jnp.float32), -1).astype(jnp.int32) - 1
    place = target * slot_size + rank
    scatter = one_hot(place, floe_slots).T
    meta_width = 128
    meta = jnp.stack(
        [row_pos % tok_rows, col_pos % tok_cols, cover[0], cover[1], cover[2]], -1
    ).astype(jnp.bfloat16)
    meta = jnp.pad(meta, ((0, 0), (0, meta_width - meta.shape[1])))
    query = jnp.dot(feat, r_wq, preferred_element_type=jnp.float32).astype(jnp.bfloat16)
    scatter = scatter.reshape(dev_total, slot_size, floe_slots)
    packed = jnp.einsum(
        "tsf,fc->tsc",
        scatter,
        jnp.concatenate([query, meta], -1),
        preferred_element_type=jnp.float32,
    ).astype(jnp.bfloat16)
    piece = lax.all_to_all(
        packed,
        ("gx", "gy"),
        split_axis=0,
        concat_axis=0,
        tiled=True,
    ).reshape(floe_slots, feat_width + meta_width)
    floe_mix = readout_call(piece, ext_tokens, r_wkv, read_scale, ext_cols)
    floe_mix, cot_ahead = lax.optimization_barrier((floe_mix, cot_ahead))
    returned = lax.all_to_all(
        floe_mix.reshape(dev_total, slot_size, feat_width),
        ("gx", "gy"),
        split_axis=0,
        concat_axis=0,
        tiled=True,
    )
    grad_ahead = pull_back(cot_ahead)[0]
    returned, grad_ahead = lax.optimization_barrier((returned, grad_ahead))
    grad_in = roll_behind(grad_ahead, 0)
    floe_mix = jnp.einsum(
        "tsf,tsc->fc", scatter, returned, preferred_element_type=jnp.float32
    ).astype(jnp.bfloat16)
    updated = feat.astype(jnp.float32) + jnp.dot(floe_mix, r_wo, preferred_element_type=jnp.float32)
    alive = jnp.arange(floe_slots, dtype=jnp.int32) < floe_count[0]
    floe_out = jnp.where(alive[:, None], updated, 0.0).astype(jnp.bfloat16)[None]
    return (patch_out, grad_in, floe_out)


def solution(mesh):
    in_specs = (
        P("gx", "gy", None),
        P("gx", "gy", None),
        P(),
        P(),
        P(),
        P(),
        P(),
        P(),
        P(),
        P(),
        P(),
        P(),
        P(),
        P(),
        P(("gx", "gy"), None, None),
        P(("gx", "gy")),
        P(("gx", "gy"), None),
        P(("gx", "gy"), None, None),
    )
    out_specs = (P("gx", "gy", None), P("gx", "gy", None), P(("gx", "gy"), None, None))
    return jax.shard_map(local, mesh=mesh, in_specs=in_specs, out_specs=out_specs, check_vma=False)
```

```python
import jax
import jax.numpy as jnp
import numpy as np
import functools

from jax import lax
from jax.experimental import pallas as pl
from jax.experimental.pallas import tpu as pltpu
from jax.sharding import PartitionSpec as P

WIN = 8
SHIFT = 4


def shifted(block, axis, distance):
    devices = range(lax.axis_size(axis))
    route = [((i - distance) % len(devices), i) for i in devices]
    return lax.ppermute(block, axis, route)


def layer_norm(values):
    centred = values - jnp.mean(values, -1, keepdims=True)
    return centred / jnp.sqrt(jnp.mean(centred * centred, -1, keepdims=True) + 1e-05)


def unit_heads(values):
    return values / jnp.maximum(jnp.sqrt(jnp.sum(values * values, -1, keepdims=True)), 1.0)


def bias_index(window):
    grid_pos = np.stack(np.meshgrid(np.arange(window), np.arange(window), indexing="ij")).reshape(
        2, -1
    )
    offsets = grid_pos[:, :, None] - grid_pos[:, None, :] + window - 1
    return offsets[0] * (2 * window - 1) + offsets[1]


def swin_block(field, w_qkv, w_proj, w_fc1, w_fc2, gain_attn, gain_mlp, attn_scale, bias_full):
    tok_rows, tok_cols, feat_width = field.shape
    head_count = attn_scale.shape[0]
    head_size = feat_width // head_count
    span = WIN * WIN
    windows = (
        field.reshape(tok_rows // WIN, WIN, tok_cols // WIN, WIN, feat_width)
        .transpose(0, 2, 1, 3, 4)
        .reshape(-1, feat_width)
    )
    win_count = windows.shape[0] // span
    qkv_all = jnp.dot(windows, w_qkv, preferred_element_type=jnp.float32).astype(jnp.bfloat16)
    qkv_all = lax.optimization_barrier(qkv_all)
    qkv_all = qkv_all.reshape(win_count, span, 3, head_count, head_size)
    queries = unit_heads(qkv_all[:, :, 0].astype(jnp.float32))
    keys_unit = unit_heads(qkv_all[:, :, 1].astype(jnp.float32))
    scores = jnp.einsum("wihd,wjhd->whij", queries, keys_unit, precision=lax.Precision.HIGHEST)
    scores = scores * attn_scale[None, :, None, None] + bias_full[None]
    expo = jnp.exp(scores)
    probs = (expo / jnp.sum(expo, -1, keepdims=True)).astype(jnp.bfloat16)
    mixed = jnp.einsum(
        "whij,wjhd->wihd", probs, qkv_all[:, :, 2], preferred_element_type=jnp.float32
    )
    mixed = mixed.astype(jnp.bfloat16).reshape(-1, feat_width)
    attn_out = jnp.dot(mixed, w_proj, preferred_element_type=jnp.float32)
    hidden_one = (windows.astype(jnp.float32) + layer_norm(attn_out) * gain_attn).astype(
        jnp.bfloat16
    )
    hidden_one = lax.optimization_barrier(hidden_one)
    inner = jax.nn.gelu(
        jnp.dot(hidden_one, w_fc1, preferred_element_type=jnp.float32), approximate=True
    ).astype(jnp.bfloat16)
    mlp_out = jnp.dot(inner, w_fc2, preferred_element_type=jnp.float32)
    result = (hidden_one.astype(jnp.float32) + layer_norm(mlp_out) * gain_mlp).astype(jnp.bfloat16)
    result = result.reshape(tok_rows // WIN, tok_cols // WIN, WIN, WIN, feat_width).transpose(
        0, 2, 1, 3, 4
    )
    return result.reshape(tok_rows, tok_cols, feat_width)


def readout_mix(query, key_vals, flags, read_scale):
    floe_rows, feat_width = query.shape
    head_count = read_scale.shape[0]
    head_size = feat_width // head_count
    query_unit = unit_heads(query.astype(jnp.float32).reshape(floe_rows, head_count, head_size))
    key_unit = unit_heads(
        key_vals[:, :, :feat_width].astype(jnp.float32).reshape(floe_rows, 4, head_count, head_size)
    )
    values = (
        key_vals[:, :, feat_width:].astype(jnp.float32).reshape(floe_rows, 4, head_count, head_size)
    )
    scores = jnp.sum(query_unit[:, None] * key_unit, -1) * read_scale
    expo = jnp.exp(scores) * flags[:, :, None]
    weights = expo / jnp.sum(expo, 1, keepdims=True)
    return (
        jnp.sum(weights[..., None] * values, 1).reshape(floe_rows, feat_width).astype(jnp.bfloat16)
    )


def pull_rows(pieces, offset):
    return shifted(pieces, "gx", offset)


def pull_cols(pieces, offset):
    return shifted(pieces, "gy", offset)


def pull_diag(pieces, offset):
    row_devs = lax.axis_size("gx")
    col_devs = lax.axis_size("gy")
    route = [
        (((i - offset) % row_devs) * col_devs + (j - offset) % col_devs, i * col_devs + j)
        for i in range(row_devs)
        for j in range(col_devs)
    ]
    return lax.ppermute(pieces, ("gx", "gy"), route)


def roll_ahead(field):
    own = field[SHIFT:, SHIFT:]
    right = pull_cols(field[SHIFT:, :SHIFT], -1)
    below = pull_rows(field[:SHIFT, SHIFT:], -1)
    corner = pull_diag(field[:SHIFT, :SHIFT], -1)
    return jnp.concatenate(
        [jnp.concatenate([own, right], 1), jnp.concatenate([below, corner], 1)], 0
    )


def roll_behind(field, extra):
    tok_rows, tok_cols = field.shape[:2]
    keep_rows = tok_rows - SHIFT + extra
    keep_cols = tok_cols - SHIFT + extra
    corner = pull_diag(field[tok_rows - SHIFT :, tok_cols - SHIFT :], 1)
    above = pull_rows(field[tok_rows - SHIFT :, :keep_cols], 1)
    left = pull_cols(field[:keep_rows, tok_cols - SHIFT :], 1)
    own = field[:keep_rows, :keep_cols]
    return jnp.concatenate(
        [jnp.concatenate([corner, above], 1), jnp.concatenate([left, own], 1)], 0
    )


def one_hot(index, size, dtype=jnp.bfloat16):
    return (index[..., None] == jnp.arange(size, dtype=jnp.int32)).astype(dtype)


def exact_dot(a, b):
    return jnp.dot(a, b, precision=lax.Precision.HIGHEST, preferred_element_type=jnp.float32)


def pick_dot(a, b):
    return jnp.dot(a, b, preferred_element_type=jnp.float32)


def bias_matrix(bias_table, window):
    span = window * window
    flat = jnp.arange(span * span, dtype=jnp.int32)
    query_at = flat // span
    key_at = flat % span
    row_step = query_at // window - key_at // window + window - 1
    col_step = query_at % window - key_at % window + window - 1
    table_at = row_step * (2 * window - 1) + col_step
    picks = one_hot(table_at, bias_table.shape[1], jnp.float32)
    return exact_dot(bias_table, picks.T).reshape(bias_table.shape[0], span, span)


def head_sum(values, head_mat):
    return exact_dot(values, head_mat)


def unit_rows(values, head_mat):
    norms = jnp.maximum(jnp.sqrt(head_sum(values * values, head_mat)), 1.0)
    return values / exact_dot(norms, head_mat.T)


def split_sum(values, picks):
    high = values.astype(jnp.bfloat16)
    low = (values - high.astype(jnp.float32)).astype(jnp.bfloat16)
    return jnp.dot(high, picks, preferred_element_type=jnp.float32) + jnp.dot(
        low, picks, preferred_element_type=jnp.float32
    )


def readout_kernel(
    ext_cols, piece_ref, tokens_ref, weight_ref, heads_ref, spread_ref, scale_ref, out_ref, aug_ref
):
    rows = piece_ref.shape[0]
    feat_width = out_ref.shape[1]
    head_count = heads_ref.shape[1]
    kv_width = weight_ref.shape[1]
    lane = 128
    heads = heads_ref[...]
    spread = spread_ref[...]

    @pl.when(pl.program_id(0) == 0)
    def _():
        table = jnp.dot(
            tokens_ref[...], weight_ref[...], preferred_element_type=jnp.float32
        ).astype(jnp.bfloat16)
        keys = table[:, :feat_width].astype(jnp.float32)
        norms = jnp.maximum(jnp.sqrt(split_sum(keys * keys, heads)), 1.0)
        place = (
            lax.broadcasted_iota(jnp.int32, (head_count, lane), 0)
            == lax.broadcasted_iota(jnp.int32, (head_count, lane), 1)
        ).astype(jnp.bfloat16)
        aug_ref[:, :kv_width] = table
        rest = norms
        for part in range(3):
            piece_part = rest.astype(jnp.bfloat16)
            rest = rest - piece_part.astype(jnp.float32)
            start = kv_width + part * lane
            aug_ref[:, start : start + lane] = jnp.dot(
                piece_part, place, preferred_element_type=jnp.float32
            ).astype(jnp.bfloat16)

    piece = piece_ref[...]
    query = piece[:, :feat_width].astype(jnp.float32)
    query_norms = jnp.maximum(jnp.sqrt(split_sum(query * query, heads)), 1.0)
    query = query / split_sum(query_norms, spread)
    meta = piece[:, feat_width:].astype(jnp.float32).astype(jnp.int32)
    aug = aug_ref[...]
    scale = scale_ref[...]
    cells = lax.broadcasted_iota(jnp.int32, (rows, aug.shape[0]), 1)
    total = jnp.zeros((rows, head_count), jnp.float32)
    mix = jnp.zeros((rows, feat_width), jnp.float32)
    for corner in range(4):
        down = corner // 2
        side = corner % 2
        at = (meta[:, 0:1] + down) * ext_cols + meta[:, 1:2] + side
        picked = jnp.dot(
            (cells == at).astype(jnp.bfloat16), aug, preferred_element_type=jnp.float32
        )
        key_norms = (
            picked[:, kv_width : kv_width + head_count]
            + picked[:, kv_width + lane : kv_width + lane + head_count]
        ) + picked[:, kv_width + 2 * lane : kv_width + 2 * lane + head_count]
        scores = split_sum(query * picked[:, :feat_width], heads) / key_norms
        expo = jnp.exp(scores * scale)
        if corner > 0:
            expo = expo * meta[:, 1 + corner : 2 + corner].astype(jnp.float32)
        total = total + expo
        mix = mix + split_sum(expo, spread) * picked[:, feat_width:kv_width]
    out_ref[...] = (mix / split_sum(total, spread)).astype(out_ref.dtype)


def readout_call(piece, tokens, weight, read_scale, ext_cols, block_rows=128):
    floe_rows, piece_width = piece.shape
    head_count = read_scale.shape[0]
    kv_width = weight.shape[1]
    feat_width = kv_width // 2
    head_size = feat_width // head_count
    table_rows = -(-tokens.shape[0] // 16) * 16
    tokens = jnp.pad(tokens, ((0, table_rows - tokens.shape[0]), (0, 0)))
    heads = (
        jnp.arange(feat_width, dtype=jnp.int32)[:, None] // head_size
        == jnp.arange(head_count, dtype=jnp.int32)[None, :]
    ).astype(jnp.bfloat16)
    return pl.pallas_call(
        functools.partial(readout_kernel, ext_cols),
        grid=(floe_rows // block_rows,),
        in_specs=[
            pl.BlockSpec((block_rows, piece_width), lambda i: (i, 0)),
            pl.BlockSpec((table_rows, feat_width), lambda i: (0, 0)),
            pl.BlockSpec((feat_width, kv_width), lambda i: (0, 0)),
            pl.BlockSpec((feat_width, head_count), lambda i: (0, 0)),
            pl.BlockSpec((head_count, feat_width), lambda i: (0, 0)),
            pl.BlockSpec((1, head_count), lambda i: (0, 0)),
        ],
        out_specs=pl.BlockSpec((block_rows, feat_width), lambda i: (i, 0)),
        out_shape=jax.ShapeDtypeStruct((floe_rows, feat_width), jnp.bfloat16),
        scratch_shapes=[pltpu.VMEM((table_rows, kv_width + 3 * 128), jnp.bfloat16)],
    )(piece, tokens, weight, heads, heads.T, read_scale.reshape(1, head_count))


def local(
    wave_tokens,
    grad_out,
    w_qkv,
    w_proj,
    w_fc1,
    w_fc2,
    gain_attn,
    gain_mlp,
    attn_scale,
    bias_table,
    r_wq,
    r_wkv,
    r_wo,
    read_scale,
    floe_feat,
    floe_count,
    floe_patch,
    floe_cover,
):
    tok_rows, tok_cols, feat_width = wave_tokens.shape
    head_count = read_scale.shape[0]
    head_size = feat_width // head_count
    bias_full = bias_matrix(bias_table, WIN)

    def local_block(field):
        return swin_block(
            field, w_qkv, w_proj, w_fc1, w_fc2, gain_attn, gain_mlp, attn_scale, bias_full
        )

    both = roll_ahead(jnp.concatenate([wave_tokens, grad_out], -1))
    ahead = both[..., :feat_width]
    cot_ahead = both[..., feat_width:]
    out_ahead, pull_back = jax.vjp(local_block, ahead)
    out_ext = roll_behind(out_ahead, 1)
    patch_out = out_ext[:tok_rows, :tok_cols]
    ext_cols = tok_cols + 1
    ext_cells = (tok_rows + 1) * ext_cols
    ext_tokens = out_ext.reshape(ext_cells, feat_width)
    row_devs = lax.axis_size("gx")
    col_devs = lax.axis_size("gy")
    dev_total = row_devs * col_devs
    grid_cols = tok_cols * col_devs
    feat = floe_feat[0]
    floe_slots = feat.shape[0]
    slot_size = floe_slots // dev_total
    patch = floe_patch[0]
    cover = floe_cover[0]
    row_pos = patch // grid_cols
    col_pos = patch % grid_cols
    target = row_pos // tok_rows * col_devs + col_pos // tok_cols
    targets = one_hot(target, dev_total)
    lower = (
        jnp.arange(floe_slots, dtype=jnp.int32)[:, None]
        >= jnp.arange(floe_slots, dtype=jnp.int32)[None, :]
    ).astype(jnp.bfloat16)
    running = pick_dot(lower, targets)
    rank = jnp.sum(running * targets.astype(jnp.float32), -1).astype(jnp.int32) - 1
    place = target * slot_size + rank
    scatter = one_hot(place, floe_slots).T
    meta_width = 128
    meta = jnp.stack(
        [row_pos % tok_rows, col_pos % tok_cols, cover[0], cover[1], cover[2]], -1
    ).astype(jnp.bfloat16)
    meta = jnp.pad(meta, ((0, 0), (0, meta_width - meta.shape[1])))
    query = jnp.dot(feat, r_wq, preferred_element_type=jnp.float32).astype(jnp.bfloat16)
    scatter = scatter.reshape(dev_total, slot_size, floe_slots)
    packed = jnp.einsum(
        "tsf,fc->tsc",
        scatter,
        jnp.concatenate([query, meta], -1),
        preferred_element_type=jnp.float32,
    ).astype(jnp.bfloat16)
    piece = lax.all_to_all(
        packed,
        ("gx", "gy"),
        split_axis=0,
        concat_axis=0,
        tiled=True,
    ).reshape(floe_slots, feat_width + meta_width)
    floe_mix = readout_call(piece, ext_tokens, r_wkv, read_scale, ext_cols)
    floe_mix, cot_ahead = lax.optimization_barrier((floe_mix, cot_ahead))
    returned = lax.all_to_all(
        floe_mix.reshape(dev_total, slot_size, feat_width),
        ("gx", "gy"),
        split_axis=0,
        concat_axis=0,
        tiled=True,
    )
    grad_ahead = pull_back(cot_ahead)[0]
    returned, grad_ahead = lax.optimization_barrier((returned, grad_ahead))
    grad_in = roll_behind(grad_ahead, 0)
    floe_mix = jnp.einsum(
        "tsf,tsc->fc", scatter, returned, preferred_element_type=jnp.float32
    ).astype(jnp.bfloat16)
    updated = feat.astype(jnp.float32) + jnp.dot(floe_mix, r_wo, preferred_element_type=jnp.float32)
    alive = jnp.arange(floe_slots, dtype=jnp.int32) < floe_count[0]
    floe_out = jnp.where(alive[:, None], updated, 0.0).astype(jnp.bfloat16)[None]
    return (patch_out, grad_in, floe_out)


def solution(mesh):
    in_specs = (
        P("gx", "gy", None),
        P("gx", "gy", None),
        P(),
        P(),
        P(),
        P(),
        P(),
        P(),
        P(),
        P(),
        P(),
        P(),
        P(),
        P(),
        P(("gx", "gy"), None, None),
        P(("gx", "gy")),
        P(("gx", "gy"), None),
        P(("gx", "gy"), None, None),
    )
    out_specs = (P("gx", "gy", None), P("gx", "gy", None), P(("gx", "gy"), None, None))
    return jax.shard_map(local, mesh=mesh, in_specs=in_specs, out_specs=out_specs, check_vma=False)
```

```python
import jax
import jax.numpy as jnp
import numpy as np
import functools

from jax import lax
from jax.experimental import pallas as pl
from jax.experimental.pallas import tpu as pltpu
from jax.sharding import PartitionSpec as P

WIN = 8
SHIFT = 4


def shifted(block, axis, distance):
    devices = range(lax.axis_size(axis))
    route = [((i - distance) % len(devices), i) for i in devices]
    return lax.ppermute(block, axis, route)


def layer_norm(values):
    centred = values - jnp.mean(values, -1, keepdims=True)
    return centred / jnp.sqrt(jnp.mean(centred * centred, -1, keepdims=True) + 1e-05)


def unit_heads(values):
    return values / jnp.maximum(jnp.sqrt(jnp.sum(values * values, -1, keepdims=True)), 1.0)


def bias_index(window):
    grid_pos = np.stack(np.meshgrid(np.arange(window), np.arange(window), indexing="ij")).reshape(
        2, -1
    )
    offsets = grid_pos[:, :, None] - grid_pos[:, None, :] + window - 1
    return offsets[0] * (2 * window - 1) + offsets[1]


def swin_attn(field, w_qkv, w_proj, gain_attn, attn_scale, bias_full):
    tok_rows, tok_cols, feat_width = field.shape
    head_count = attn_scale.shape[0]
    head_size = feat_width // head_count
    span = WIN * WIN
    windows = (
        field.reshape(tok_rows // WIN, WIN, tok_cols // WIN, WIN, feat_width)
        .transpose(0, 2, 1, 3, 4)
        .reshape(-1, feat_width)
    )
    win_count = windows.shape[0] // span
    qkv_all = jnp.dot(windows, w_qkv, preferred_element_type=jnp.float32).astype(jnp.bfloat16)
    qkv_all = lax.optimization_barrier(qkv_all)
    qkv_all = qkv_all.reshape(win_count, span, 3, head_count, head_size)
    queries = unit_heads(qkv_all[:, :, 0].astype(jnp.float32))
    keys_unit = unit_heads(qkv_all[:, :, 1].astype(jnp.float32))
    scores = jnp.einsum("wihd,wjhd->whij", queries, keys_unit, precision=lax.Precision.HIGHEST)
    scores = scores * attn_scale[None, :, None, None] + bias_full[None]
    expo = jnp.exp(scores)
    probs = (expo / jnp.sum(expo, -1, keepdims=True)).astype(jnp.bfloat16)
    mixed = jnp.einsum(
        "whij,wjhd->wihd", probs, qkv_all[:, :, 2], preferred_element_type=jnp.float32
    )
    mixed = mixed.astype(jnp.bfloat16).reshape(-1, feat_width)
    attn_out = jnp.dot(mixed, w_proj, preferred_element_type=jnp.float32)
    hidden_one = (windows.astype(jnp.float32) + layer_norm(attn_out) * gain_attn).astype(
        jnp.bfloat16
    )
    return lax.optimization_barrier(hidden_one)


def swin_mlp(hidden_one, w_fc1, w_fc2, gain_mlp, tok_rows, tok_cols):
    feat_width = hidden_one.shape[-1]
    inner = jax.nn.gelu(
        jnp.dot(hidden_one, w_fc1, preferred_element_type=jnp.float32), approximate=True
    ).astype(jnp.bfloat16)
    mlp_out = jnp.dot(inner, w_fc2, preferred_element_type=jnp.float32)
    result = (hidden_one.astype(jnp.float32) + layer_norm(mlp_out) * gain_mlp).astype(jnp.bfloat16)
    result = result.reshape(tok_rows // WIN, tok_cols // WIN, WIN, WIN, feat_width).transpose(
        0, 2, 1, 3, 4
    )
    return result.reshape(tok_rows, tok_cols, feat_width)


def readout_mix(query, key_vals, flags, read_scale):
    floe_rows, feat_width = query.shape
    head_count = read_scale.shape[0]
    head_size = feat_width // head_count
    query_unit = unit_heads(query.astype(jnp.float32).reshape(floe_rows, head_count, head_size))
    key_unit = unit_heads(
        key_vals[:, :, :feat_width].astype(jnp.float32).reshape(floe_rows, 4, head_count, head_size)
    )
    values = (
        key_vals[:, :, feat_width:].astype(jnp.float32).reshape(floe_rows, 4, head_count, head_size)
    )
    scores = jnp.sum(query_unit[:, None] * key_unit, -1) * read_scale
    expo = jnp.exp(scores) * flags[:, :, None]
    weights = expo / jnp.sum(expo, 1, keepdims=True)
    return (
        jnp.sum(weights[..., None] * values, 1).reshape(floe_rows, feat_width).astype(jnp.bfloat16)
    )


def pull_rows(pieces, offset):
    return shifted(pieces, "gx", offset)


def pull_cols(pieces, offset):
    return shifted(pieces, "gy", offset)


def pull_diag(pieces, offset):
    row_devs = lax.axis_size("gx")
    col_devs = lax.axis_size("gy")
    route = [
        (((i - offset) % row_devs) * col_devs + (j - offset) % col_devs, i * col_devs + j)
        for i in range(row_devs)
        for j in range(col_devs)
    ]
    return lax.ppermute(pieces, ("gx", "gy"), route)


def roll_ahead(field):
    own = field[SHIFT:, SHIFT:]
    right = pull_cols(field[SHIFT:, :SHIFT], -1)
    below = pull_rows(field[:SHIFT, SHIFT:], -1)
    corner = pull_diag(field[:SHIFT, :SHIFT], -1)
    return jnp.concatenate(
        [jnp.concatenate([own, right], 1), jnp.concatenate([below, corner], 1)], 0
    )


def roll_behind(field, extra):
    tok_rows, tok_cols = field.shape[:2]
    keep_rows = tok_rows - SHIFT + extra
    keep_cols = tok_cols - SHIFT + extra
    corner = pull_diag(field[tok_rows - SHIFT :, tok_cols - SHIFT :], 1)
    above = pull_rows(field[tok_rows - SHIFT :, :keep_cols], 1)
    left = pull_cols(field[:keep_rows, tok_cols - SHIFT :], 1)
    own = field[:keep_rows, :keep_cols]
    return jnp.concatenate(
        [jnp.concatenate([corner, above], 1), jnp.concatenate([left, own], 1)], 0
    )


def one_hot(index, size, dtype=jnp.bfloat16):
    return (index[..., None] == jnp.arange(size, dtype=jnp.int32)).astype(dtype)


def exact_dot(a, b):
    return jnp.dot(a, b, precision=lax.Precision.HIGHEST, preferred_element_type=jnp.float32)


def pick_dot(a, b):
    return jnp.dot(a, b, preferred_element_type=jnp.float32)


def bias_matrix(bias_table, window):
    span = window * window
    flat = jnp.arange(span * span, dtype=jnp.int32)
    query_at = flat // span
    key_at = flat % span
    row_step = query_at // window - key_at // window + window - 1
    col_step = query_at % window - key_at % window + window - 1
    table_at = row_step * (2 * window - 1) + col_step
    picks = one_hot(table_at, bias_table.shape[1], jnp.float32)
    return exact_dot(bias_table, picks.T).reshape(bias_table.shape[0], span, span)


def head_sum(values, head_mat):
    return exact_dot(values, head_mat)


def unit_rows(values, head_mat):
    norms = jnp.maximum(jnp.sqrt(head_sum(values * values, head_mat)), 1.0)
    return values / exact_dot(norms, head_mat.T)


def split_sum(values, picks):
    high = values.astype(jnp.bfloat16)
    low = (values - high.astype(jnp.float32)).astype(jnp.bfloat16)
    return jnp.dot(high, picks, preferred_element_type=jnp.float32) + jnp.dot(
        low, picks, preferred_element_type=jnp.float32
    )


def readout_kernel(
    ext_cols, piece_ref, tokens_ref, weight_ref, heads_ref, spread_ref, scale_ref, out_ref, aug_ref
):
    rows = piece_ref.shape[0]
    feat_width = out_ref.shape[1]
    head_count = heads_ref.shape[1]
    kv_width = weight_ref.shape[1]
    lane = 128
    heads = heads_ref[...]
    spread = spread_ref[...]

    @pl.when(pl.program_id(0) == 0)
    def _():
        table = jnp.dot(
            tokens_ref[...], weight_ref[...], preferred_element_type=jnp.float32
        ).astype(jnp.bfloat16)
        keys = table[:, :feat_width].astype(jnp.float32)
        norms = jnp.maximum(jnp.sqrt(split_sum(keys * keys, heads)), 1.0)
        place = (
            lax.broadcasted_iota(jnp.int32, (head_count, lane), 0)
            == lax.broadcasted_iota(jnp.int32, (head_count, lane), 1)
        ).astype(jnp.bfloat16)
        aug_ref[:, :kv_width] = table
        rest = norms
        for part in range(3):
            piece_part = rest.astype(jnp.bfloat16)
            rest = rest - piece_part.astype(jnp.float32)
            start = kv_width + part * lane
            aug_ref[:, start : start + lane] = jnp.dot(
                piece_part, place, preferred_element_type=jnp.float32
            ).astype(jnp.bfloat16)

    piece = piece_ref[...]
    query = piece[:, :feat_width].astype(jnp.float32)
    query_norms = jnp.maximum(jnp.sqrt(split_sum(query * query, heads)), 1.0)
    query = query / split_sum(query_norms, spread)
    meta = piece[:, feat_width:].astype(jnp.float32).astype(jnp.int32)
    aug = aug_ref[...]
    scale = scale_ref[...]
    cells = lax.broadcasted_iota(jnp.int32, (rows, aug.shape[0]), 1)
    total = jnp.zeros((rows, head_count), jnp.float32)
    mix = jnp.zeros((rows, feat_width), jnp.float32)
    for corner in range(4):
        down = corner // 2
        side = corner % 2
        at = (meta[:, 0:1] + down) * ext_cols + meta[:, 1:2] + side
        picked = jnp.dot(
            (cells == at).astype(jnp.bfloat16), aug, preferred_element_type=jnp.float32
        )
        key_norms = (
            picked[:, kv_width : kv_width + head_count]
            + picked[:, kv_width + lane : kv_width + lane + head_count]
        ) + picked[:, kv_width + 2 * lane : kv_width + 2 * lane + head_count]
        scores = split_sum(query * picked[:, :feat_width], heads) / key_norms
        expo = jnp.exp(scores * scale)
        if corner > 0:
            expo = expo * meta[:, 1 + corner : 2 + corner].astype(jnp.float32)
        total = total + expo
        mix = mix + split_sum(expo, spread) * picked[:, feat_width:kv_width]
    out_ref[...] = (mix / split_sum(total, spread)).astype(out_ref.dtype)


def readout_call(piece, tokens, weight, read_scale, ext_cols, block_rows=256):
    floe_rows, piece_width = piece.shape
    head_count = read_scale.shape[0]
    kv_width = weight.shape[1]
    feat_width = kv_width // 2
    head_size = feat_width // head_count
    table_rows = -(-tokens.shape[0] // 16) * 16
    tokens = jnp.pad(tokens, ((0, table_rows - tokens.shape[0]), (0, 0)))
    heads = (
        jnp.arange(feat_width, dtype=jnp.int32)[:, None] // head_size
        == jnp.arange(head_count, dtype=jnp.int32)[None, :]
    ).astype(jnp.bfloat16)
    return pl.pallas_call(
        functools.partial(readout_kernel, ext_cols),
        grid=(floe_rows // block_rows,),
        in_specs=[
            pl.BlockSpec((block_rows, piece_width), lambda i: (i, 0)),
            pl.BlockSpec((table_rows, feat_width), lambda i: (0, 0)),
            pl.BlockSpec((feat_width, kv_width), lambda i: (0, 0)),
            pl.BlockSpec((feat_width, head_count), lambda i: (0, 0)),
            pl.BlockSpec((head_count, feat_width), lambda i: (0, 0)),
            pl.BlockSpec((1, head_count), lambda i: (0, 0)),
        ],
        out_specs=pl.BlockSpec((block_rows, feat_width), lambda i: (i, 0)),
        out_shape=jax.ShapeDtypeStruct((floe_rows, feat_width), jnp.bfloat16),
        scratch_shapes=[pltpu.VMEM((table_rows, kv_width + 3 * 128), jnp.bfloat16)],
    )(piece, tokens, weight, heads, heads.T, read_scale.reshape(1, head_count))


def local(
    wave_tokens,
    grad_out,
    w_qkv,
    w_proj,
    w_fc1,
    w_fc2,
    gain_attn,
    gain_mlp,
    attn_scale,
    bias_table,
    r_wq,
    r_wkv,
    r_wo,
    read_scale,
    floe_feat,
    floe_count,
    floe_patch,
    floe_cover,
):
    tok_rows, tok_cols, feat_width = wave_tokens.shape
    head_count = read_scale.shape[0]
    head_size = feat_width // head_count
    bias_full = bias_matrix(bias_table, WIN)

    def attn_part(field):
        return swin_attn(field, w_qkv, w_proj, gain_attn, attn_scale, bias_full)

    def mlp_part(hidden):
        return swin_mlp(hidden, w_fc1, w_fc2, gain_mlp, tok_rows, tok_cols)

    both = roll_ahead(jnp.concatenate([wave_tokens, grad_out], -1))
    ahead = both[..., :feat_width]
    cot_ahead = both[..., feat_width:]
    hidden, pull_attn = jax.vjp(attn_part, ahead)
    out_ahead, pull_mlp = jax.vjp(mlp_part, hidden)
    out_ext = roll_behind(out_ahead, 1)
    cot_hidden = pull_mlp(cot_ahead)[0]
    out_ext, cot_hidden = lax.optimization_barrier((out_ext, cot_hidden))
    patch_out = out_ext[:tok_rows, :tok_cols]
    ext_cols = tok_cols + 1
    ext_cells = (tok_rows + 1) * ext_cols
    ext_tokens = out_ext.reshape(ext_cells, feat_width)
    row_devs = lax.axis_size("gx")
    col_devs = lax.axis_size("gy")
    dev_total = row_devs * col_devs
    grid_cols = tok_cols * col_devs
    feat = floe_feat[0]
    floe_slots = feat.shape[0]
    slot_size = floe_slots // dev_total
    patch = floe_patch[0]
    cover = floe_cover[0]
    row_pos = patch // grid_cols
    col_pos = patch % grid_cols
    target = row_pos // tok_rows * col_devs + col_pos // tok_cols
    targets = one_hot(target, dev_total)
    lower = (
        jnp.arange(floe_slots, dtype=jnp.int32)[:, None]
        >= jnp.arange(floe_slots, dtype=jnp.int32)[None, :]
    ).astype(jnp.bfloat16)
    running = pick_dot(lower, targets)
    rank = jnp.sum(running * targets.astype(jnp.float32), -1).astype(jnp.int32) - 1
    place = target * slot_size + rank
    scatter = one_hot(place, floe_slots).T
    meta_width = 128
    meta = jnp.stack(
        [row_pos % tok_rows, col_pos % tok_cols, cover[0], cover[1], cover[2]], -1
    ).astype(jnp.bfloat16)
    meta = jnp.pad(meta, ((0, 0), (0, meta_width - meta.shape[1])))
    query = jnp.dot(feat, r_wq, preferred_element_type=jnp.float32).astype(jnp.bfloat16)
    scatter = scatter.reshape(dev_total, slot_size, floe_slots)
    packed = jnp.einsum(
        "tsf,fc->tsc",
        scatter,
        jnp.concatenate([query, meta], -1),
        preferred_element_type=jnp.float32,
    ).astype(jnp.bfloat16)
    piece = lax.all_to_all(
        packed,
        ("gx", "gy"),
        split_axis=0,
        concat_axis=0,
        tiled=True,
    ).reshape(floe_slots, feat_width + meta_width)
    floe_mix = readout_call(piece, ext_tokens, r_wkv, read_scale, ext_cols)
    floe_mix, cot_hidden = lax.optimization_barrier((floe_mix, cot_hidden))
    returned = lax.all_to_all(
        floe_mix.reshape(dev_total, slot_size, feat_width),
        ("gx", "gy"),
        split_axis=0,
        concat_axis=0,
        tiled=True,
    )
    grad_ahead = pull_attn(cot_hidden)[0]
    returned, grad_ahead = lax.optimization_barrier((returned, grad_ahead))
    grad_in = roll_behind(grad_ahead, 0)
    floe_mix = jnp.einsum(
        "tsf,tsc->fc", scatter, returned, preferred_element_type=jnp.float32
    ).astype(jnp.bfloat16)
    updated = feat.astype(jnp.float32) + jnp.dot(floe_mix, r_wo, preferred_element_type=jnp.float32)
    alive = jnp.arange(floe_slots, dtype=jnp.int32) < floe_count[0]
    floe_out = jnp.where(alive[:, None], updated, 0.0).astype(jnp.bfloat16)[None]
    return (patch_out, grad_in, floe_out)


def solution(mesh):
    in_specs = (
        P("gx", "gy", None),
        P("gx", "gy", None),
        P(),
        P(),
        P(),
        P(),
        P(),
        P(),
        P(),
        P(),
        P(),
        P(),
        P(),
        P(),
        P(("gx", "gy"), None, None),
        P(("gx", "gy")),
        P(("gx", "gy"), None),
        P(("gx", "gy"), None, None),
    )
    out_specs = (P("gx", "gy", None), P("gx", "gy", None), P(("gx", "gy"), None, None))
    return jax.shard_map(local, mesh=mesh, in_specs=in_specs, out_specs=out_specs, check_vma=False)
```
